32 devices in a mesh: groups: 2 (over y), ctx: 4 (over z), head: 2 (over x), rep: 2 (over core).
Axes of the slice: x: 2, y: 2, z: 4, core: 2. Of those that a mesh axis runs over, the one named last changes fastest.
Arguments:
- query: bfloat16 [2048, 4096], P(('groups', 'ctx', 'rep'), 'head'), parts along dimension 0, may hold values from -23.069359 to 23.069359
- key: bfloat16 [4096, 1024], P(('groups', 'ctx'), 'head'), parts along dimension 0, may hold values from -6 to 6
- value: bfloat16 [4096, 1024], P(('groups', 'ctx'), 'head'), parts along dimension 0, may hold values from -24 to 24
- out_weight: bfloat16 [4096, 4096], P('head'), may hold values from -0.375 to 0.375
- cotangent: bfloat16 [2048, 4096], P(('groups', 'ctx', 'rep')), parts along dimension 0, may hold values from -6 to 6
- response: int32 [2048], P(('groups', 'ctx', 'rep')), parts along dimension 0, may hold values 0 or 1
- segment_ids: int32 [4096], P(('groups', 'ctx')), parts along dimension 0, may hold values from 0 to 31, never falling along the last dimension, each value on 1 to 128 neighbouring positions
- masked_segments: int32 [8], P('groups'), parts along dimension 0, may hold values from 0 to 31
Outputs:
- patch_effect: bfloat16 [2048, 4096], P(('groups', 'ctx', 'rep'), 'head'), parts along dimension 0
- token_attr: float32 [4096], P(('groups', 'ctx')), parts along dimension 0
- segment_attr: float32 [64], P('groups'), parts along dimension 0
The draws below stay inside these ranges and needn't reach their ends.
There are 2 independent parts, one for each index of `groups`. The reference program is written for one: setup_inputs(seed, part) draws one part's arguments, and reference() takes and returns one part's arrays. A program takes and returns all parts, laid end to end along the dimension named above; an argument that names none is the same for every part. Nothing has to cross between parts.
All inputs are finite; a program needn't handle non-finite values. No bound on the sum of `response` on one device may be relied on, other than what follows from the above.
Results may differ from the reference program's by a relative error of at most 0.0095.
Values may be sent and summed in bfloat16 or wider, within the bound.
No kernel may reach another device: no remote copies, remote signals or barrier semaphores. Data moves between devices by JAX's collectives and lax.ppermute only.
A program may use at most 128 MiB of HBM per device.

```python
import math
import jax
import jax.numpy as jnp
import numpy as np
from jax import lax

D = 4096
H = 32
KVH = 8
HD = 128
CTX_LEN = 2048
Q_LEN = 1024
NSEG = 32
MOST_SEG = 128
NMASK = 4


def draw_key(key, part):
    base = jnp.clip(jax.random.normal(jax.random.fold_in(key, 76), (CTX_LEN, KVH * HD), jnp.float32), -6.0, 6.0)
    return base.astype(jnp.bfloat16)


def draw_query(key, part):
    base = jnp.clip(2.0 * jax.random.normal(jax.random.fold_in(key, 77), (Q_LEN, H * HD), jnp.float32), -12.0, 12.0)
    return base.astype(jnp.bfloat16)


def plant(values, key, smallest, high):
    dims = values.shape
    spot = [jax.random.randint(jax.random.fold_in(key, axis), (), 0, dims[axis]) for axis in range(len(dims))]
    values = values.at[tuple(spot)].set(smallest)
    longest = dims.index(max(dims))
    spot[longest] = (spot[longest] + 1) % dims[longest]
    return values.at[tuple(spot)].set(high)


def block_levels(key, dims, shards, smallest, high):
    def one(position, shards_of):
        heights = jax.random.uniform(jax.random.fold_in(jax.random.fold_in(key, 6), position), (shards_of,), jnp.float32, smallest / len(shards), high / len(shards))
        return jnp.repeat(jnp.exp(heights), dims[position] // shards_of).reshape((-1,) + (1,) * (len(dims) - position - 1))

    level = one(*shards[0])
    for cut in shards[1:]:
        level = level * one(*cut)
    return level


def profile(count, total, bound, skew):
    portions = [(1 << 20) // math.isqrt(standing ** skew) + 1 for standing in range(2, count + 1)]
    spare, counts = total - bound - (count - 1), [1] * (count - 1)
    while spare > 0:
        free = [i for i in range(count - 1) if counts[i] < bound]
        mass, budget = sum([portions[i] for i in free]), spare
        for i in free:
            addition = min(bound - counts[i], max(1, budget * portions[i] // mass), spare)
            counts[i] = counts[i] + addition
            spare = spare - addition
    return np.array([bound] + counts)


def uneven_parts(key, count, total, reach, skew):
    if count == 2:
        one = jax.random.randint(key, (), max(1, total - reach), min(reach, total - 1) + 1)
        return jnp.stack([one, total - one])
    lengths = jnp.asarray(profile(count, total, reach, skew), jnp.int32)
    pairs = (count - 1) // 2
    source_of, receiver = lengths[1:1 + 2 * pairs:2], lengths[2:2 + 2 * pairs:2]
    slack = jnp.minimum(source_of - 1, reach - receiver)
    moved = jax.random.randint(jax.random.fold_in(key, 1), (pairs,), 0, 1 << 20) % (slack + 1)
    lengths = lengths.at[1:1 + 2 * pairs:2].set(source_of - moved).at[2:2 + 2 * pairs:2].set(receiver + moved)
    return lengths[jax.random.permutation(jax.random.fold_in(key, 2), count)]


def noise(key, shape, deviation, reach, pieces=(), held_as=jnp.bfloat16):
    factor_of = block_levels(key, shape, pieces, -0.22, 0.18) if pieces else 1.0
    result = jax.random.normal(key, shape, jnp.float32) * deviation * factor_of
    return jnp.minimum(jnp.maximum(result, -reach), reach).astype(held_as)


def setup_inputs(seed: int = 0, part: int = 0) -> dict:
    keys = jax.random.split(jax.random.key(seed), 9)
    part_keys = jax.random.split(jax.random.fold_in(keys[8], part), 9)
    query = draw_query(jax.random.fold_in(jax.random.fold_in(keys[8], part), 71), part)
    key = draw_key(jax.random.fold_in(jax.random.fold_in(keys[8], part), 71), part)
    value = noise(part_keys[2], (CTX_LEN, KVH * HD), 4.0, 24.0, ((0, 4), (1, 2)))
    out_weight = noise(keys[3], (H * HD, D), (D // 16) ** -0.5, 0.375, ((0, 2),))
    cotangent = noise(part_keys[4], (Q_LEN, D), 1.0, 6.0, ((0, 8),))
    response = plant((jax.random.randint(part_keys[5], (Q_LEN,), 0, 4) < 3).astype(jnp.int32), jax.random.fold_in(part_keys[5], 1), 0, 1)
    segment_ids = jnp.searchsorted(jnp.cumsum(uneven_parts(part_keys[6], NSEG, CTX_LEN, MOST_SEG, 1)), jnp.arange(CTX_LEN), side="right").astype(jnp.int32)
    masked_segments = plant(jax.random.randint(part_keys[7], (NMASK,), 0, NSEG), jax.random.fold_in(part_keys[7], 1), 0, NSEG - 1).astype(jnp.int32)
    return dict(query=query, key=key, value=value, out_weight=out_weight, cotangent=cotangent, response=response, segment_ids=segment_ids, masked_segments=masked_segments)


def reference(query, key, value, out_weight, cotangent, response, segment_ids, masked_segments):
    group_size = H // KVH
    score_scale = HD ** -0.5
    query_pos = (CTX_LEN - Q_LEN) + jnp.arange(Q_LEN, dtype=jnp.int32)
    key_pos = jnp.arange(CTX_LEN, dtype=jnp.int32)
    visible = key_pos[None, :] <= query_pos[:, None]
    kept_keys = jnp.logical_not(jnp.any(segment_ids[:, None] == masked_segments[None, :], axis=1))
    kept_visible = jnp.logical_and(visible, kept_keys[None, :])
    grad_rows = jnp.where(response[:, None] > 0, cotangent, jnp.zeros_like(cotangent))
    grad_out = jnp.dot(grad_rows, out_weight.T, preferred_element_type=jnp.float32).astype(jnp.bfloat16)
    query_heads = query.reshape(Q_LEN, H, HD).transpose(1, 0, 2)
    grad_heads = grad_out.reshape(Q_LEN, H, HD).transpose(1, 0, 2)
    key_heads = key.reshape(CTX_LEN, KVH, HD).transpose(1, 0, 2)
    value_heads = value.reshape(CTX_LEN, KVH, HD).transpose(1, 0, 2)

    def attend(scores, allowed, value_one):
        chosen = jnp.where(allowed, scores, -jnp.inf)
        row_top = jnp.max(chosen, axis=1, keepdims=True)
        weights = jnp.exp(chosen - row_top)
        row_total = jnp.sum(weights, axis=1, keepdims=True)
        mixed_out = jnp.dot(weights.astype(jnp.bfloat16), value_one, preferred_element_type=jnp.float32) / row_total
        return mixed_out, weights / row_total, row_top + jnp.log(row_total)

    def one_head(inputs):
        query_one, grad_one, head_at = inputs
        key_one = lax.dynamic_index_in_dim(key_heads, head_at // group_size, 0, keepdims=False)
        value_one = lax.dynamic_index_in_dim(value_heads, head_at // group_size, 0, keepdims=False)
        scores = jnp.dot(query_one, key_one.T, preferred_element_type=jnp.float32) * score_scale
        clean_out, clean_prob, clean_log = attend(scores, visible, value_one)
        masked_out, _, _ = attend(scores, kept_visible, value_one)
        row_dot = jnp.sum(grad_one.astype(jnp.float32) * clean_out, axis=1, keepdims=True)
        grad_prob = jnp.dot(grad_one, value_one.T, preferred_element_type=jnp.float32)
        shifted = jnp.where(visible, scores - clean_log, 0.0)
        attribution = jnp.sum(clean_prob * (grad_prob + (grad_prob - row_dot) * shifted), axis=0)
        return clean_out, masked_out, attribution

    clean_out, masked_out, attribution = lax.map(one_head, (query_heads, grad_heads, jnp.arange(H, dtype=jnp.int32)))
    out_change = (masked_out - clean_out).transpose(1, 0, 2).reshape(Q_LEN, H * HD).astype(jnp.bfloat16)
    patch_effect = jnp.dot(out_change, out_weight, preferred_element_type=jnp.float32).astype(jnp.bfloat16)
    token_attr = jnp.sum(attribution, axis=0)
    onehot = (segment_ids[:, None] == jnp.arange(NSEG, dtype=jnp.int32)[None, :]).astype(jnp.float32)
    segment_attr = jnp.dot(token_attr, onehot, precision=lax.Precision.HIGHEST)
    return patch_effect, token_attr, segment_attr
```

```python
import functools

import jax
import jax.numpy as jnp
from jax import lax
from jax.experimental import pallas as pl
from jax.experimental.pallas import tpu as pltpu
from jax.sharding import PartitionSpec as P

HD = 128
SEG_DEV = 8
NEG_FILL = -1e30
NT_DIMS = (((1,), (1,)), ((), ()))


def attention_kernel(base_ref, q_ref, k_ref, v_ref, kept_ref, do_ref, delta_ref, attr_ref, *, tq):
    r = pl.program_id(2)
    first = (pl.program_id(0) == 0) & (pl.program_id(1) == 0) & (r == 0)

    @pl.when(first)
    def _():
        attr_ref[...] = jnp.zeros_like(attr_ref)

    q = q_ref[...]
    k = k_ref[...]
    v = v_ref[...]
    keys = k.shape[0]
    s = lax.dot_general(q, k, NT_DIMS, preferred_element_type=jnp.float32) * (HD ** -0.5)
    row_pos = base_ref[0] + r * tq + lax.broadcasted_iota(jnp.int32, (tq, keys), 0)
    key_pos = lax.broadcasted_iota(jnp.int32, (tq, keys), 1)
    vis = key_pos <= row_pos
    kvis = jnp.logical_and(vis, kept_ref[...] > 0.0)
    m_c = jnp.max(jnp.where(vis, s, NEG_FILL), axis=1, keepdims=True)
    m_m = jnp.max(jnp.where(kvis, s, NEG_FILL), axis=1, keepdims=True)
    e_c = jnp.where(vis, jnp.exp(s - m_c), 0.0)
    e_m = jnp.where(kvis, jnp.exp(s - m_m), 0.0)
    l_c = jnp.sum(e_c, axis=1, keepdims=True)
    l_m = jnp.sum(e_m, axis=1, keepdims=True)
    o_c = jnp.dot(e_c.astype(jnp.bfloat16), v, preferred_element_type=jnp.float32) / l_c
    o_m = jnp.dot(e_m.astype(jnp.bfloat16), v, preferred_element_type=jnp.float32) / l_m
    delta_ref[...] = (o_m - o_c).astype(delta_ref.dtype)
    g_rows = do_ref[...]
    row_dot = jnp.sum(g_rows.astype(jnp.float32) * o_c, axis=1, keepdims=True)
    d_p = lax.dot_general(g_rows, v, NT_DIMS, preferred_element_type=jnp.float32)
    log_total = m_c + jnp.log(l_c)
    prob = e_c * (1.0 / l_c)
    contrib = prob * (d_p + (d_p - row_dot) * (s - log_total))
    attr_ref[...] += jnp.sum(contrib, axis=0, keepdims=True)


def fused_attention(base, query, key_all, value_all, kept, grad_out, group_size):
    qc, width = query.shape
    keys, kv_width = key_all.shape
    kv_local = kv_width // HD
    tq = max(8, min(qc, (128 * 2048) // keys))
    n_rows = qc // tq
    grid = (kv_local, group_size, n_rows)

    def head_map(g, j, r, b):
        return (r, g * group_size + j)

    def kv_map(g, j, r, b):
        return (0, g)

    def fixed(g, j, r, b):
        return (0, 0)

    flops = 8 * qc * keys * HD * kv_local * group_size
    cost = pl.CostEstimate(
        flops=flops,
        transcendentals=2 * qc * keys * kv_local * group_size,
        bytes_accessed=2 * (query.size + key_all.size + value_all.size + grad_out.size + query.size)
        + 4 * keys,
    )
    return pl.pallas_call(
        functools.partial(attention_kernel, tq=tq),
        grid_spec=pltpu.PrefetchScalarGridSpec(
            num_scalar_prefetch=1,
            grid=grid,
            in_specs=[
                pl.BlockSpec((tq, HD), head_map),
                pl.BlockSpec((keys, HD), kv_map),
                pl.BlockSpec((keys, HD), kv_map),
                pl.BlockSpec((1, keys), fixed),
                pl.BlockSpec((tq, HD), head_map),
            ],
            out_specs=[
                pl.BlockSpec((tq, HD), head_map),
                pl.BlockSpec((1, keys), fixed),
            ],
        ),
        out_shape=[
            jax.ShapeDtypeStruct((qc, width), jnp.bfloat16),
            jax.ShapeDtypeStruct((1, keys), jnp.float32),
        ],
        compiler_params=pltpu.CompilerParams(
            dimension_semantics=("arbitrary", "arbitrary", "arbitrary")
        ),
        cost_estimate=cost,
    )(base, query, key_all, value_all, kept, grad_out)


def gather_kv(key, value, rep_at, rep_count):
    if rep_count != 2:
        return (
            lax.all_gather(key, "ctx", axis=0, tiled=True),
            lax.all_gather(value, "ctx", axis=0, tiled=True),
        )
    payload = jnp.where(rep_at == 0, key, value)
    mine = lax.all_gather(payload, "ctx", axis=0, tiled=True)
    other = lax.ppermute(mine, "rep", [(0, 1), (1, 0)])
    first = rep_at == 0
    return jnp.where(first, mine, other), jnp.where(first, other, mine)


def local(query, key, value, out_weight, cotangent, response, segment_ids, masked_segments):
    ctx_count = lax.axis_size("ctx")
    rep_count = lax.axis_size("rep")
    ctx_at = lax.axis_index("ctx")
    rep_at = lax.axis_index("rep")
    query_count = query.shape[0]
    key_count = key.shape[0]
    kv_local = key.shape[1] // HD
    heads_local = query.shape[1] // HD
    group_size = heads_local // kv_local
    context_len = key_count * ctx_count
    query_base = context_len - query_count * ctx_count * rep_count
    base = (query_base + (ctx_at * rep_count + rep_at) * query_count).astype(jnp.int32)
    base = jnp.reshape(base, (1,))

    seg_all = lax.all_gather(segment_ids, "ctx", axis=0, tiled=True)
    kept = jnp.where(
        jnp.any(seg_all[:, None] == masked_segments[None, :], axis=1), 0.0, 1.0
    ).astype(jnp.float32)[None, :]
    key_all, value_all = gather_kv(key, value, rep_at, rep_count)

    grad_masked = jnp.where(response[:, None] > 0, cotangent, jnp.zeros_like(cotangent))
    grad_out = jnp.dot(grad_masked, out_weight.T, preferred_element_type=jnp.float32).astype(
        jnp.bfloat16
    )
    delta, attr = fused_attention(base, query, key_all, value_all, kept, grad_out, group_size)

    projected = jnp.dot(delta, out_weight, preferred_element_type=jnp.float32).astype(jnp.bfloat16)
    patch_effect = lax.psum_scatter(projected, "head", scatter_dimension=1, tiled=True)

    attr_all = lax.psum(attr[0], ("ctx", "head", "rep"))
    token_attr = lax.dynamic_slice_in_dim(attr_all, ctx_at * key_count, key_count, 0)
    onehot = (
        seg_all[:, None] == jnp.arange(SEG_DEV * ctx_count, dtype=jnp.int32)[None, :]
    ).astype(jnp.float32)
    segment_attr = jnp.dot(attr_all, onehot, precision=lax.Precision.HIGHEST)
    return (patch_effect, token_attr, segment_attr)


def solution(mesh):
    return jax.shard_map(
        local,
        mesh=mesh,
        in_specs=(
            P(("groups", "ctx", "rep"), "head"),
            P(("groups", "ctx"), "head"),
            P(("groups", "ctx"), "head"),
            P("head", None),
            P(("groups", "ctx", "rep"), None),
            P(("groups", "ctx", "rep")),
            P(("groups", "ctx")),
            P("groups"),
        ),
        out_specs=(P(("groups", "ctx", "rep"), "head"), P(("groups", "ctx")), P("groups")),
        check_vma=False,
    )
```

```python
import functools

import jax
import jax.numpy as jnp
from jax import lax
from jax.experimental import pallas as pl
from jax.experimental.pallas import tpu as pltpu
from jax.sharding import PartitionSpec as P

HD = 128
SEG_DEV = 8
NEG_FILL = -1e30
NT_DIMS = (((1,), (1,)), ((), ()))


def attention_kernel(base_ref, kpos_ref, q_ref, k_ref, v_ref, kept_ref, do_ref, delta_ref, attr_ref, *, tq):
    r = pl.program_id(2)
    first = (pl.program_id(0) == 0) & (pl.program_id(1) == 0) & (r == 0)

    @pl.when(first)
    def _():
        attr_ref[...] = jnp.zeros_like(attr_ref)

    q = q_ref[...]
    k = k_ref[...]
    v = v_ref[...]
    keys = k.shape[0]
    s = lax.dot_general(q, k, NT_DIMS, preferred_element_type=jnp.float32) * (HD ** -0.5)
    row_pos = base_ref[0] + r * tq + lax.broadcasted_iota(jnp.int32, (tq, keys), 0)
    vis = kpos_ref[...] <= row_pos
    kvis = jnp.logical_and(vis, kept_ref[...] > 0.0)
    m_c = jnp.max(jnp.where(vis, s, NEG_FILL), axis=1, keepdims=True)
    m_m = jnp.max(jnp.where(kvis, s, NEG_FILL), axis=1, keepdims=True)
    e_c = jnp.where(vis, jnp.exp(s - m_c), 0.0)
    e_m = jnp.where(kvis, jnp.exp(s - m_m), 0.0)
    l_c = jnp.sum(e_c, axis=1, keepdims=True)
    l_m = jnp.sum(e_m, axis=1, keepdims=True)
    o_c = jnp.dot(e_c.astype(jnp.bfloat16), v, preferred_element_type=jnp.float32) / l_c
    o_m = jnp.dot(e_m.astype(jnp.bfloat16), v, preferred_element_type=jnp.float32) / l_m
    delta_ref[...] = (o_m - o_c).astype(delta_ref.dtype)
    g_rows = do_ref[...]
    row_dot = jnp.sum(g_rows.astype(jnp.float32) * o_c, axis=1, keepdims=True)
    d_p = lax.dot_general(g_rows, v, NT_DIMS, preferred_element_type=jnp.float32)
    log_total = m_c + jnp.log(l_c)
    prob = e_c * (1.0 / l_c)
    contrib = prob * (d_p + (d_p - row_dot) * (s - log_total))
    attr_ref[...] += jnp.sum(contrib, axis=0, keepdims=True)


def fused_attention(base, key_pos, query, key_all, value_all, kept, grad_out, group_size):
    qc, width = query.shape
    keys, kv_width = key_all.shape
    kv_local = kv_width // HD
    tq = max(8, min(qc, (128 * 2048) // keys))
    n_rows = qc // tq
    grid = (kv_local, group_size, n_rows)

    def head_map(g, j, r, b):
        return (r, g * group_size + j)

    def kv_map(g, j, r, b):
        return (0, g)

    def fixed(g, j, r, b):
        return (0, 0)

    flops = 8 * qc * keys * HD * kv_local * group_size
    cost = pl.CostEstimate(
        flops=flops,
        transcendentals=2 * qc * keys * kv_local * group_size,
        bytes_accessed=2 * (query.size + key_all.size + value_all.size + grad_out.size + query.size)
        + 4 * keys,
    )
    return pl.pallas_call(
        functools.partial(attention_kernel, tq=tq),
        grid_spec=pltpu.PrefetchScalarGridSpec(
            num_scalar_prefetch=1,
            grid=grid,
            in_specs=[
                pl.BlockSpec((1, keys), fixed),
                pl.BlockSpec((tq, HD), head_map),
                pl.BlockSpec((keys, HD), kv_map),
                pl.BlockSpec((keys, HD), kv_map),
                pl.BlockSpec((1, keys), fixed),
                pl.BlockSpec((tq, HD), head_map),
            ],
            out_specs=[
                pl.BlockSpec((tq, HD), head_map),
                pl.BlockSpec((1, keys), fixed),
            ],
        ),
        out_shape=[
            jax.ShapeDtypeStruct((qc, width), jnp.bfloat16),
            jax.ShapeDtypeStruct((1, keys), jnp.float32),
        ],
        compiler_params=pltpu.CompilerParams(
            dimension_semantics=("arbitrary", "arbitrary", "arbitrary")
        ),
        cost_estimate=cost,
    )(base, key_pos, query, key_all, value_all, kept, grad_out)


def gather_kv(key, value, segment_ids, ctx_at, rep_at, rep_count):
    n = lax.axis_size("ctx")
    key_count, width = key.shape
    seg_rows = -(-key_count // width)
    seg_pad = -(-seg_rows // 16) * 16
    seg_block = jnp.zeros((seg_pad * width,), jnp.bfloat16)
    seg_block = seg_block.at[:key_count].set(segment_ids.astype(jnp.bfloat16))
    seg_block = seg_block.reshape(seg_pad, width)
    split = rep_count == 2
    halves = [jnp.where(rep_at == 0, key, value)] if split else [key, value]
    payloads = [jnp.concatenate([h, seg_block], axis=0) for h in halves]
    gathered = []
    for payload in payloads:
        parts = [payload] + [
            lax.ppermute(payload, "ctx", [(i, (i + d) % n) for i in range(n)]) for d in range(1, n)
        ]
        gathered.append(parts)
    if split:
        mine = gathered[0]
        theirs = [lax.ppermute(p, "rep", [(0, 1), (1, 0)]) for p in mine]
        first = rep_at == 0
        key_parts = [jnp.where(first, a, b) for a, b in zip(mine, theirs)]
        value_parts = [jnp.where(first, b, a) for a, b in zip(mine, theirs)]
    else:
        key_parts, value_parts = gathered
    key_all = jnp.concatenate([p[:key_count] for p in key_parts], axis=0)
    value_all = jnp.concatenate([p[:key_count] for p in value_parts], axis=0)
    seg_all = jnp.concatenate(
        [p[key_count:].reshape(-1)[:key_count] for p in key_parts], axis=0
    ).astype(jnp.int32)
    source = (ctx_at - jnp.arange(n, dtype=jnp.int32)) % n
    key_pos = (source[:, None] * key_count + jnp.arange(key_count, dtype=jnp.int32)[None, :])
    return key_all, value_all, seg_all, key_pos.reshape(1, -1), source


def butterfly_sum(total, axes):
    for axis in axes:
        n = lax.axis_size(axis)
        if n & (n - 1):
            total = lax.psum(total, axis)
            continue
        bit = 1
        while bit < n:
            total = total + lax.ppermute(total, axis, [(i, i ^ bit) for i in range(n)])
            bit *= 2
    return total


def local(query, key, value, out_weight, cotangent, response, segment_ids, masked_segments):
    ctx_count = lax.axis_size("ctx")
    rep_count = lax.axis_size("rep")
    head_count = lax.axis_size("head")
    ctx_at = lax.axis_index("ctx")
    rep_at = lax.axis_index("rep")
    head_at = lax.axis_index("head")
    query_count = query.shape[0]
    key_count = key.shape[0]
    kv_local = key.shape[1] // HD
    heads_local = query.shape[1] // HD
    group_size = heads_local // kv_local
    context_len = key_count * ctx_count
    query_base = context_len - query_count * ctx_count * rep_count
    base = (query_base + (ctx_at * rep_count + rep_at) * query_count).astype(jnp.int32)
    base = jnp.reshape(base, (1,))

    key_all, value_all, seg_shift, key_pos, source = gather_kv(
        key, value, segment_ids, ctx_at, rep_at, rep_count
    )
    kept = jnp.where(
        jnp.any(seg_shift[:, None] == masked_segments[None, :], axis=1), 0.0, 1.0
    ).astype(jnp.float32)[None, :]

    grad_masked = jnp.where(response[:, None] > 0, cotangent, jnp.zeros_like(cotangent))
    grad_out = jnp.dot(grad_masked, out_weight.T, preferred_element_type=jnp.float32).astype(
        jnp.bfloat16
    )
    delta, attr = fused_attention(
        base, key_pos, query, key_all, value_all, kept, grad_out, group_size
    )

    inverse = (ctx_at - jnp.arange(ctx_count, dtype=jnp.int32)) % ctx_count
    attr_abs = attr.reshape(ctx_count, key_count)[inverse].reshape(-1)
    seg_abs = seg_shift.reshape(ctx_count, key_count)[inverse].reshape(-1)
    attr_all = butterfly_sum(attr_abs, ("rep", "head", "ctx"))

    projected = jnp.dot(delta, out_weight, preferred_element_type=jnp.float32)
    if head_count == 2:
        cols = projected.shape[1] // 2
        keep = lax.dynamic_slice_in_dim(projected, head_at * cols, cols, 1)
        send = lax.dynamic_slice_in_dim(projected, (1 - head_at) * cols, cols, 1)
        got = lax.ppermute(send.astype(jnp.bfloat16), "head", [(0, 1), (1, 0)])
        patch_effect = (keep + got.astype(jnp.float32)).astype(jnp.bfloat16)
    else:
        patch_effect = lax.psum_scatter(
            projected.astype(jnp.bfloat16), "head", scatter_dimension=1, tiled=True
        )

    token_attr = lax.dynamic_slice_in_dim(attr_all, ctx_at * key_count, key_count, 0)
    onehot = (
        seg_abs[:, None] == jnp.arange(SEG_DEV * ctx_count, dtype=jnp.int32)[None, :]
    ).astype(jnp.float32)
    segment_attr = jnp.dot(attr_all, onehot, precision=lax.Precision.HIGHEST)
    return (patch_effect, token_attr, segment_attr)


def solution(mesh):
    return jax.shard_map(
        local,
        mesh=mesh,
        in_specs=(
            P(("groups", "ctx", "rep"), "head"),
            P(("groups", "ctx"), "head"),
            P(("groups", "ctx"), "head"),
            P("head", None),
            P(("groups", "ctx", "rep"), None),
            P(("groups", "ctx", "rep")),
            P(("groups", "ctx")),
            P("groups"),
        ),
        out_specs=(P(("groups", "ctx", "rep"), "head"), P(("groups", "ctx")), P("groups")),
        check_vma=False,
    )
```

```python
import functools

import jax
import jax.numpy as jnp
from jax import lax
from jax.experimental import pallas as pl
from jax.experimental.pallas import tpu as pltpu
from jax.sharding import PartitionSpec as P

HD = 128
SEG_DEV = 8
NEG_FILL = -1e30
NT_DIMS = (((1,), (1,)), ((), ()))


def score_block(base_ref, kpos_ref, q_ref, k_ref, tq):
    r = pl.program_id(2)
    s = lax.dot_general(q_ref[...], k_ref[...], NT_DIMS, preferred_element_type=jnp.float32)
    s = s * (HD ** -0.5)
    row_pos = base_ref[0] + r * tq + lax.broadcasted_iota(jnp.int32, s.shape, 0)
    return s, kpos_ref[...] <= row_pos


def forward_kernel(
    base_ref, kpos_ref, q_ref, k_ref, v_ref, kept_ref, do_ref, w_ref,
    delta_ref, lse_ref, dot_ref, patch_ref, *, tq
):
    r = pl.program_id(2)
    first = (pl.program_id(0) == 0) & (pl.program_id(1) == 0) & (r == 0)

    @pl.when(first)
    def _():
        patch_ref[...] = jnp.zeros_like(patch_ref)

    s, vis = score_block(base_ref, kpos_ref, q_ref, k_ref, tq)
    v = v_ref[...]
    kvis = jnp.logical_and(vis, kept_ref[...] > 0.0)
    m_c = jnp.max(jnp.where(vis, s, NEG_FILL), axis=1, keepdims=True)
    m_m = jnp.max(jnp.where(kvis, s, NEG_FILL), axis=1, keepdims=True)
    e_c = jnp.where(vis, jnp.exp(s - m_c), 0.0)
    e_m = jnp.where(kvis, jnp.exp(s - m_m), 0.0)
    l_c = jnp.sum(e_c, axis=1, keepdims=True)
    l_m = jnp.sum(e_m, axis=1, keepdims=True)
    o_c = jnp.dot(e_c.astype(jnp.bfloat16), v, preferred_element_type=jnp.float32) / l_c
    o_m = jnp.dot(e_m.astype(jnp.bfloat16), v, preferred_element_type=jnp.float32) / l_m
    delta = (o_m - o_c).astype(jnp.bfloat16)
    delta_ref[...] = delta
    lse_ref[0] = m_c + jnp.log(l_c)
    dot_ref[0] = jnp.sum(do_ref[...].astype(jnp.float32) * o_c, axis=1, keepdims=True)
    rows = pl.ds(pl.multiple_of(r * tq, 8), tq)
    patch_ref[rows, :] += jnp.dot(delta, w_ref[...], preferred_element_type=jnp.float32)


def backward_kernel(
    base_ref, kpos_ref, q_ref, k_ref, v_ref, do_ref, lse_ref, dot_ref, attr_ref, *, tq
):
    r = pl.program_id(2)
    first = (pl.program_id(0) == 0) & (pl.program_id(1) == 0) & (r == 0)

    @pl.when(first)
    def _():
        attr_ref[...] = jnp.zeros_like(attr_ref)

    s, vis = score_block(base_ref, kpos_ref, q_ref, k_ref, tq)
    shifted = s - lse_ref[0]
    prob = jnp.where(vis, jnp.exp(shifted), 0.0)
    d_p = lax.dot_general(do_ref[...], v_ref[...], NT_DIMS, preferred_element_type=jnp.float32)
    contrib = prob * (d_p + (d_p - dot_ref[0]) * shifted)
    attr_ref[...] += jnp.sum(contrib, axis=0, keepdims=True)


def fused_attention(base, key_pos, query, key_all, value_all, kept, grad_out, out_weight, group_size):
    qc, width = query.shape
    keys, kv_width = key_all.shape
    kv_local = kv_width // HD
    heads_local = kv_local * group_size
    model = out_weight.shape[1]
    tq = max(8, min(qc, (128 * 2048) // keys))
    n_rows = qc // tq
    grid = (kv_local, group_size, n_rows)

    def head_map(g, j, r, b):
        return (r, g * group_size + j)

    def kv_map(g, j, r, b):
        return (0, g)

    def fixed(g, j, r, b):
        return (0, 0)

    def weight_map(g, j, r, b):
        return (g * group_size + j, 0)

    def stat_map(g, j, r, b):
        return (g * group_size + j, r, 0)

    params = pltpu.CompilerParams(dimension_semantics=("arbitrary", "arbitrary", "arbitrary"))
    pair = qc * keys * HD * heads_local * 2
    delta, lse, row_dot, patch = pl.pallas_call(
        functools.partial(forward_kernel, tq=tq),
        grid_spec=pltpu.PrefetchScalarGridSpec(
            num_scalar_prefetch=1,
            grid=grid,
            in_specs=[
                pl.BlockSpec((1, keys), fixed),
                pl.BlockSpec((tq, HD), head_map),
                pl.BlockSpec((keys, HD), kv_map),
                pl.BlockSpec((keys, HD), kv_map),
                pl.BlockSpec((1, keys), fixed),
                pl.BlockSpec((tq, HD), head_map),
                pl.BlockSpec((HD, model), weight_map),
            ],
            out_specs=[
                pl.BlockSpec((tq, HD), head_map),
                pl.BlockSpec((1, tq, 1), stat_map),
                pl.BlockSpec((1, tq, 1), stat_map),
                pl.BlockSpec((qc, model), fixed),
            ],
        ),
        out_shape=[
            jax.ShapeDtypeStruct((qc, width), jnp.bfloat16),
            jax.ShapeDtypeStruct((heads_local, qc, 1), jnp.float32),
            jax.ShapeDtypeStruct((heads_local, qc, 1), jnp.float32),
            jax.ShapeDtypeStruct((qc, model), jnp.float32),
        ],
        compiler_params=params,
        cost_estimate=pl.CostEstimate(
            flops=3 * pair + 2 * qc * width * model,
            transcendentals=2 * qc * keys * heads_local,
            bytes_accessed=2 * (3 * query.size + key_all.size + value_all.size + out_weight.size)
            + 4 * qc * model,
        ),
    )(base, key_pos, query, key_all, value_all, kept, grad_out, out_weight)
    attr = pl.pallas_call(
        functools.partial(backward_kernel, tq=tq),
        grid_spec=pltpu.PrefetchScalarGridSpec(
            num_scalar_prefetch=1,
            grid=grid,
            in_specs=[
                pl.BlockSpec((1, keys), fixed),
                pl.BlockSpec((tq, HD), head_map),
                pl.BlockSpec((keys, HD), kv_map),
                pl.BlockSpec((keys, HD), kv_map),
                pl.BlockSpec((tq, HD), head_map),
                pl.BlockSpec((1, tq, 1), stat_map),
                pl.BlockSpec((1, tq, 1), stat_map),
            ],
            out_specs=pl.BlockSpec((1, keys), fixed),
        ),
        out_shape=jax.ShapeDtypeStruct((1, keys), jnp.float32),
        compiler_params=params,
        cost_estimate=pl.CostEstimate(
            flops=2 * pair,
            transcendentals=qc * keys * heads_local,
            bytes_accessed=2 * (2 * query.size + key_all.size + value_all.size) + 4 * keys,
        ),
    )(base, key_pos, query, key_all, value_all, grad_out, lse, row_dot)
    return delta, attr, patch


def gather_kv(key, value, segment_ids, ctx_at, rep_at, rep_count):
    n = lax.axis_size("ctx")
    key_count, width = key.shape
    seg_rows = -(-key_count // width)
    seg_pad = -(-seg_rows // 16) * 16
    seg_block = jnp.zeros((seg_pad * width,), jnp.bfloat16)
    seg_block = seg_block.at[:key_count].set(segment_ids.astype(jnp.bfloat16))
    seg_block = seg_block.reshape(seg_pad, width)
    split = rep_count == 2
    halves = [jnp.where(rep_at == 0, key, value)] if split else [key, value]
    payloads = [jnp.concatenate([h, seg_block], axis=0) for h in halves]
    gathered = []
    for payload in payloads:
        parts = [payload] + [
            lax.ppermute(payload, "ctx", [(i, (i + d) % n) for i in range(n)]) for d in range(1, n)
        ]
        gathered.append(parts)
    if split:
        mine = gathered[0]
        theirs = [lax.ppermute(p, "rep", [(0, 1), (1, 0)]) for p in mine]
        first = rep_at == 0
        key_parts = [jnp.where(first, a, b) for a, b in zip(mine, theirs)]
        value_parts = [jnp.where(first, b, a) for a, b in zip(mine, theirs)]
    else:
        key_parts, value_parts = gathered
    key_all = jnp.concatenate([p[:key_count] for p in key_parts], axis=0)
    value_all = jnp.concatenate([p[:key_count] for p in value_parts], axis=0)
    seg_all = jnp.concatenate(
        [p[key_count:].reshape(-1)[:key_count] for p in key_parts], axis=0
    ).astype(jnp.int32)
    source = (ctx_at - jnp.arange(n, dtype=jnp.int32)) % n
    key_pos = (source[:, None] * key_count + jnp.arange(key_count, dtype=jnp.int32)[None, :])
    return key_all, value_all, seg_all, key_pos.reshape(1, -1), source


def butterfly_sum(total, axes):
    for axis in axes:
        n = lax.axis_size(axis)
        if n & (n - 1):
            total = lax.psum(total, axis)
            continue
        bit = 1
        while bit < n:
            total = total + lax.ppermute(total, axis, [(i, i ^ bit) for i in range(n)])
            bit *= 2
    return total


def local(query, key, value, out_weight, cotangent, response, segment_ids, masked_segments):
    ctx_count = lax.axis_size("ctx")
    rep_count = lax.axis_size("rep")
    head_count = lax.axis_size("head")
    ctx_at = lax.axis_index("ctx")
    rep_at = lax.axis_index("rep")
    head_at = lax.axis_index("head")
    query_count = query.shape[0]
    key_count = key.shape[0]
    kv_local = key.shape[1] // HD
    heads_local = query.shape[1] // HD
    group_size = heads_local // kv_local
    context_len = key_count * ctx_count
    query_base = context_len - query_count * ctx_count * rep_count
    base = (query_base + (ctx_at * rep_count + rep_at) * query_count).astype(jnp.int32)
    base = jnp.reshape(base, (1,))

    key_all, value_all, seg_shift, key_pos, source = gather_kv(
        key, value, segment_ids, ctx_at, rep_at, rep_count
    )
    kept = jnp.where(
        jnp.any(seg_shift[:, None] == masked_segments[None, :], axis=1), 0.0, 1.0
    ).astype(jnp.float32)[None, :]

    grad_masked = jnp.where(response[:, None] > 0, cotangent, jnp.zeros_like(cotangent))
    grad_out = jnp.dot(grad_masked, out_weight.T, preferred_element_type=jnp.float32).astype(
        jnp.bfloat16
    )
    delta, attr, projected = fused_attention(
        base, key_pos, query, key_all, value_all, kept, grad_out, out_weight, group_size
    )

    inverse = (ctx_at - jnp.arange(ctx_count, dtype=jnp.int32)) % ctx_count
    attr_abs = attr.reshape(ctx_count, key_count)[inverse].reshape(-1)
    seg_abs = seg_shift.reshape(ctx_count, key_count)[inverse].reshape(-1)
    attr_all = butterfly_sum(attr_abs, ("rep", "head", "ctx"))

    if head_count == 2:
        cols = projected.shape[1] // 2
        keep = lax.dynamic_slice_in_dim(projected, head_at * cols, cols, 1)
        send = lax.dynamic_slice_in_dim(projected, (1 - head_at) * cols, cols, 1)
        got = lax.ppermute(send.astype(jnp.bfloat16), "head", [(0, 1), (1, 0)])
        patch_effect = (keep + got.astype(jnp.float32)).astype(jnp.bfloat16)
    else:
        patch_effect = lax.psum_scatter(
            projected.astype(jnp.bfloat16), "head", scatter_dimension=1, tiled=True
        )

    token_attr = lax.dynamic_slice_in_dim(attr_all, ctx_at * key_count, key_count, 0)
    onehot = (
        seg_abs[:, None] == jnp.arange(SEG_DEV * ctx_count, dtype=jnp.int32)[None, :]
    ).astype(jnp.float32)
    segment_attr = jnp.dot(attr_all, onehot, precision=lax.Precision.HIGHEST)
    return (patch_effect, token_attr, segment_attr)


def solution(mesh):
    return jax.shard_map(
        local,
        mesh=mesh,
        in_specs=(
            P(("groups", "ctx", "rep"), "head"),
            P(("groups", "ctx"), "head"),
            P(("groups", "ctx"), "head"),
            P("head", None),
            P(("groups", "ctx", "rep"), None),
            P(("groups", "ctx", "rep")),
            P(("groups", "ctx")),
            P("groups"),
        ),
        out_specs=(P(("groups", "ctx", "rep"), "head"), P(("groups", "ctx")), P("groups")),
        check_vma=False,
    )
```

```python
import functools

import jax
import jax.numpy as jnp
from jax import lax
from jax.experimental import pallas as pl
from jax.experimental.pallas import tpu as pltpu
from jax.sharding import PartitionSpec as P

HD = 128
SEG_DEV = 8
NEG_FILL = -1e30
NT_DIMS = (((1,), (1,)), ((), ()))


def attention_kernel(base_ref, kpos_ref, q_ref, k_ref, v_ref, kept_ref, do_ref, delta_ref, attr_ref, *, tq):
    r = pl.program_id(2)
    first = (pl.program_id(0) == 0) & (pl.program_id(1) == 0) & (r == 0)

    @pl.when(first)
    def _():
        attr_ref[...] = jnp.zeros_like(attr_ref)

    q = q_ref[...]
    k = k_ref[...]
    v = v_ref[...]
    keys = k.shape[0]
    s = lax.dot_general(q, k, NT_DIMS, preferred_element_type=jnp.float32) * (HD ** -0.5)
    row_pos = base_ref[0] + r * tq + lax.broadcasted_iota(jnp.int32, (tq, keys), 0)
    vis = kpos_ref[...] <= row_pos
    kvis = jnp.logical_and(vis, kept_ref[...] > 0.0)
    m_c = jnp.max(jnp.where(vis, s, NEG_FILL), axis=1, keepdims=True)
    m_m = jnp.max(jnp.where(kvis, s, NEG_FILL), axis=1, keepdims=True)
    e_c = jnp.where(vis, jnp.exp(s - m_c), 0.0)
    e_m = jnp.where(kvis, jnp.exp(s - m_m), 0.0)
    l_c = jnp.sum(e_c, axis=1, keepdims=True)
    l_m = jnp.sum(e_m, axis=1, keepdims=True)
    o_c = jnp.dot(e_c.astype(jnp.bfloat16), v, preferred_element_type=jnp.float32) / l_c
    o_m = jnp.dot(e_m.astype(jnp.bfloat16), v, preferred_element_type=jnp.float32) / l_m
    delta_ref[...] = (o_m - o_c).astype(delta_ref.dtype)
    g_rows = do_ref[...]
    row_dot = jnp.sum(g_rows.astype(jnp.float32) * o_c, axis=1, keepdims=True)
    d_p = lax.dot_general(g_rows, v, NT_DIMS, preferred_element_type=jnp.float32)
    log_total = m_c + jnp.log(l_c)
    prob = e_c * (1.0 / l_c)
    contrib = prob * (d_p + (d_p - row_dot) * (s - log_total))
    attr_ref[...] += jnp.sum(contrib, axis=0, keepdims=True)


def fused_attention(base, key_pos, query, key_all, value_all, kept, grad_out, group_size):
    qc, width = query.shape
    keys, kv_width = key_all.shape
    kv_local = kv_width // HD
    tq = max(8, min(qc, (128 * 2048) // keys))
    n_rows = qc // tq
    grid = (kv_local, group_size, n_rows)

    def head_map(g, j, r, b):
        return (r, g * group_size + j)

    def kv_map(g, j, r, b):
        return (0, g)

    def fixed(g, j, r, b):
        return (0, 0)

    flops = 8 * qc * keys * HD * kv_local * group_size
    cost = pl.CostEstimate(
        flops=flops,
        transcendentals=2 * qc * keys * kv_local * group_size,
        bytes_accessed=2 * (query.size + key_all.size + value_all.size + grad_out.size + query.size)
        + 4 * keys,
    )
    return pl.pallas_call(
        functools.partial(attention_kernel, tq=tq),
        grid_spec=pltpu.PrefetchScalarGridSpec(
            num_scalar_prefetch=1,
            grid=grid,
            in_specs=[
                pl.BlockSpec((1, keys), fixed),
                pl.BlockSpec((tq, HD), head_map),
                pl.BlockSpec((keys, HD), kv_map),
                pl.BlockSpec((keys, HD), kv_map),
                pl.BlockSpec((1, keys), fixed),
                pl.BlockSpec((tq, HD), head_map),
            ],
            out_specs=[
                pl.BlockSpec((tq, HD), head_map),
                pl.BlockSpec((1, keys), fixed),
            ],
        ),
        out_shape=[
            jax.ShapeDtypeStruct((qc, width), jnp.bfloat16),
            jax.ShapeDtypeStruct((1, keys), jnp.float32),
        ],
        compiler_params=pltpu.CompilerParams(
            dimension_semantics=("arbitrary", "arbitrary", "arbitrary")
        ),
        cost_estimate=cost,
    )(base, key_pos, query, key_all, value_all, kept, grad_out)


def relay_gather(payload, needed, ctx_at):
    n = lax.axis_size("ctx")
    zero = jnp.zeros_like(payload)
    forward, backward = [payload], [payload]
    for k in range(1, n):
        pairs = [(i, i + 1) for i in range(k - 1, n - 1) if needed(i + 1, i + 1 - k)]
        forward.append(lax.ppermute(forward[-1], "ctx", pairs) if pairs else zero)
        pairs = [(i + 1, i) for i in range(0, n - k) if needed(i, i + k)]
        backward.append(lax.ppermute(backward[-1], "ctx", pairs) if pairs else zero)
    parts = [payload]
    for k in range(1, n):
        parts.append(jnp.where(k <= ctx_at, forward[k], backward[n - k]))
    return parts


def gather_kv(key, value, segment_ids, ctx_at, rep_at, rep_count, needed):
    n = lax.axis_size("ctx")
    key_count, width = key.shape
    seg_rows = -(-key_count // width)
    seg_pad = -(-seg_rows // 16) * 16
    seg_block = jnp.zeros((seg_pad * width,), jnp.bfloat16)
    seg_block = seg_block.at[:key_count].set(segment_ids.astype(jnp.bfloat16))
    seg_block = seg_block.reshape(seg_pad, width)
    split = rep_count == 2
    halves = [jnp.where(rep_at == 0, key, value)] if split else [key, value]
    payloads = [jnp.concatenate([h, seg_block], axis=0) for h in halves]
    gathered = [relay_gather(p, needed, ctx_at) for p in payloads]
    if split:
        mine = gathered[0]
        theirs = [lax.ppermute(p, "rep", [(0, 1), (1, 0)]) for p in mine]
        first = rep_at == 0
        key_parts = [jnp.where(first, a, b) for a, b in zip(mine, theirs)]
        value_parts = [jnp.where(first, b, a) for a, b in zip(mine, theirs)]
    else:
        key_parts, value_parts = gathered
    key_all = jnp.concatenate([p[:key_count] for p in key_parts], axis=0)
    value_all = jnp.concatenate([p[:key_count] for p in value_parts], axis=0)
    seg_all = jnp.concatenate(
        [p[key_count:].reshape(-1)[:key_count] for p in key_parts], axis=0
    ).astype(jnp.int32)
    source = (ctx_at - jnp.arange(n, dtype=jnp.int32)) % n
    key_pos = (source[:, None] * key_count + jnp.arange(key_count, dtype=jnp.int32)[None, :])
    return key_all, value_all, seg_all, key_pos.reshape(1, -1), source


def butterfly_sum(total, axes):
    for axis in axes:
        n = lax.axis_size(axis)
        if n & (n - 1):
            total = lax.psum(total, axis)
            continue
        bit = 1
        while bit < n:
            total = total + lax.ppermute(total, axis, [(i, i ^ bit) for i in range(n)])
            bit *= 2
    return total


def local(query, key, value, out_weight, cotangent, response, segment_ids, masked_segments):
    ctx_count = lax.axis_size("ctx")
    rep_count = lax.axis_size("rep")
    head_count = lax.axis_size("head")
    ctx_at = lax.axis_index("ctx")
    rep_at = lax.axis_index("rep")
    head_at = lax.axis_index("head")
    query_count = query.shape[0]
    key_count = key.shape[0]
    kv_local = key.shape[1] // HD
    heads_local = query.shape[1] // HD
    group_size = heads_local // kv_local
    context_len = key_count * ctx_count
    query_base = context_len - query_count * ctx_count * rep_count
    base = (query_base + (ctx_at * rep_count + rep_at) * query_count).astype(jnp.int32)
    base = jnp.reshape(base, (1,))

    def needed(receiver, block):
        last_query = query_base + (receiver * rep_count + rep_count) * query_count - 1
        return block * key_count <= last_query

    key_all, value_all, seg_shift, key_pos, source = gather_kv(
        key, value, segment_ids, ctx_at, rep_at, rep_count, needed
    )
    kept = jnp.where(
        jnp.any(seg_shift[:, None] == masked_segments[None, :], axis=1), 0.0, 1.0
    ).astype(jnp.float32)[None, :]

    grad_masked = jnp.where(response[:, None] > 0, cotangent, jnp.zeros_like(cotangent))
    grad_out = jnp.dot(grad_masked, out_weight.T, preferred_element_type=jnp.float32).astype(
        jnp.bfloat16
    )
    delta, attr = fused_attention(
        base, key_pos, query, key_all, value_all, kept, grad_out, group_size
    )

    inverse = (ctx_at - jnp.arange(ctx_count, dtype=jnp.int32)) % ctx_count
    attr_abs = attr.reshape(ctx_count, key_count)[inverse].reshape(-1)
    seg_abs = seg_shift.reshape(ctx_count, key_count)[inverse].reshape(-1)
    onehot = (
        seg_abs[:, None] == jnp.arange(SEG_DEV * ctx_count, dtype=jnp.int32)[None, :]
    ).astype(jnp.float32)
    seg_part = jnp.dot(attr_abs, onehot, precision=lax.Precision.HIGHEST)
    summed = butterfly_sum(jnp.concatenate([attr_abs, seg_part]), ("rep", "head", "ctx"))
    attr_all = summed[:context_len]
    segment_attr = summed[context_len:]

    projected = jnp.dot(delta, out_weight, preferred_element_type=jnp.float32)
    if head_count == 2:
        cols = projected.shape[1] // 2
        keep = lax.dynamic_slice_in_dim(projected, head_at * cols, cols, 1)
        send = lax.dynamic_slice_in_dim(projected, (1 - head_at) * cols, cols, 1)
        got = lax.ppermute(send.astype(jnp.bfloat16), "head", [(0, 1), (1, 0)])
        patch_effect = (keep + got.astype(jnp.float32)).astype(jnp.bfloat16)
    else:
        patch_effect = lax.psum_scatter(
            projected.astype(jnp.bfloat16), "head", scatter_dimension=1, tiled=True
        )

    token_attr = lax.dynamic_slice_in_dim(attr_all, ctx_at * key_count, key_count, 0)
    return (patch_effect, token_attr, segment_attr)


def solution(mesh):
    return jax.shard_map(
        local,
        mesh=mesh,
        in_specs=(
            P(("groups", "ctx", "rep"), "head"),
            P(("groups", "ctx"), "head"),
            P(("groups", "ctx"), "head"),
            P("head", None),
            P(("groups", "ctx", "rep"), None),
            P(("groups", "ctx", "rep")),
            P(("groups", "ctx")),
            P("groups"),
        ),
        out_specs=(P(("groups", "ctx", "rep"), "head"), P(("groups", "ctx")), P("groups")),
        check_vma=False,
    )
```

```python
import functools

import jax
import jax.numpy as jnp
from jax import lax
from jax.experimental import pallas as pl
from jax.experimental.pallas import tpu as pltpu
from jax.sharding import PartitionSpec as P

HD = 128
SEG_DEV = 8
NEG_FILL = -1e30
NT_DIMS = (((1,), (1,)), ((), ()))


def attention_kernel(base_ref, kpos_ref, q_ref, k_ref, v_ref, kept_ref, do_ref, delta_ref, attr_ref, *, tq):
    r = pl.program_id(2)
    first = (pl.program_id(0) == 0) & (pl.program_id(1) == 0) & (r == 0)

    @pl.when(first)
    def _():
        attr_ref[...] = jnp.zeros_like(attr_ref)

    q = q_ref[...]
    k = k_ref[...]
    v = v_ref[...]
    keys = k.shape[0]
    s = lax.dot_general(q, k, NT_DIMS, preferred_element_type=jnp.float32) * (HD ** -0.5)
    row_pos = base_ref[0] + r * tq + lax.broadcasted_iota(jnp.int32, (tq, keys), 0)
    vis = kpos_ref[...] <= row_pos
    kvis = jnp.logical_and(vis, kept_ref[...] > 0.0)
    m_c = jnp.max(jnp.where(vis, s, NEG_FILL), axis=1, keepdims=True)
    m_m = jnp.max(jnp.where(kvis, s, NEG_FILL), axis=1, keepdims=True)
    e_c = jnp.where(vis, jnp.exp(s - m_c), 0.0)
    e_m = jnp.where(kvis, jnp.exp(s - m_m), 0.0)
    l_c = jnp.sum(e_c, axis=1, keepdims=True)
    l_m = jnp.sum(e_m, axis=1, keepdims=True)
    o_c = jnp.dot(e_c.astype(jnp.bfloat16), v, preferred_element_type=jnp.float32) / l_c
    o_m = jnp.dot(e_m.astype(jnp.bfloat16), v, preferred_element_type=jnp.float32) / l_m
    delta_ref[...] = (o_m - o_c).astype(delta_ref.dtype)
    g_rows = do_ref[...]
    row_dot = jnp.sum(g_rows.astype(jnp.float32) * o_c, axis=1, keepdims=True)
    d_p = lax.dot_general(g_rows, v, NT_DIMS, preferred_element_type=jnp.float32)
    log_total = m_c + jnp.log(l_c)
    prob = e_c * (1.0 / l_c)
    contrib = prob * (d_p + (d_p - row_dot) * (s - log_total))
    attr_ref[...] += jnp.sum(contrib, axis=0, keepdims=True)


def fused_attention(base, key_pos, query, key_all, value_all, kept, grad_out, group_size):
    qc, width = query.shape
    keys, kv_width = key_all.shape
    kv_local = kv_width // HD
    tq = max(8, min(qc, (128 * 2048) // keys))
    n_rows = qc // tq
    grid = (kv_local, group_size, n_rows)

    def head_map(g, j, r, b):
        return (r, g * group_size + j)

    def kv_map(g, j, r, b):
        return (0, g)

    def fixed(g, j, r, b):
        return (0, 0)

    flops = 8 * qc * keys * HD * kv_local * group_size
    cost = pl.CostEstimate(
        flops=flops,
        transcendentals=2 * qc * keys * kv_local * group_size,
        bytes_accessed=2 * (query.size + key_all.size + value_all.size + grad_out.size + query.size)
        + 4 * keys,
    )
    return pl.pallas_call(
        functools.partial(attention_kernel, tq=tq),
        grid_spec=pltpu.PrefetchScalarGridSpec(
            num_scalar_prefetch=1,
            grid=grid,
            in_specs=[
                pl.BlockSpec((1, keys), fixed),
                pl.BlockSpec((tq, HD), head_map),
                pl.BlockSpec((keys, HD), kv_map),
                pl.BlockSpec((keys, HD), kv_map),
                pl.BlockSpec((1, keys), fixed),
                pl.BlockSpec((tq, HD), head_map),
            ],
            out_specs=[
                pl.BlockSpec((tq, HD), head_map),
                pl.BlockSpec((1, keys), fixed),
            ],
        ),
        out_shape=[
            jax.ShapeDtypeStruct((qc, width), jnp.bfloat16),
            jax.ShapeDtypeStruct((1, keys), jnp.float32),
        ],
        compiler_params=pltpu.CompilerParams(
            dimension_semantics=("arbitrary", "arbitrary", "arbitrary")
        ),
        cost_estimate=cost,
    )(base, key_pos, query, key_all, value_all, kept, grad_out)


def relay_gather(payload, needed, ctx_at):
    n = lax.axis_size("ctx")
    zero = jnp.zeros_like(payload)
    forward, backward = [payload], [payload]
    for k in range(1, n):
        fwd = [(i, i + k) for i in range(n - k) if needed(i + k, i)]
        relay = [(i + k - 1, i + k) for i, _ in fwd]
        if k > 2 and relay and all(needed(s, r - k) for s, r in relay):
            forward.append(lax.ppermute(forward[-1], "ctx", relay))
        else:
            forward.append(lax.ppermute(payload, "ctx", fwd) if fwd else zero)
        bwd = [(i + k, i) for i in range(n - k) if needed(i, i + k)]
        relay = [(r + 1, r) for _, r in bwd]
        if k > 2 and relay and all(needed(s, r + k) for s, r in relay):
            backward.append(lax.ppermute(backward[-1], "ctx", relay))
        else:
            backward.append(lax.ppermute(payload, "ctx", bwd) if bwd else zero)
    parts = [payload]
    for k in range(1, n):
        parts.append(jnp.where(k <= ctx_at, forward[k], backward[n - k]))
    return parts


def gather_kv(key, value, segment_ids, ctx_at, rep_at, rep_count, needed):
    n = lax.axis_size("ctx")
    key_count, width = key.shape
    seg_rows = -(-key_count // width)
    seg_pad = -(-seg_rows // 16) * 16
    seg_block = jnp.zeros((seg_pad * width,), jnp.bfloat16)
    seg_block = seg_block.at[:key_count].set(segment_ids.astype(jnp.bfloat16))
    seg_block = seg_block.reshape(seg_pad, width)
    split = rep_count == 2
    halves = [jnp.where(rep_at == 0, key, value)] if split else [key, value]
    payloads = [jnp.concatenate([h, seg_block], axis=0) for h in halves]
    gathered = [relay_gather(p, needed, ctx_at) for p in payloads]
    if split:
        mine = gathered[0]
        theirs = [lax.ppermute(p, "rep", [(0, 1), (1, 0)]) for p in mine]
        first = rep_at == 0
        key_parts = [jnp.where(first, a, b) for a, b in zip(mine, theirs)]
        value_parts = [jnp.where(first, b, a) for a, b in zip(mine, theirs)]
    else:
        key_parts, value_parts = gathered
    key_all = jnp.concatenate([p[:key_count] for p in key_parts], axis=0)
    value_all = jnp.concatenate([p[:key_count] for p in value_parts], axis=0)
    seg_all = jnp.concatenate(
        [p[key_count:].reshape(-1)[:key_count] for p in key_parts], axis=0
    ).astype(jnp.int32)
    source = (ctx_at - jnp.arange(n, dtype=jnp.int32)) % n
    key_pos = (source[:, None] * key_count + jnp.arange(key_count, dtype=jnp.int32)[None, :])
    return key_all, value_all, seg_all, key_pos.reshape(1, -1), source


def butterfly_sum(total, axes):
    for axis in axes:
        n = lax.axis_size(axis)
        if n & (n - 1):
            total = lax.psum(total, axis)
            continue
        bit = 1
        while bit < n:
            total = total + lax.ppermute(total, axis, [(i, i ^ bit) for i in range(n)])
            bit *= 2
    return total


def local(query, key, value, out_weight, cotangent, response, segment_ids, masked_segments):
    ctx_count = lax.axis_size("ctx")
    rep_count = lax.axis_size("rep")
    head_count = lax.axis_size("head")
    ctx_at = lax.axis_index("ctx")
    rep_at = lax.axis_index("rep")
    head_at = lax.axis_index("head")
    query_count = query.shape[0]
    key_count = key.shape[0]
    kv_local = key.shape[1] // HD
    heads_local = query.shape[1] // HD
    group_size = heads_local // kv_local
    context_len = key_count * ctx_count
    query_base = context_len - query_count * ctx_count * rep_count
    base = (query_base + (ctx_at * rep_count + rep_at) * query_count).astype(jnp.int32)
    base = jnp.reshape(base, (1,))

    def needed(receiver, block):
        last_query = query_base + (receiver * rep_count + rep_count) * query_count - 1
        return block * key_count <= last_query

    key_all, value_all, seg_shift, key_pos, source = gather_kv(
        key, value, segment_ids, ctx_at, rep_at, rep_count, needed
    )
    kept = jnp.where(
        jnp.any(seg_shift[:, None] == masked_segments[None, :], axis=1), 0.0, 1.0
    ).astype(jnp.float32)[None, :]

    grad_masked = jnp.where(response[:, None] > 0, cotangent, jnp.zeros_like(cotangent))
    grad_out = jnp.dot(grad_masked, out_weight.T, preferred_element_type=jnp.float32).astype(
        jnp.bfloat16
    )
    delta, attr = fused_attention(
        base, key_pos, query, key_all, value_all, kept, grad_out, group_size
    )

    inverse = (ctx_at - jnp.arange(ctx_count, dtype=jnp.int32)) % ctx_count
    attr_abs = attr.reshape(ctx_count, key_count)[inverse].reshape(-1)
    seg_abs = seg_shift.reshape(ctx_count, key_count)[inverse].reshape(-1)
    onehot = (
        seg_abs[:, None] == jnp.arange(SEG_DEV * ctx_count, dtype=jnp.int32)[None, :]
    ).astype(jnp.float32)
    seg_part = jnp.dot(attr_abs, onehot, precision=lax.Precision.HIGHEST)
    summed = butterfly_sum(jnp.concatenate([attr_abs, seg_part]), ("rep", "ctx", "head"))
    attr_all = summed[:context_len]
    segment_attr = summed[context_len:]

    projected = jnp.dot(delta, out_weight, preferred_element_type=jnp.float32)
    if head_count == 2:
        cols = projected.shape[1] // 2
        keep = lax.dynamic_slice_in_dim(projected, head_at * cols, cols, 1)
        send = lax.dynamic_slice_in_dim(projected, (1 - head_at) * cols, cols, 1)
        got = lax.ppermute(send.astype(jnp.bfloat16), "head", [(0, 1), (1, 0)])
        patch_effect = (keep + got.astype(jnp.float32)).astype(jnp.bfloat16)
    else:
        patch_effect = lax.psum_scatter(
            projected.astype(jnp.bfloat16), "head", scatter_dimension=1, tiled=True
        )

    token_attr = lax.dynamic_slice_in_dim(attr_all, ctx_at * key_count, key_count, 0)
    return (patch_effect, token_attr, segment_attr)


def solution(mesh):
    return jax.shard_map(
        local,
        mesh=mesh,
        in_specs=(
            P(("groups", "ctx", "rep"), "head"),
            P(("groups", "ctx"), "head"),
            P(("groups", "ctx"), "head"),
            P("head", None),
            P(("groups", "ctx", "rep"), None),
            P(("groups", "ctx", "rep")),
            P(("groups", "ctx")),
            P("groups"),
        ),
        out_specs=(P(("groups", "ctx", "rep"), "head"), P(("groups", "ctx")), P("groups")),
        check_vma=False,
    )
```

```python
import functools

import jax
import jax.numpy as jnp
from jax import lax
from jax.experimental import pallas as pl
from jax.experimental.pallas import tpu as pltpu
from jax.sharding import PartitionSpec as P

HD = 128
SEG_DEV = 8
NEG_FILL = -1e30
NT_DIMS = (((1,), (1,)), ((), ()))


def attention_kernel(
    base_ref, kpos_ref, q_ref, k_ref, v_ref, kept_ref, gm_ref, w_ref, delta_ref, attr_ref, *, tq
):
    r = pl.program_id(2)
    first = (pl.program_id(0) == 0) & (pl.program_id(1) == 0) & (r == 0)

    @pl.when(first)
    def _():
        attr_ref[...] = jnp.zeros_like(attr_ref)

    q = q_ref[...]
    k = k_ref[...]
    v = v_ref[...]
    keys = k.shape[0]
    s = lax.dot_general(q, k, NT_DIMS, preferred_element_type=jnp.float32) * (HD ** -0.5)
    row_pos = base_ref[0] + r * tq + lax.broadcasted_iota(jnp.int32, (tq, keys), 0)
    vis = kpos_ref[...] <= row_pos
    s_c = jnp.where(vis, s, NEG_FILL)
    s_m = jnp.where(kept_ref[...] > 0.0, s_c, NEG_FILL)
    m_c = jnp.max(s_c, axis=1, keepdims=True)
    m_m = jnp.max(s_m, axis=1, keepdims=True)
    e_c = jnp.exp(s_c - m_c)
    e_m = jnp.exp(s_m - m_m)
    l_c = jnp.sum(e_c, axis=1, keepdims=True)
    l_m = jnp.sum(e_m, axis=1, keepdims=True)
    o_c = jnp.dot(e_c.astype(jnp.bfloat16), v, preferred_element_type=jnp.float32) / l_c
    o_m = jnp.dot(e_m.astype(jnp.bfloat16), v, preferred_element_type=jnp.float32) / l_m
    delta_ref[...] = (o_m - o_c).astype(delta_ref.dtype)
    g_rows = lax.dot_general(
        gm_ref[...], w_ref[...], NT_DIMS, preferred_element_type=jnp.float32
    ).astype(jnp.bfloat16)
    row_dot = jnp.sum(g_rows.astype(jnp.float32) * o_c, axis=1, keepdims=True)
    d_p = lax.dot_general(g_rows, v, NT_DIMS, preferred_element_type=jnp.float32)
    log_total = m_c + jnp.log(l_c)
    prob = e_c * (1.0 / l_c)
    contrib = prob * (d_p + (d_p - row_dot) * (s - log_total))
    attr_ref[...] += jnp.sum(contrib, axis=0, keepdims=True)


def fused_attention(base, key_pos, query, key_all, value_all, kept, grad_rows, out_weight, group_size):
    qc, width = query.shape
    keys, kv_width = key_all.shape
    kv_local = kv_width // HD
    model = out_weight.shape[1]
    tq = max(8, min(qc, (128 * 2048) // keys))
    n_rows = qc // tq
    grid = (kv_local, group_size, n_rows)

    def head_map(g, j, r, b):
        return (r, g * group_size + j)

    def kv_map(g, j, r, b):
        return (0, g)

    def fixed(g, j, r, b):
        return (0, 0)

    def row_map(g, j, r, b):
        return (r, 0)

    def weight_map(g, j, r, b):
        return (g * group_size + j, 0)

    flops = 8 * qc * keys * HD * kv_local * group_size + 2 * qc * width * model
    cost = pl.CostEstimate(
        flops=flops,
        transcendentals=2 * qc * keys * kv_local * group_size,
        bytes_accessed=2 * (2 * query.size + key_all.size + value_all.size + out_weight.size)
        + 4 * keys,
    )
    return pl.pallas_call(
        functools.partial(attention_kernel, tq=tq),
        grid_spec=pltpu.PrefetchScalarGridSpec(
            num_scalar_prefetch=1,
            grid=grid,
            in_specs=[
                pl.BlockSpec((1, keys), fixed),
                pl.BlockSpec((tq, HD), head_map),
                pl.BlockSpec((keys, HD), kv_map),
                pl.BlockSpec((keys, HD), kv_map),
                pl.BlockSpec((1, keys), fixed),
                pl.BlockSpec((tq, model), row_map),
                pl.BlockSpec((HD, model), weight_map),
            ],
            out_specs=[
                pl.BlockSpec((tq, HD), head_map),
                pl.BlockSpec((1, keys), fixed),
            ],
        ),
        out_shape=[
            jax.ShapeDtypeStruct((qc, width), jnp.bfloat16),
            jax.ShapeDtypeStruct((1, keys), jnp.float32),
        ],
        compiler_params=pltpu.CompilerParams(
            dimension_semantics=("arbitrary", "arbitrary", "arbitrary")
        ),
        cost_estimate=cost,
    )(base, key_pos, query, key_all, value_all, kept, grad_rows, out_weight)


def relay_gather(payload, needed, ctx_at):
    n = lax.axis_size("ctx")
    zero = jnp.zeros_like(payload)
    forward, backward = [payload], [payload]
    for k in range(1, n):
        fwd = [(i, i + k) for i in range(n - k) if needed(i + k, i)]
        relay = [(i + k - 1, i + k) for i, _ in fwd]
        if k > 2 and relay and all(needed(s, r - k) for s, r in relay):
            forward.append(lax.ppermute(forward[-1], "ctx", relay))
        else:
            forward.append(lax.ppermute(payload, "ctx", fwd) if fwd else zero)
        bwd = [(i + k, i) for i in range(n - k) if needed(i, i + k)]
        relay = [(r + 1, r) for _, r in bwd]
        if k > 2 and relay and all(needed(s, r + k) for s, r in relay):
            backward.append(lax.ppermute(backward[-1], "ctx", relay))
        else:
            backward.append(lax.ppermute(payload, "ctx", bwd) if bwd else zero)
    parts = [payload]
    for k in range(1, n):
        parts.append(jnp.where(k <= ctx_at, forward[k], backward[n - k]))
    return parts


def gather_kv(key, value, segment_ids, ctx_at, rep_at, rep_count, needed):
    n = lax.axis_size("ctx")
    key_count, width = key.shape
    seg_rows = -(-key_count // width)
    seg_pad = -(-seg_rows // 16) * 16
    seg_block = jnp.zeros((seg_pad * width,), jnp.bfloat16)
    seg_block = seg_block.at[:key_count].set(segment_ids.astype(jnp.bfloat16))
    seg_block = seg_block.reshape(seg_pad, width)
    split = rep_count == 2
    halves = [jnp.where(rep_at == 0, key, value)] if split else [key, value]
    payloads = [jnp.concatenate([h, seg_block], axis=0) for h in halves]
    gathered = [relay_gather(p, needed, ctx_at) for p in payloads]
    if split:
        mine = gathered[0]
        theirs = [lax.ppermute(p, "rep", [(0, 1), (1, 0)]) for p in mine]
        first = rep_at == 0
        key_parts = [jnp.where(first, a, b) for a, b in zip(mine, theirs)]
        value_parts = [jnp.where(first, b, a) for a, b in zip(mine, theirs)]
    else:
        key_parts, value_parts = gathered
    key_all = jnp.concatenate([p[:key_count] for p in key_parts], axis=0)
    value_all = jnp.concatenate([p[:key_count] for p in value_parts], axis=0)
    seg_all = jnp.concatenate(
        [p[key_count:].reshape(-1)[:key_count] for p in key_parts], axis=0
    ).astype(jnp.int32)
    source = (ctx_at - jnp.arange(n, dtype=jnp.int32)) % n
    key_pos = (source[:, None] * key_count + jnp.arange(key_count, dtype=jnp.int32)[None, :])
    return key_all, value_all, seg_all, key_pos.reshape(1, -1), source


def butterfly_sum(total, axes):
    for axis in axes:
        n = lax.axis_size(axis)
        if n & (n - 1):
            total = lax.psum(total, axis)
            continue
        bit = 1
        while bit < n:
            total = total + lax.ppermute(total, axis, [(i, i ^ bit) for i in range(n)])
            bit *= 2
    return total


def local(query, key, value, out_weight, cotangent, response, segment_ids, masked_segments):
    ctx_count = lax.axis_size("ctx")
    rep_count = lax.axis_size("rep")
    head_count = lax.axis_size("head")
    ctx_at = lax.axis_index("ctx")
    rep_at = lax.axis_index("rep")
    head_at = lax.axis_index("head")
    query_count = query.shape[0]
    key_count = key.shape[0]
    kv_local = key.shape[1] // HD
    heads_local = query.shape[1] // HD
    group_size = heads_local // kv_local
    context_len = key_count * ctx_count
    query_base = context_len - query_count * ctx_count * rep_count
    base = (query_base + (ctx_at * rep_count + rep_at) * query_count).astype(jnp.int32)
    base = jnp.reshape(base, (1,))

    def needed(receiver, block):
        last_query = query_base + (receiver * rep_count + rep_count) * query_count - 1
        return block * key_count <= last_query

    key_all, value_all, seg_shift, key_pos, source = gather_kv(
        key, value, segment_ids, ctx_at, rep_at, rep_count, needed
    )
    kept = jnp.where(
        jnp.any(seg_shift[:, None] == masked_segments[None, :], axis=1), 0.0, 1.0
    ).astype(jnp.float32)[None, :]

    grad_masked = jnp.where(response[:, None] > 0, cotangent, jnp.zeros_like(cotangent))
    delta, attr = fused_attention(
        base, key_pos, query, key_all, value_all, kept, grad_masked, out_weight, group_size
    )

    inverse = (ctx_at - jnp.arange(ctx_count, dtype=jnp.int32)) % ctx_count
    attr_abs = attr.reshape(ctx_count, key_count)[inverse].reshape(-1)
    seg_abs = seg_shift.reshape(ctx_count, key_count)[inverse].reshape(-1)
    onehot = (
        seg_abs[:, None] == jnp.arange(SEG_DEV * ctx_count, dtype=jnp.int32)[None, :]
    ).astype(jnp.float32)
    seg_part = jnp.dot(attr_abs, onehot, precision=lax.Precision.HIGHEST)
    summed = butterfly_sum(jnp.concatenate([attr_abs, seg_part]), ("rep", "ctx", "head"))
    attr_all = summed[:context_len]
    segment_attr = summed[context_len:]

    projected = jnp.dot(delta, out_weight, preferred_element_type=jnp.float32)
    if head_count == 2:
        cols = projected.shape[1] // 2
        keep = lax.dynamic_slice_in_dim(projected, head_at * cols, cols, 1)
        send = lax.dynamic_slice_in_dim(projected, (1 - head_at) * cols, cols, 1)
        got = lax.ppermute(send.astype(jnp.bfloat16), "head", [(0, 1), (1, 0)])
        patch_effect = (keep + got.astype(jnp.float32)).astype(jnp.bfloat16)
    else:
        patch_effect = lax.psum_scatter(
            projected.astype(jnp.bfloat16), "head", scatter_dimension=1, tiled=True
        )

    token_attr = lax.dynamic_slice_in_dim(attr_all, ctx_at * key_count, key_count, 0)
    return (patch_effect, token_attr, segment_attr)


def solution(mesh):
    return jax.shard_map(
        local,
        mesh=mesh,
        in_specs=(
            P(("groups", "ctx", "rep"), "head"),
            P(("groups", "ctx"), "head"),
            P(("groups", "ctx"), "head"),
            P("head", None),
            P(("groups", "ctx", "rep"), None),
            P(("groups", "ctx", "rep")),
            P(("groups", "ctx")),
            P("groups"),
        ),
        out_specs=(P(("groups", "ctx", "rep"), "head"), P(("groups", "ctx")), P("groups")),
        check_vma=False,
    )
```

```python
import functools

import jax
import jax.numpy as jnp
from jax import lax
from jax.experimental import pallas as pl
from jax.experimental.pallas import tpu as pltpu
from jax.sharding import PartitionSpec as P

HD = 128
SEG_DEV = 8
NEG_FILL = -1e30
NT_DIMS = (((1,), (1,)), ((), ()))


def attention_kernel(base_ref, kpos_ref, q_ref, k_ref, v_ref, kept_ref, do_ref, delta_ref, attr_ref, *, tq):
    r = pl.program_id(2)
    first = (pl.program_id(0) == 0) & (pl.program_id(1) == 0) & (r == 0)

    @pl.when(first)
    def _():
        attr_ref[...] = jnp.zeros_like(attr_ref)

    q = q_ref[...]
    k = k_ref[...]
    v = v_ref[...]
    keys = k.shape[0]
    s = lax.dot_general(q, k, NT_DIMS, preferred_element_type=jnp.float32) * (HD ** -0.5)
    row_pos = base_ref[0] + r * tq + lax.broadcasted_iota(jnp.int32, (tq, keys), 0)
    vis = kpos_ref[...] <= row_pos
    s_c = jnp.where(vis, s, NEG_FILL)
    s_m = jnp.where(kept_ref[...] > 0.0, s_c, NEG_FILL)
    m_c = jnp.max(s_c, axis=1, keepdims=True)
    m_m = jnp.max(s_m, axis=1, keepdims=True)
    e_c = jnp.exp(s_c - m_c)
    e_m = jnp.exp(s_m - m_m)
    l_c = jnp.sum(e_c, axis=1, keepdims=True)
    l_m = jnp.sum(e_m, axis=1, keepdims=True)
    o_c = jnp.dot(e_c.astype(jnp.bfloat16), v, preferred_element_type=jnp.float32) / l_c
    o_m = jnp.dot(e_m.astype(jnp.bfloat16), v, preferred_element_type=jnp.float32) / l_m
    delta_ref[...] = (o_m - o_c).astype(delta_ref.dtype)
    g_rows = do_ref[...]
    row_dot = jnp.sum(g_rows.astype(jnp.float32) * o_c, axis=1, keepdims=True)
    d_p = lax.dot_general(g_rows, v, NT_DIMS, preferred_element_type=jnp.float32)
    log_total = m_c + jnp.log(l_c)
    prob = e_c * (1.0 / l_c)
    contrib = prob * (d_p + (d_p - row_dot) * (s - log_total))
    attr_ref[...] += jnp.sum(contrib, axis=0, keepdims=True)


def fused_attention(base, key_pos, query, key_all, value_all, kept, grad_out, group_size):
    qc, width = query.shape
    keys, kv_width = key_all.shape
    kv_local = kv_width // HD
    tq = max(8, min(qc, (128 * 2048) // keys))
    n_rows = qc // tq
    grid = (kv_local, group_size, n_rows)

    def head_map(g, j, r, b):
        return (r, g * group_size + j)

    def kv_map(g, j, r, b):
        return (0, g)

    def fixed(g, j, r, b):
        return (0, 0)

    flops = 8 * qc * keys * HD * kv_local * group_size
    cost = pl.CostEstimate(
        flops=flops,
        transcendentals=2 * qc * keys * kv_local * group_size,
        bytes_accessed=2 * (query.size + key_all.size + value_all.size + grad_out.size + query.size)
        + 4 * keys,
    )
    return pl.pallas_call(
        functools.partial(attention_kernel, tq=tq),
        grid_spec=pltpu.PrefetchScalarGridSpec(
            num_scalar_prefetch=1,
            grid=grid,
            in_specs=[
                pl.BlockSpec((1, keys), fixed),
                pl.BlockSpec((tq, HD), head_map),
                pl.BlockSpec((keys, HD), kv_map),
                pl.BlockSpec((keys, HD), kv_map),
                pl.BlockSpec((1, keys), fixed),
                pl.BlockSpec((tq, HD), head_map),
            ],
            out_specs=[
                pl.BlockSpec((tq, HD), head_map),
                pl.BlockSpec((1, keys), fixed),
            ],
        ),
        out_shape=[
            jax.ShapeDtypeStruct((qc, width), jnp.bfloat16),
            jax.ShapeDtypeStruct((1, keys), jnp.float32),
        ],
        compiler_params=pltpu.CompilerParams(
            dimension_semantics=("arbitrary", "arbitrary", "arbitrary")
        ),
        cost_estimate=cost,
    )(base, key_pos, query, key_all, value_all, kept, grad_out)


def relay_gather(payload, needed, ctx_at):
    n = lax.axis_size("ctx")
    zero = jnp.zeros_like(payload)
    forward, backward = [payload], [payload]
    for k in range(1, n):
        fwd = [(i, i + k) for i in range(n - k) if needed(i + k, i)]
        relay = [(i + k - 1, i + k) for i, _ in fwd]
        if k > 2 and relay and all(needed(s, r - k) for s, r in relay):
            forward.append(lax.ppermute(forward[-1], "ctx", relay))
        else:
            forward.append(lax.ppermute(payload, "ctx", fwd) if fwd else zero)
        bwd = [(i + k, i) for i in range(n - k) if needed(i, i + k)]
        relay = [(r + 1, r) for _, r in bwd]
        if k > 2 and relay and all(needed(s, r + k) for s, r in relay):
            backward.append(lax.ppermute(backward[-1], "ctx", relay))
        else:
            backward.append(lax.ppermute(payload, "ctx", bwd) if bwd else zero)
    parts = [payload]
    for k in range(1, n):
        parts.append(jnp.where(k <= ctx_at, forward[k], backward[n - k]))
    return parts


def gather_kv(key, value, segment_ids, ctx_at, rep_at, rep_count, needed):
    n = lax.axis_size("ctx")
    key_count, width = key.shape
    seg_rows = -(-key_count // width)
    seg_pad = -(-seg_rows // 16) * 16
    seg_block = jnp.zeros((seg_pad * width,), jnp.bfloat16)
    seg_block = seg_block.at[:key_count].set(segment_ids.astype(jnp.bfloat16))
    seg_block = seg_block.reshape(seg_pad, width)
    split = rep_count == 2
    halves = [jnp.where(rep_at == 0, key, value)] if split else [key, value]
    payloads = [jnp.concatenate([h, seg_block], axis=0) for h in halves]
    gathered = [relay_gather(p, needed, ctx_at) for p in payloads]
    if split:
        mine = gathered[0]
        theirs = [lax.ppermute(p, "rep", [(0, 1), (1, 0)]) for p in mine]
        first = rep_at == 0
        key_parts = [jnp.where(first, a, b) for a, b in zip(mine, theirs)]
        value_parts = [jnp.where(first, b, a) for a, b in zip(mine, theirs)]
    else:
        key_parts, value_parts = gathered
    key_all = jnp.concatenate([p[:key_count] for p in key_parts], axis=0)
    value_all = jnp.concatenate([p[:key_count] for p in value_parts], axis=0)
    seg_all = jnp.concatenate(
        [p[key_count:].reshape(-1)[:key_count] for p in key_parts], axis=0
    ).astype(jnp.int32)
    source = (ctx_at - jnp.arange(n, dtype=jnp.int32)) % n
    key_pos = (source[:, None] * key_count + jnp.arange(key_count, dtype=jnp.int32)[None, :])
    return key_all, value_all, seg_all, key_pos.reshape(1, -1), source


def ordered_sum(total, axes):
    sizes = [lax.axis_size(a) for a in axes]
    count = 1
    for size in sizes:
        count *= size
    if count > 16:
        return lax.psum(total, axes)
    at = 0
    for axis, size in zip(axes, sizes):
        at = at * size + lax.axis_index(axis)
    got = [total] + [
        lax.ppermute(total, axes, [(i, (i + d) % count) for i in range(count)])
        for d in range(1, count)
    ]
    stacked = jnp.stack(got)
    result = None
    for a in range(count):
        piece = lax.dynamic_index_in_dim(stacked, (at - a) % count, 0, keepdims=False)
        result = piece if result is None else result + piece
    return result


def local(query, key, value, out_weight, cotangent, response, segment_ids, masked_segments):
    ctx_count = lax.axis_size("ctx")
    rep_count = lax.axis_size("rep")
    head_count = lax.axis_size("head")
    ctx_at = lax.axis_index("ctx")
    rep_at = lax.axis_index("rep")
    head_at = lax.axis_index("head")
    query_count = query.shape[0]
    key_count = key.shape[0]
    kv_local = key.shape[1] // HD
    heads_local = query.shape[1] // HD
    group_size = heads_local // kv_local
    context_len = key_count * ctx_count
    query_base = context_len - query_count * ctx_count * rep_count
    base = (query_base + (ctx_at * rep_count + rep_at) * query_count).astype(jnp.int32)
    base = jnp.reshape(base, (1,))

    def needed(receiver, block):
        last_query = query_base + (receiver * rep_count + rep_count) * query_count - 1
        return block * key_count <= last_query

    key_all, value_all, seg_shift, key_pos, source = gather_kv(
        key, value, segment_ids, ctx_at, rep_at, rep_count, needed
    )
    kept = jnp.where(
        jnp.any(seg_shift[:, None] == masked_segments[None, :], axis=1), 0.0, 1.0
    ).astype(jnp.float32)[None, :]

    grad_masked = jnp.where(response[:, None] > 0, cotangent, jnp.zeros_like(cotangent))
    grad_out = jnp.dot(grad_masked, out_weight.T, preferred_element_type=jnp.float32).astype(
        jnp.bfloat16
    )
    delta, attr = fused_attention(
        base, key_pos, query, key_all, value_all, kept, grad_out, group_size
    )

    inverse = (ctx_at - jnp.arange(ctx_count, dtype=jnp.int32)) % ctx_count
    attr_abs = attr.reshape(ctx_count, key_count)[inverse].reshape(-1)
    seg_abs = seg_shift.reshape(ctx_count, key_count)[inverse].reshape(-1)
    onehot = (
        seg_abs[:, None] == jnp.arange(SEG_DEV * ctx_count, dtype=jnp.int32)[None, :]
    ).astype(jnp.float32)
    seg_part = jnp.dot(attr_abs, onehot, precision=lax.Precision.HIGHEST)
    summed = ordered_sum(jnp.concatenate([attr_abs, seg_part]), ("ctx", "head", "rep"))
    attr_all = summed[:context_len]
    segment_attr = summed[context_len:]

    projected = jnp.dot(delta, out_weight, preferred_element_type=jnp.float32)
    if head_count == 2:
        cols = projected.shape[1] // 2
        keep = lax.dynamic_slice_in_dim(projected, head_at * cols, cols, 1)
        send = lax.dynamic_slice_in_dim(projected, (1 - head_at) * cols, cols, 1)
        got = lax.ppermute(send.astype(jnp.bfloat16), "head", [(0, 1), (1, 0)])
        patch_effect = (keep + got.astype(jnp.float32)).astype(jnp.bfloat16)
    else:
        patch_effect = lax.psum_scatter(
            projected.astype(jnp.bfloat16), "head", scatter_dimension=1, tiled=True
        )

    token_attr = lax.dynamic_slice_in_dim(attr_all, ctx_at * key_count, key_count, 0)
    return (patch_effect, token_attr, segment_attr)


def solution(mesh):
    return jax.shard_map(
        local,
        mesh=mesh,
        in_specs=(
            P(("groups", "ctx", "rep"), "head"),
            P(("groups", "ctx"), "head"),
            P(("groups", "ctx"), "head"),
            P("head", None),
            P(("groups", "ctx", "rep"), None),
            P(("groups", "ctx", "rep")),
            P(("groups", "ctx")),
            P("groups"),
        ),
        out_specs=(P(("groups", "ctx", "rep"), "head"), P(("groups", "ctx")), P("groups")),
        check_vma=False,
    )
```

```python
import functools

import jax
import jax.numpy as jnp
from jax import lax
from jax.experimental import pallas as pl
from jax.experimental.pallas import tpu as pltpu
from jax.sharding import PartitionSpec as P

HD = 128
SEG_DEV = 8
NEG_FILL = -1e30
NT_DIMS = (((1,), (1,)), ((), ()))


def attention_kernel(base_ref, kpos_ref, q_ref, k_ref, v_ref, kept_ref, do_ref, delta_ref, attr_ref, *, tq):
    r = pl.program_id(2)
    first = (pl.program_id(0) == 0) & (pl.program_id(1) == 0) & (r == 0)

    @pl.when(first)
    def _():
        attr_ref[...] = jnp.zeros_like(attr_ref)

    q = q_ref[...]
    k = k_ref[...]
    v = v_ref[...]
    keys = k.shape[0]
    s = lax.dot_general(q, k, NT_DIMS, preferred_element_type=jnp.float32) * (HD ** -0.5)
    row_pos = base_ref[0] + r * tq + lax.broadcasted_iota(jnp.int32, (tq, keys), 0)
    vis = kpos_ref[...] <= row_pos
    s_c = jnp.where(vis, s, NEG_FILL)
    s_m = jnp.where(kept_ref[...] > 0.0, s_c, NEG_FILL)
    m_c = jnp.max(s_c, axis=1, keepdims=True)
    m_m = jnp.max(s_m, axis=1, keepdims=True)
    e_c = jnp.exp(s_c - m_c)
    e_m = jnp.exp(s_m - m_m)
    l_c = jnp.sum(e_c, axis=1, keepdims=True)
    l_m = jnp.sum(e_m, axis=1, keepdims=True)
    o_c = jnp.dot(e_c.astype(jnp.bfloat16), v, preferred_element_type=jnp.float32) / l_c
    o_m = jnp.dot(e_m.astype(jnp.bfloat16), v, preferred_element_type=jnp.float32) / l_m
    delta_ref[...] = (o_m - o_c).astype(delta_ref.dtype)
    g_rows = do_ref[...]
    row_dot = jnp.sum(g_rows.astype(jnp.float32) * o_c, axis=1, keepdims=True)
    d_p = lax.dot_general(g_rows, v, NT_DIMS, preferred_element_type=jnp.float32)
    log_total = m_c + jnp.log(l_c)
    prob = e_c * (1.0 / l_c)
    contrib = prob * (d_p + (d_p - row_dot) * (s - log_total))
    attr_ref[...] += jnp.sum(contrib, axis=0, keepdims=True)


def fused_attention(base, key_pos, query, key_all, value_all, kept, grad_out, group_size):
    qc, width = query.shape
    keys, kv_width = key_all.shape
    kv_local = kv_width // HD
    tq = max(8, min(qc, (128 * 2048) // keys))
    n_rows = qc // tq
    grid = (kv_local, group_size, n_rows)

    def head_map(g, j, r, b):
        return (r, g * group_size + j)

    def kv_map(g, j, r, b):
        return (0, g)

    def fixed(g, j, r, b):
        return (0, 0)

    flops = 8 * qc * keys * HD * kv_local * group_size
    cost = pl.CostEstimate(
        flops=flops,
        transcendentals=2 * qc * keys * kv_local * group_size,
        bytes_accessed=2 * (query.size + key_all.size + value_all.size + grad_out.size + query.size)
        + 4 * keys,
    )
    return pl.pallas_call(
        functools.partial(attention_kernel, tq=tq),
        grid_spec=pltpu.PrefetchScalarGridSpec(
            num_scalar_prefetch=1,
            grid=grid,
            in_specs=[
                pl.BlockSpec((1, keys), fixed),
                pl.BlockSpec((tq, HD), head_map),
                pl.BlockSpec((keys, HD), kv_map),
                pl.BlockSpec((keys, HD), kv_map),
                pl.BlockSpec((1, keys), fixed),
                pl.BlockSpec((tq, HD), head_map),
            ],
            out_specs=[
                pl.BlockSpec((tq, HD), head_map),
                pl.BlockSpec((1, keys), fixed),
            ],
        ),
        out_shape=[
            jax.ShapeDtypeStruct((qc, width), jnp.bfloat16),
            jax.ShapeDtypeStruct((1, keys), jnp.float32),
        ],
        compiler_params=pltpu.CompilerParams(
            dimension_semantics=("arbitrary", "arbitrary", "arbitrary")
        ),
        cost_estimate=cost,
    )(base, key_pos, query, key_all, value_all, kept, grad_out)


def relay_gather(payload, needed, ctx_at):
    n = lax.axis_size("ctx")
    zero = jnp.zeros_like(payload)
    forward, backward = [payload], [payload]
    for k in range(1, n):
        fwd = [(i, i + k) for i in range(n - k) if needed(i + k, i)]
        relay = [(i + k - 1, i + k) for i, _ in fwd]
        if k > 2 and relay and all(needed(s, r - k) for s, r in relay):
            forward.append(lax.ppermute(forward[-1], "ctx", relay))
        else:
            forward.append(lax.ppermute(payload, "ctx", fwd) if fwd else zero)
        bwd = [(i + k, i) for i in range(n - k) if needed(i, i + k)]
        relay = [(r + 1, r) for _, r in bwd]
        if k > 2 and relay and all(needed(s, r + k) for s, r in relay):
            backward.append(lax.ppermute(backward[-1], "ctx", relay))
        else:
            backward.append(lax.ppermute(payload, "ctx", bwd) if bwd else zero)
    parts = [payload]
    for k in range(1, n):
        parts.append(jnp.where(k <= ctx_at, forward[k], backward[n - k]))
    return parts


def gather_kv(key, value, segment_ids, ctx_at, rep_at, rep_count, needed):
    n = lax.axis_size("ctx")
    key_count, width = key.shape
    seg_rows = -(-key_count // width)
    seg_pad = -(-seg_rows // 16) * 16
    seg_block = jnp.zeros((seg_pad * width,), jnp.bfloat16)
    seg_block = seg_block.at[:key_count].set(segment_ids.astype(jnp.bfloat16))
    seg_block = seg_block.reshape(seg_pad, width)
    split = rep_count == 2
    halves = [jnp.where(rep_at == 0, key, value)] if split else [key, value]
    payloads = [jnp.concatenate([h, seg_block], axis=0) for h in halves]
    gathered = [relay_gather(p, needed, ctx_at) for p in payloads]
    if split:
        mine = gathered[0]
        theirs = [lax.ppermute(p, "rep", [(0, 1), (1, 0)]) for p in mine]
        first = rep_at == 0
        key_parts = [jnp.where(first, a, b) for a, b in zip(mine, theirs)]
        value_parts = [jnp.where(first, b, a) for a, b in zip(mine, theirs)]
    else:
        key_parts, value_parts = gathered
    key_all = jnp.concatenate([p[:key_count] for p in key_parts], axis=0)
    value_all = jnp.concatenate([p[:key_count] for p in value_parts], axis=0)
    seg_all = jnp.concatenate(
        [p[key_count:].reshape(-1)[:key_count] for p in key_parts], axis=0
    ).astype(jnp.int32)
    source = (ctx_at - jnp.arange(n, dtype=jnp.int32)) % n
    key_pos = (source[:, None] * key_count + jnp.arange(key_count, dtype=jnp.int32)[None, :])
    return key_all, value_all, seg_all, key_pos.reshape(1, -1), source


def butterfly_sum(total, axes):
    for axis in axes:
        n = lax.axis_size(axis)
        if n & (n - 1):
            total = lax.psum(total, axis)
            continue
        bit = 1
        while bit < n:
            total = total + lax.ppermute(total, axis, [(i, i ^ bit) for i in range(n)])
            bit *= 2
    return total


def local(query, key, value, out_weight, cotangent, response, segment_ids, masked_segments):
    ctx_count = lax.axis_size("ctx")
    rep_count = lax.axis_size("rep")
    head_count = lax.axis_size("head")
    ctx_at = lax.axis_index("ctx")
    rep_at = lax.axis_index("rep")
    head_at = lax.axis_index("head")
    query_count = query.shape[0]
    key_count = key.shape[0]
    kv_local = key.shape[1] // HD
    heads_local = query.shape[1] // HD
    group_size = heads_local // kv_local
    context_len = key_count * ctx_count
    query_base = context_len - query_count * ctx_count * rep_count
    base = (query_base + (ctx_at * rep_count + rep_at) * query_count).astype(jnp.int32)
    base = jnp.reshape(base, (1,))

    def needed(receiver, block):
        last_query = query_base + (receiver * rep_count + rep_count) * query_count - 1
        return block * key_count <= last_query

    key_all, value_all, seg_shift, key_pos, source = gather_kv(
        key, value, segment_ids, ctx_at, rep_at, rep_count, needed
    )
    kept = jnp.where(
        jnp.any(seg_shift[:, None] == masked_segments[None, :], axis=1), 0.0, 1.0
    ).astype(jnp.float32)[None, :]

    grad_masked = jnp.where(response[:, None] > 0, cotangent, jnp.zeros_like(cotangent))
    grad_out = jnp.dot(grad_masked, out_weight.T, preferred_element_type=jnp.float32).astype(
        jnp.bfloat16
    )
    delta, attr = fused_attention(
        base, key_pos, query, key_all, value_all, kept, grad_out, group_size
    )

    inverse = (ctx_at - jnp.arange(ctx_count, dtype=jnp.int32)) % ctx_count
    attr_abs = attr.reshape(ctx_count, key_count)[inverse].reshape(-1)
    seg_abs = seg_shift.reshape(ctx_count, key_count)[inverse].reshape(-1)
    onehot = (
        seg_abs[:, None] == jnp.arange(SEG_DEV * ctx_count, dtype=jnp.int32)[None, :]
    ).astype(jnp.float32)
    seg_part = jnp.dot(attr_abs, onehot, precision=lax.Precision.HIGHEST)
    summed = butterfly_sum(jnp.concatenate([attr_abs, seg_part]), ("rep", "ctx", "head"))
    attr_all = summed[:context_len]
    segment_attr = summed[context_len:]

    projected = jnp.dot(delta, out_weight, preferred_element_type=jnp.float32)
    if head_count == 2:
        cols = projected.shape[1] // 2
        keep = lax.dynamic_slice_in_dim(projected, head_at * cols, cols, 1)
        send = lax.dynamic_slice_in_dim(projected, (1 - head_at) * cols, cols, 1)
        got = lax.ppermute(send.astype(jnp.bfloat16), "head", [(0, 1), (1, 0)])
        patch_effect = (keep + got.astype(jnp.float32)).astype(jnp.bfloat16)
    else:
        patch_effect = lax.psum_scatter(
            projected.astype(jnp.bfloat16), "head", scatter_dimension=1, tiled=True
        )

    token_attr = lax.dynamic_slice_in_dim(attr_all, ctx_at * key_count, key_count, 0)
    return (patch_effect, token_attr, segment_attr)


def solution(mesh):
    return jax.shard_map(
        local,
        mesh=mesh,
        in_specs=(
            P(("groups", "ctx", "rep"), "head"),
            P(("groups", "ctx"), "head"),
            P(("groups", "ctx"), "head"),
            P("head", None),
            P(("groups", "ctx", "rep"), None),
            P(("groups", "ctx", "rep")),
            P(("groups", "ctx")),
            P("groups"),
        ),
        out_specs=(P(("groups", "ctx", "rep"), "head"), P(("groups", "ctx")), P("groups")),
        check_vma=False,
    )
```

```python
import functools

import jax
import jax.numpy as jnp
from jax import lax
from jax.experimental import pallas as pl
from jax.experimental.pallas import tpu as pltpu
from jax.sharding import PartitionSpec as P

HD = 128
SEG_DEV = 8
NEG_FILL = -1e30
NT_DIMS = (((1,), (1,)), ((), ()))


def attention_kernel(base_ref, kpos_ref, q_ref, k_ref, v_ref, kept_ref, do_ref, delta_ref, attr_ref, *, tq, hp):
    r = pl.program_id(2)
    first = (pl.program_id(0) == 0) & (pl.program_id(1) == 0) & (r == 0)

    @pl.when(first)
    def _():
        attr_ref[...] = jnp.zeros_like(attr_ref)

    k = k_ref[...]
    v = v_ref[...]
    row_pos = base_ref[0] + r * tq + lax.broadcasted_iota(jnp.int32, (tq, 1), 0)
    vis = kpos_ref[...] <= row_pos
    kept = kept_ref[...] > 0.0
    total = None
    for h in range(hp):
        cols = slice(h * HD, (h + 1) * HD)
        s = lax.dot_general(q_ref[:, cols], k, NT_DIMS, preferred_element_type=jnp.float32)
        s = s * (HD ** -0.5)
        s_c = jnp.where(vis, s, NEG_FILL)
        s_m = jnp.where(kept, s_c, NEG_FILL)
        m_c = jnp.max(s_c, axis=1, keepdims=True)
        m_m = jnp.max(s_m, axis=1, keepdims=True)
        e_c = jnp.exp(s_c - m_c)
        e_m = jnp.exp(s_m - m_m)
        l_c = jnp.sum(e_c, axis=1, keepdims=True)
        l_m = jnp.sum(e_m, axis=1, keepdims=True)
        o_c = jnp.dot(e_c.astype(jnp.bfloat16), v, preferred_element_type=jnp.float32) / l_c
        o_m = jnp.dot(e_m.astype(jnp.bfloat16), v, preferred_element_type=jnp.float32) / l_m
        delta_ref[:, cols] = (o_m - o_c).astype(delta_ref.dtype)
        g_rows = do_ref[:, cols]
        row_dot = jnp.sum(g_rows.astype(jnp.float32) * o_c, axis=1, keepdims=True)
        d_p = lax.dot_general(g_rows, v, NT_DIMS, preferred_element_type=jnp.float32)
        log_total = m_c + jnp.log(l_c)
        prob = e_c * (1.0 / l_c)
        contrib = prob * (d_p + (d_p - row_dot) * (s - log_total))
        part = jnp.sum(contrib, axis=0, keepdims=True)
        total = part if total is None else total + part
    attr_ref[...] += total


def fused_attention(base, key_pos, query, key_all, value_all, kept, grad_out, group_size):
    qc, width = query.shape
    keys, kv_width = key_all.shape
    kv_local = kv_width // HD
    tq = max(8, min(qc, (128 * 2048) // keys))
    n_rows = qc // tq
    hp = 2 if group_size % 2 == 0 else 1
    steps = group_size // hp
    grid = (kv_local, steps, n_rows)

    def head_map(g, j, r, b):
        return (r, g * steps + j)

    def kv_map(g, j, r, b):
        return (0, g)

    def fixed(g, j, r, b):
        return (0, 0)

    flops = 8 * qc * keys * HD * kv_local * group_size
    cost = pl.CostEstimate(
        flops=flops,
        transcendentals=2 * qc * keys * kv_local * group_size,
        bytes_accessed=2 * (query.size + key_all.size + value_all.size + grad_out.size + query.size)
        + 4 * keys,
    )
    return pl.pallas_call(
        functools.partial(attention_kernel, tq=tq, hp=hp),
        grid_spec=pltpu.PrefetchScalarGridSpec(
            num_scalar_prefetch=1,
            grid=grid,
            in_specs=[
                pl.BlockSpec((1, keys), fixed),
                pl.BlockSpec((tq, hp * HD), head_map),
                pl.BlockSpec((keys, HD), kv_map),
                pl.BlockSpec((keys, HD), kv_map),
                pl.BlockSpec((1, keys), fixed),
                pl.BlockSpec((tq, hp * HD), head_map),
            ],
            out_specs=[
                pl.BlockSpec((tq, hp * HD), head_map),
                pl.BlockSpec((1, keys), fixed),
            ],
        ),
        out_shape=[
            jax.ShapeDtypeStruct((qc, width), jnp.bfloat16),
            jax.ShapeDtypeStruct((1, keys), jnp.float32),
        ],
        compiler_params=pltpu.CompilerParams(
            dimension_semantics=("arbitrary", "arbitrary", "arbitrary")
        ),
        cost_estimate=cost,
    )(base, key_pos, query, key_all, value_all, kept, grad_out)


def relay_gather(payload, needed, ctx_at):
    n = lax.axis_size("ctx")
    zero = jnp.zeros_like(payload)
    forward, backward = [payload], [payload]
    for k in range(1, n):
        fwd = [(i, i + k) for i in range(n - k) if needed(i + k, i)]
        relay = [(i + k - 1, i + k) for i, _ in fwd]
        if k > 2 and relay and all(needed(s, r - k) for s, r in relay):
            forward.append(lax.ppermute(forward[-1], "ctx", relay))
        else:
            forward.append(lax.ppermute(payload, "ctx", fwd) if fwd else zero)
        bwd = [(i + k, i) for i in range(n - k) if needed(i, i + k)]
        relay = [(r + 1, r) for _, r in bwd]
        if k > 2 and relay and all(needed(s, r + k) for s, r in relay):
            backward.append(lax.ppermute(backward[-1], "ctx", relay))
        else:
            backward.append(lax.ppermute(payload, "ctx", bwd) if bwd else zero)
    parts = [payload]
    for k in range(1, n):
        parts.append(jnp.where(k <= ctx_at, forward[k], backward[n - k]))
    return parts


def gather_kv(key, value, segment_ids, ctx_at, rep_at, rep_count, needed):
    n = lax.axis_size("ctx")
    key_count, width = key.shape
    seg_rows = -(-key_count // width)
    seg_pad = -(-seg_rows // 16) * 16
    seg_block = jnp.zeros((seg_pad * width,), jnp.bfloat16)
    seg_block = seg_block.at[:key_count].set(segment_ids.astype(jnp.bfloat16))
    seg_block = seg_block.reshape(seg_pad, width)
    split = rep_count == 2
    halves = [jnp.where(rep_at == 0, key, value)] if split else [key, value]
    payloads = [jnp.concatenate([h, seg_block], axis=0) for h in halves]
    gathered = [relay_gather(p, needed, ctx_at) for p in payloads]
    if split:
        mine = gathered[0]
        theirs = [lax.ppermute(p, "rep", [(0, 1), (1, 0)]) for p in mine]
        first = rep_at == 0
        key_parts = [jnp.where(first, a, b) for a, b in zip(mine, theirs)]
        value_parts = [jnp.where(first, b, a) for a, b in zip(mine, theirs)]
    else:
        key_parts, value_parts = gathered
    key_all = jnp.concatenate([p[:key_count] for p in key_parts], axis=0)
    value_all = jnp.concatenate([p[:key_count] for p in value_parts], axis=0)
    seg_all = jnp.concatenate(
        [p[key_count:].reshape(-1)[:key_count] for p in key_parts], axis=0
    ).astype(jnp.int32)
    source = (ctx_at - jnp.arange(n, dtype=jnp.int32)) % n
    key_pos = (source[:, None] * key_count + jnp.arange(key_count, dtype=jnp.int32)[None, :])
    return key_all, value_all, seg_all, key_pos.reshape(1, -1), source


def butterfly_sum(total, axes):
    for axis in axes:
        n = lax.axis_size(axis)
        if n & (n - 1):
            total = lax.psum(total, axis)
            continue
        bit = 1
        while bit < n:
            total = total + lax.ppermute(total, axis, [(i, i ^ bit) for i in range(n)])
            bit *= 2
    return total


def local(query, key, value, out_weight, cotangent, response, segment_ids, masked_segments):
    ctx_count = lax.axis_size("ctx")
    rep_count = lax.axis_size("rep")
    head_count = lax.axis_size("head")
    ctx_at = lax.axis_index("ctx")
    rep_at = lax.axis_index("rep")
    head_at = lax.axis_index("head")
    query_count = query.shape[0]
    key_count = key.shape[0]
    kv_local = key.shape[1] // HD
    heads_local = query.shape[1] // HD
    group_size = heads_local // kv_local
    context_len = key_count * ctx_count
    query_base = context_len - query_count * ctx_count * rep_count
    base = (query_base + (ctx_at * rep_count + rep_at) * query_count).astype(jnp.int32)
    base = jnp.reshape(base, (1,))

    def needed(receiver, block):
        last_query = query_base + (receiver * rep_count + rep_count) * query_count - 1
        return block * key_count <= last_query

    key_all, value_all, seg_shift, key_pos, source = gather_kv(
        key, value, segment_ids, ctx_at, rep_at, rep_count, needed
    )
    kept = jnp.where(
        jnp.any(seg_shift[:, None] == masked_segments[None, :], axis=1), 0.0, 1.0
    ).astype(jnp.float32)[None, :]

    grad_masked = jnp.where(response[:, None] > 0, cotangent, jnp.zeros_like(cotangent))
    grad_out = jnp.dot(grad_masked, out_weight.T, preferred_element_type=jnp.float32).astype(
        jnp.bfloat16
    )
    delta, attr = fused_attention(
        base, key_pos, query, key_all, value_all, kept, grad_out, group_size
    )

    inverse = (ctx_at - jnp.arange(ctx_count, dtype=jnp.int32)) % ctx_count
    attr_abs = attr.reshape(ctx_count, key_count)[inverse].reshape(-1)
    seg_abs = seg_shift.reshape(ctx_count, key_count)[inverse].reshape(-1)
    onehot = (
        seg_abs[:, None] == jnp.arange(SEG_DEV * ctx_count, dtype=jnp.int32)[None, :]
    ).astype(jnp.float32)
    seg_part = jnp.dot(attr_abs, onehot, precision=lax.Precision.HIGHEST)
    summed = butterfly_sum(jnp.concatenate([attr_abs, seg_part]), ("rep", "ctx", "head"))
    attr_all = summed[:context_len]
    segment_attr = summed[context_len:]

    projected = jnp.dot(delta, out_weight, preferred_element_type=jnp.float32)
    if head_count == 2:
        cols = projected.shape[1] // 2
        keep = lax.dynamic_slice_in_dim(projected, head_at * cols, cols, 1)
        send = lax.dynamic_slice_in_dim(projected, (1 - head_at) * cols, cols, 1)
        got = lax.ppermute(send.astype(jnp.bfloat16), "head", [(0, 1), (1, 0)])
        patch_effect = (keep + got.astype(jnp.float32)).astype(jnp.bfloat16)
    else:
        patch_effect = lax.psum_scatter(
            projected.astype(jnp.bfloat16), "head", scatter_dimension=1, tiled=True
        )

    token_attr = lax.dynamic_slice_in_dim(attr_all, ctx_at * key_count, key_count, 0)
    return (patch_effect, token_attr, segment_attr)


def solution(mesh):
    return jax.shard_map(
        local,
        mesh=mesh,
        in_specs=(
            P(("groups", "ctx", "rep"), "head"),
            P(("groups", "ctx"), "head"),
            P(("groups", "ctx"), "head"),
            P("head", None),
            P(("groups", "ctx", "rep"), None),
            P(("groups", "ctx", "rep")),
            P(("groups", "ctx")),
            P("groups"),
        ),
        out_specs=(P(("groups", "ctx", "rep"), "head"), P(("groups", "ctx")), P("groups")),
        check_vma=False,
    )
```

```python
import functools

import jax
import jax.numpy as jnp
from jax import lax
from jax.experimental import pallas as pl
from jax.experimental.pallas import tpu as pltpu
from jax.sharding import PartitionSpec as P

HD = 128
SEG_DEV = 8
NEG_FILL = -1e30
NT_DIMS = (((1,), (1,)), ((), ()))


def attention_kernel(base_ref, kpos_ref, q_ref, k_ref, v_ref, kept_ref, do_ref, delta_ref, attr_ref, *, tq, hp):
    r = pl.program_id(2)
    first = (pl.program_id(0) == 0) & (pl.program_id(1) == 0) & (r == 0)

    @pl.when(first)
    def _():
        attr_ref[...] = jnp.zeros_like(attr_ref)

    k = k_ref[...]
    v = v_ref[...]
    row_pos = base_ref[0] + r * tq + lax.broadcasted_iota(jnp.int32, (tq, 1), 0)
    vis = kpos_ref[...] <= row_pos
    kept = kept_ref[...] > 0.0
    total = None
    for h in range(hp):
        cols = slice(h * HD, (h + 1) * HD)
        s = lax.dot_general(q_ref[:, cols], k, NT_DIMS, preferred_element_type=jnp.float32)
        s = s * (HD ** -0.5)
        s_c = jnp.where(vis, s, NEG_FILL)
        s_m = jnp.where(kept, s_c, NEG_FILL)
        m_c = jnp.max(s_c, axis=1, keepdims=True)
        m_m = jnp.max(s_m, axis=1, keepdims=True)
        e_c = jnp.exp(s_c - m_c)
        e_m = jnp.exp(s_m - m_m)
        l_c = jnp.sum(e_c, axis=1, keepdims=True)
        l_m = jnp.sum(e_m, axis=1, keepdims=True)
        o_c = jnp.dot(e_c.astype(jnp.bfloat16), v, preferred_element_type=jnp.float32) / l_c
        o_m = jnp.dot(e_m.astype(jnp.bfloat16), v, preferred_element_type=jnp.float32) / l_m
        delta_ref[:, cols] = (o_m - o_c).astype(delta_ref.dtype)
        g_rows = do_ref[:, cols]
        row_dot = jnp.sum(g_rows.astype(jnp.float32) * o_c, axis=1, keepdims=True)
        d_p = lax.dot_general(g_rows, v, NT_DIMS, preferred_element_type=jnp.float32)
        log_total = m_c + jnp.log(l_c)
        prob = e_c * (1.0 / l_c)
        contrib = prob * (d_p + (d_p - row_dot) * (s - log_total))
        part = jnp.sum(contrib, axis=0, keepdims=True)
        total = part if total is None else total + part
    attr_ref[...] += total


def fused_attention(base, key_pos, query, key_all, value_all, kept, grad_out, group_size):
    qc, width = query.shape
    keys, kv_width = key_all.shape
    kv_local = kv_width // HD
    tq = max(8, min(qc, (128 * 2048) // keys))
    n_rows = qc // tq
    hp = 2 if group_size % 2 == 0 else 1
    steps = group_size // hp
    grid = (kv_local, steps, n_rows)

    def head_map(g, j, r, b):
        return (r, g * steps + j)

    def kv_map(g, j, r, b):
        return (0, g)

    def fixed(g, j, r, b):
        return (0, 0)

    flops = 8 * qc * keys * HD * kv_local * group_size
    cost = pl.CostEstimate(
        flops=flops,
        transcendentals=2 * qc * keys * kv_local * group_size,
        bytes_accessed=2 * (query.size + key_all.size + value_all.size + grad_out.size + query.size)
        + 4 * keys,
    )
    return pl.pallas_call(
        functools.partial(attention_kernel, tq=tq, hp=hp),
        grid_spec=pltpu.PrefetchScalarGridSpec(
            num_scalar_prefetch=1,
            grid=grid,
            in_specs=[
                pl.BlockSpec((1, keys), fixed),
                pl.BlockSpec((tq, hp * HD), head_map),
                pl.BlockSpec((keys, HD), kv_map),
                pl.BlockSpec((keys, HD), kv_map),
                pl.BlockSpec((1, keys), fixed),
                pl.BlockSpec((tq, hp * HD), head_map),
            ],
            out_specs=[
                pl.BlockSpec((tq, hp * HD), head_map),
                pl.BlockSpec((1, keys), fixed),
            ],
        ),
        out_shape=[
            jax.ShapeDtypeStruct((qc, width), jnp.bfloat16),
            jax.ShapeDtypeStruct((1, keys), jnp.float32),
        ],
        compiler_params=pltpu.CompilerParams(
            dimension_semantics=("arbitrary", "arbitrary", "arbitrary")
        ),
        cost_estimate=cost,
    )(base, key_pos, query, key_all, value_all, kept, grad_out)


def relay_gather(payload, needed, ctx_at):
    n = lax.axis_size("ctx")
    zero = jnp.zeros_like(payload)
    forward, backward = [payload], [payload]
    for k in range(1, n):
        fwd = [(i, i + k) for i in range(n - k) if needed(i + k, i)]
        relay = [(i + k - 1, i + k) for i, _ in fwd]
        if k > 2 and relay and all(needed(s, r - k) for s, r in relay):
            forward.append(lax.ppermute(forward[-1], "ctx", relay))
        else:
            forward.append(lax.ppermute(payload, "ctx", fwd) if fwd else zero)
        bwd = [(i + k, i) for i in range(n - k) if needed(i, i + k)]
        relay = [(r + 1, r) for _, r in bwd]
        if k > 2 and relay and all(needed(s, r + k) for s, r in relay):
            backward.append(lax.ppermute(backward[-1], "ctx", relay))
        else:
            backward.append(lax.ppermute(payload, "ctx", bwd) if bwd else zero)
    parts = [payload]
    for k in range(1, n):
        parts.append(jnp.where(k <= ctx_at, forward[k], backward[n - k]))
    return parts


def gather_kv(key, value, segment_ids, ctx_at, rep_at, rep_count, needed):
    n = lax.axis_size("ctx")
    key_count, width = key.shape
    seg_rows = -(-key_count // width)
    seg_pad = -(-seg_rows // 16) * 16
    seg_block = jnp.zeros((seg_pad * width,), jnp.bfloat16)
    seg_block = seg_block.at[:key_count].set(segment_ids.astype(jnp.bfloat16))
    seg_block = seg_block.reshape(seg_pad, width)
    split = rep_count == 2
    halves = [jnp.where(rep_at == 0, key, value)] if split else [key, value]
    payloads = [jnp.concatenate([h, seg_block], axis=0) for h in halves]
    gathered = [relay_gather(p, needed, ctx_at) for p in payloads]
    if split:
        mine = gathered[0]
        theirs = [lax.ppermute(p, "rep", [(0, 1), (1, 0)]) for p in mine]
        first = rep_at == 0
        key_parts = [jnp.where(first, a, b) for a, b in zip(mine, theirs)]
        value_parts = [jnp.where(first, b, a) for a, b in zip(mine, theirs)]
    else:
        key_parts, value_parts = gathered
    key_all = jnp.concatenate([p[:key_count] for p in key_parts], axis=0)
    value_all = jnp.concatenate([p[:key_count] for p in value_parts], axis=0)
    seg_all = jnp.concatenate(
        [p[key_count:].reshape(-1)[:key_count] for p in key_parts], axis=0
    ).astype(jnp.int32)
    source = (ctx_at - jnp.arange(n, dtype=jnp.int32)) % n
    key_pos = (source[:, None] * key_count + jnp.arange(key_count, dtype=jnp.int32)[None, :])
    return key_all, value_all, seg_all, key_pos.reshape(1, -1), source


def butterfly_sum(total, axes):
    for axis in axes:
        n = lax.axis_size(axis)
        if n & (n - 1):
            total = lax.psum(total, axis)
            continue
        bit = 1
        while bit < n:
            total = total + lax.ppermute(total, axis, [(i, i ^ bit) for i in range(n)])
            bit *= 2
    return total


def local(query, key, value, out_weight, cotangent, response, segment_ids, masked_segments):
    ctx_count = lax.axis_size("ctx")
    rep_count = lax.axis_size("rep")
    head_count = lax.axis_size("head")
    ctx_at = lax.axis_index("ctx")
    rep_at = lax.axis_index("rep")
    head_at = lax.axis_index("head")
    query_count = query.shape[0]
    key_count = key.shape[0]
    kv_local = key.shape[1] // HD
    heads_local = query.shape[1] // HD
    group_size = heads_local // kv_local
    context_len = key_count * ctx_count
    query_base = context_len - query_count * ctx_count * rep_count
    base = (query_base + (ctx_at * rep_count + rep_at) * query_count).astype(jnp.int32)
    base = jnp.reshape(base, (1,))

    def needed(receiver, block):
        last_query = query_base + (receiver * rep_count + rep_count) * query_count - 1
        return block * key_count <= last_query

    key_all, value_all, seg_shift, key_pos, source = gather_kv(
        key, value, segment_ids, ctx_at, rep_at, rep_count, needed
    )
    kept = jnp.where(
        jnp.any(seg_shift[:, None] == masked_segments[None, :], axis=1), 0.0, 1.0
    ).astype(jnp.float32)[None, :]
    onehot = (
        seg_shift[:, None] == jnp.arange(SEG_DEV * ctx_count, dtype=jnp.int32)[None, :]
    ).astype(jnp.float32)

    grad_masked = jnp.where(response[:, None] > 0, cotangent, jnp.zeros_like(cotangent))
    grad_out = jnp.dot(grad_masked, out_weight.T, preferred_element_type=jnp.float32).astype(
        jnp.bfloat16
    )
    delta, attr = fused_attention(
        base, key_pos, query, key_all, value_all, kept, grad_out, group_size
    )

    inverse = (ctx_at - jnp.arange(ctx_count, dtype=jnp.int32)) % ctx_count
    attr_abs = attr.reshape(ctx_count, key_count)[inverse].reshape(-1)
    seg_part = jnp.dot(attr[0], onehot, precision=lax.Precision.HIGHEST)
    summed = butterfly_sum(jnp.concatenate([attr_abs, seg_part]), ("rep", "ctx", "head"))
    attr_all = summed[:context_len]
    segment_attr = summed[context_len:]

    if head_count == 2:
        cols = out_weight.shape[1] // 2
        send_w = lax.dynamic_slice_in_dim(out_weight, (1 - head_at) * cols, cols, 1)
        send = jnp.dot(delta, send_w, preferred_element_type=jnp.float32)
        got = lax.ppermute(send.astype(jnp.bfloat16), "head", [(0, 1), (1, 0)])
        keep_w = lax.dynamic_slice_in_dim(out_weight, head_at * cols, cols, 1)
        keep = jnp.dot(delta, keep_w, preferred_element_type=jnp.float32)
        patch_effect = (keep + got.astype(jnp.float32)).astype(jnp.bfloat16)
    else:
        projected = jnp.dot(delta, out_weight, preferred_element_type=jnp.float32)
        patch_effect = lax.psum_scatter(
            projected.astype(jnp.bfloat16), "head", scatter_dimension=1, tiled=True
        )

    token_attr = lax.dynamic_slice_in_dim(attr_all, ctx_at * key_count, key_count, 0)
    return (patch_effect, token_attr, segment_attr)


def solution(mesh):
    return jax.shard_map(
        local,
        mesh=mesh,
        in_specs=(
            P(("groups", "ctx", "rep"), "head"),
            P(("groups", "ctx"), "head"),
            P(("groups", "ctx"), "head"),
            P("head", None),
            P(("groups", "ctx", "rep"), None),
            P(("groups", "ctx", "rep")),
            P(("groups", "ctx")),
            P("groups"),
        ),
        out_specs=(P(("groups", "ctx", "rep"), "head"), P(("groups", "ctx")), P("groups")),
        check_vma=False,
    )
```

```python
import functools

import jax
import jax.numpy as jnp
from jax import lax
from jax.experimental import pallas as pl
from jax.experimental.pallas import tpu as pltpu
from jax.sharding import PartitionSpec as P

HD = 128
SEG_DEV = 8
NEG_FILL = -1e30
NT_DIMS = (((1,), (1,)), ((), ()))


def attention_kernel(base_ref, kpos_ref, q_ref, k_ref, v_ref, kept_ref, do_ref, delta_ref, attr_ref, *, tq, hp):
    r = pl.program_id(2)
    first = (pl.program_id(0) == 0) & (pl.program_id(1) == 0) & (r == 0)

    @pl.when(first)
    def _():
        attr_ref[...] = jnp.zeros_like(attr_ref)

    k = k_ref[...]
    v = v_ref[...]
    row_pos = base_ref[0] + r * tq + lax.broadcasted_iota(jnp.int32, (tq, 1), 0)
    vis = kpos_ref[...] <= row_pos
    kept = kept_ref[...] > 0.0
    total = None
    for h in range(hp):
        cols = slice(h * HD, (h + 1) * HD)
        s = lax.dot_general(q_ref[:, cols], k, NT_DIMS, preferred_element_type=jnp.float32)
        s = s * (HD ** -0.5)
        s_c = jnp.where(vis, s, NEG_FILL)
        s_m = jnp.where(kept, s_c, NEG_FILL)
        m_c = jnp.max(s_c, axis=1, keepdims=True)
        m_m = jnp.max(s_m, axis=1, keepdims=True)
        e_c = jnp.exp(s_c - m_c)
        e_m = jnp.exp(s_m - m_m)
        l_c = jnp.sum(e_c, axis=1, keepdims=True)
        l_m = jnp.sum(e_m, axis=1, keepdims=True)
        o_c = jnp.dot(e_c.astype(jnp.bfloat16), v, preferred_element_type=jnp.float32) / l_c
        o_m = jnp.dot(e_m.astype(jnp.bfloat16), v, preferred_element_type=jnp.float32) / l_m
        delta_ref[:, cols] = (o_m - o_c).astype(delta_ref.dtype)
        g_rows = do_ref[:, cols]
        row_dot = jnp.sum(g_rows.astype(jnp.float32) * o_c, axis=1, keepdims=True)
        d_p = lax.dot_general(g_rows, v, NT_DIMS, preferred_element_type=jnp.float32)
        log_total = m_c + jnp.log(l_c)
        prob = e_c * (1.0 / l_c)
        contrib = prob * (d_p + (d_p - row_dot) * (s - log_total))
        part = jnp.sum(contrib, axis=0, keepdims=True)
        total = part if total is None else total + part
    attr_ref[...] += total


def fused_attention(base, key_pos, query, key_all, value_all, kept, grad_out, group_size):
    qc, width = query.shape
    keys, kv_width = key_all.shape
    kv_local = kv_width // HD
    tq = max(8, min(qc, (128 * 2048) // keys))
    n_rows = qc // tq
    hp = 2 if group_size % 2 == 0 else 1
    steps = group_size // hp
    grid = (kv_local, steps, n_rows)

    def head_map(g, j, r, b):
        return (r, g * steps + j)

    def kv_map(g, j, r, b):
        return (0, g)

    def fixed(g, j, r, b):
        return (0, 0)

    flops = 8 * qc * keys * HD * kv_local * group_size
    cost = pl.CostEstimate(
        flops=flops,
        transcendentals=2 * qc * keys * kv_local * group_size,
        bytes_accessed=2 * (query.size + key_all.size + value_all.size + grad_out.size + query.size)
        + 4 * keys,
    )
    return pl.pallas_call(
        functools.partial(attention_kernel, tq=tq, hp=hp),
        grid_spec=pltpu.PrefetchScalarGridSpec(
            num_scalar_prefetch=1,
            grid=grid,
            in_specs=[
                pl.BlockSpec((1, keys), fixed),
                pl.BlockSpec((tq, hp * HD), head_map),
                pl.BlockSpec((keys, HD), kv_map),
                pl.BlockSpec((keys, HD), kv_map),
                pl.BlockSpec((1, keys), fixed),
                pl.BlockSpec((tq, hp * HD), head_map),
            ],
            out_specs=[
                pl.BlockSpec((tq, hp * HD), head_map),
                pl.BlockSpec((1, keys), fixed),
            ],
        ),
        out_shape=[
            jax.ShapeDtypeStruct((qc, width), jnp.bfloat16),
            jax.ShapeDtypeStruct((1, keys), jnp.float32),
        ],
        compiler_params=pltpu.CompilerParams(
            dimension_semantics=("arbitrary", "arbitrary", "arbitrary")
        ),
        cost_estimate=cost,
    )(base, key_pos, query, key_all, value_all, kept, grad_out)


def relay_gather(payload, needed, ctx_at):
    n = lax.axis_size("ctx")
    zero = jnp.zeros_like(payload)
    forward, backward = [payload], [payload]
    for k in range(1, n):
        fwd = [(i, i + k) for i in range(n - k) if needed(i + k, i)]
        relay = [(i + k - 1, i + k) for i, _ in fwd]
        if k > 2 and relay and all(needed(s, r - k) for s, r in relay):
            forward.append(lax.ppermute(forward[-1], "ctx", relay))
        else:
            forward.append(lax.ppermute(payload, "ctx", fwd) if fwd else zero)
        bwd = [(i + k, i) for i in range(n - k) if needed(i, i + k)]
        relay = [(r + 1, r) for _, r in bwd]
        if k > 2 and relay and all(needed(s, r + k) for s, r in relay):
            backward.append(lax.ppermute(backward[-1], "ctx", relay))
        else:
            backward.append(lax.ppermute(payload, "ctx", bwd) if bwd else zero)
    parts = [payload]
    for k in range(1, n):
        parts.append(jnp.where(k <= ctx_at, forward[k], backward[n - k]))
    return parts


def gather_kv(key, value, segment_ids, ctx_at, rep_at, rep_count, needed):
    n = lax.axis_size("ctx")
    key_count, width = key.shape
    seg_rows = -(-key_count // width)
    seg_pad = -(-seg_rows // 16) * 16
    seg_block = jnp.zeros((seg_pad * width,), jnp.bfloat16)
    seg_block = seg_block.at[:key_count].set(segment_ids.astype(jnp.bfloat16))
    seg_block = seg_block.reshape(seg_pad, width)
    split = rep_count == 2
    halves = [jnp.where(rep_at == 0, key, value)] if split else [key, value]
    payloads = [jnp.concatenate([h, seg_block], axis=0) for h in halves]
    gathered = [relay_gather(p, needed, ctx_at) for p in payloads]
    if split:
        mine = gathered[0]
        theirs = [lax.ppermute(p, "rep", [(0, 1), (1, 0)]) for p in mine]
        first = rep_at == 0
        key_parts = [jnp.where(first, a, b) for a, b in zip(mine, theirs)]
        value_parts = [jnp.where(first, b, a) for a, b in zip(mine, theirs)]
    else:
        key_parts, value_parts = gathered
    key_all = jnp.concatenate([p[:key_count] for p in key_parts], axis=0)
    value_all = jnp.concatenate([p[:key_count] for p in value_parts], axis=0)
    seg_all = jnp.concatenate(
        [p[key_count:].reshape(-1)[:key_count] for p in key_parts], axis=0
    ).astype(jnp.int32)
    source = (ctx_at - jnp.arange(n, dtype=jnp.int32)) % n
    key_pos = (source[:, None] * key_count + jnp.arange(key_count, dtype=jnp.int32)[None, :])
    return key_all, value_all, seg_all, key_pos.reshape(1, -1), source


def butterfly_sum(total, axes):
    for axis in axes:
        n = lax.axis_size(axis)
        if n & (n - 1):
            total = lax.psum(total, axis)
            continue
        bit = 1
        while bit < n:
            total = total + lax.ppermute(total, axis, [(i, i ^ bit) for i in range(n)])
            bit *= 2
    return total


def local(query, key, value, out_weight, cotangent, response, segment_ids, masked_segments):
    ctx_count = lax.axis_size("ctx")
    rep_count = lax.axis_size("rep")
    head_count = lax.axis_size("head")
    ctx_at = lax.axis_index("ctx")
    rep_at = lax.axis_index("rep")
    head_at = lax.axis_index("head")
    query_count = query.shape[0]
    key_count = key.shape[0]
    kv_local = key.shape[1] // HD
    heads_local = query.shape[1] // HD
    group_size = heads_local // kv_local
    context_len = key_count * ctx_count
    query_base = context_len - query_count * ctx_count * rep_count
    base = (query_base + (ctx_at * rep_count + rep_at) * query_count).astype(jnp.int32)
    base = jnp.reshape(base, (1,))

    def needed(receiver, block):
        last_query = query_base + (receiver * rep_count + rep_count) * query_count - 1
        return block * key_count <= last_query

    key_all, value_all, seg_shift, key_pos, source = gather_kv(
        key, value, segment_ids, ctx_at, rep_at, rep_count, needed
    )
    kept = jnp.where(
        jnp.any(seg_shift[:, None] == masked_segments[None, :], axis=1), 0.0, 1.0
    ).astype(jnp.float32)[None, :]
    onehot = (
        seg_shift[:, None] == jnp.arange(SEG_DEV * ctx_count, dtype=jnp.int32)[None, :]
    ).astype(jnp.float32)

    grad_masked = jnp.where(response[:, None] > 0, cotangent, jnp.zeros_like(cotangent))
    grad_out = jnp.dot(grad_masked, out_weight.T, preferred_element_type=jnp.float32).astype(
        jnp.bfloat16
    )
    delta, attr = fused_attention(
        base, key_pos, query, key_all, value_all, kept, grad_out, group_size
    )

    inverse = (ctx_at - jnp.arange(ctx_count, dtype=jnp.int32)) % ctx_count
    attr_abs = attr.reshape(ctx_count, key_count)[inverse].reshape(-1)
    seg_part = jnp.dot(attr[0], onehot, precision=lax.Precision.HIGHEST)
    summed = butterfly_sum(jnp.concatenate([attr_abs, seg_part]), ("rep", "ctx", "head"))
    attr_all = summed[:context_len]
    segment_attr = summed[context_len:]

    if head_count == 2:
        cols = out_weight.shape[1] // 2
        send_w = lax.dynamic_slice_in_dim(out_weight, (1 - head_at) * cols, cols, 1)
        send = jnp.dot(delta, send_w, preferred_element_type=jnp.float32)
        got = lax.ppermute(send.astype(jnp.bfloat16), "head", [(0, 1), (1, 0)])
        keep_w = lax.dynamic_slice_in_dim(out_weight, head_at * cols, cols, 1)
        keep = lax.optimization_barrier(jnp.dot(delta, keep_w, preferred_element_type=jnp.float32))
        patch_effect = (keep + got.astype(jnp.float32)).astype(jnp.bfloat16)
    else:
        projected = jnp.dot(delta, out_weight, preferred_element_type=jnp.float32)
        patch_effect = lax.psum_scatter(
            projected.astype(jnp.bfloat16), "head", scatter_dimension=1, tiled=True
        )

    token_attr = lax.dynamic_slice_in_dim(attr_all, ctx_at * key_count, key_count, 0)
    return (patch_effect, token_attr, segment_attr)


def solution(mesh):
    return jax.shard_map(
        local,
        mesh=mesh,
        in_specs=(
            P(("groups", "ctx", "rep"), "head"),
            P(("groups", "ctx"), "head"),
            P(("groups", "ctx"), "head"),
            P("head", None),
            P(("groups", "ctx", "rep"), None),
            P(("groups", "ctx", "rep")),
            P(("groups", "ctx")),
            P("groups"),
        ),
        out_specs=(P(("groups", "ctx", "rep"), "head"), P(("groups", "ctx")), P("groups")),
        check_vma=False,
    )
```

```python
import functools

import jax
import jax.numpy as jnp
from jax import lax
from jax.experimental import pallas as pl
from jax.experimental.pallas import tpu as pltpu
from jax.sharding import PartitionSpec as P

HD = 128
SEG_DEV = 8
NEG_FILL = -1e30
NT_DIMS = (((1,), (1,)), ((), ()))


def attention_kernel(base_ref, kpos_ref, q_ref, k_ref, v_ref, kept_ref, do_ref, delta_ref, attr_ref, *, tq, hp):
    r = pl.program_id(2)
    first = (pl.program_id(0) == 0) & (pl.program_id(1) == 0) & (r == 0)

    @pl.when(first)
    def _():
        attr_ref[...] = jnp.zeros_like(attr_ref)

    k = k_ref[...]
    v = v_ref[...]
    row_pos = base_ref[0] + r * tq + lax.broadcasted_iota(jnp.int32, (tq, 1), 0)
    vis = kpos_ref[...] <= row_pos
    kept = kept_ref[...] > 0.0
    total = None
    for h in range(hp):
        cols = slice(h * HD, (h + 1) * HD)
        s = lax.dot_general(q_ref[:, cols], k, NT_DIMS, preferred_element_type=jnp.float32)
        s = s * (HD ** -0.5)
        s_c = jnp.where(vis, s, NEG_FILL)
        s_m = jnp.where(kept, s_c, NEG_FILL)
        m_c = jnp.max(s_c, axis=1, keepdims=True)
        m_m = jnp.max(s_m, axis=1, keepdims=True)
        e_c = jnp.exp(s_c - m_c)
        e_m = jnp.exp(s_m - m_m)
        l_c = jnp.sum(e_c, axis=1, keepdims=True)
        l_m = jnp.sum(e_m, axis=1, keepdims=True)
        o_c = jnp.dot(e_c.astype(jnp.bfloat16), v, preferred_element_type=jnp.float32) / l_c
        o_m = jnp.dot(e_m.astype(jnp.bfloat16), v, preferred_element_type=jnp.float32) / l_m
        delta_ref[:, cols] = (o_m - o_c).astype(delta_ref.dtype)
        g_rows = do_ref[:, cols]
        row_dot = jnp.sum(g_rows.astype(jnp.float32) * o_c, axis=1, keepdims=True)
        d_p = lax.dot_general(g_rows, v, NT_DIMS, preferred_element_type=jnp.float32)
        log_total = m_c + jnp.log(l_c)
        prob = e_c * (1.0 / l_c)
        contrib = prob * (d_p + (d_p - row_dot) * (s - log_total))
        part = jnp.sum(contrib, axis=0, keepdims=True)
        total = part if total is None else total + part
    attr_ref[...] += total


def fused_attention(base, key_pos, query, key_all, value_all, kept, grad_out, group_size, col_off=0):
    qc = query.shape[0]
    width = key_all.shape[1] * group_size
    keys, kv_width = key_all.shape
    kv_local = kv_width // HD
    tq = max(8, min(qc, (128 * 2048) // keys))
    n_rows = qc // tq
    hp = 2 if group_size % 2 == 0 else 1
    steps = group_size // hp
    grid = (kv_local, steps, n_rows)

    def head_map(g, j, r, b):
        return (r, col_off + g * steps + j)

    def out_map(g, j, r, b):
        return (r, g * steps + j)

    def kv_map(g, j, r, b):
        return (0, g)

    def fixed(g, j, r, b):
        return (0, 0)

    flops = 8 * qc * keys * HD * kv_local * group_size
    cost = pl.CostEstimate(
        flops=flops,
        transcendentals=2 * qc * keys * kv_local * group_size,
        bytes_accessed=2 * (3 * qc * width + key_all.size + value_all.size)
        + 4 * keys,
    )
    return pl.pallas_call(
        functools.partial(attention_kernel, tq=tq, hp=hp),
        grid_spec=pltpu.PrefetchScalarGridSpec(
            num_scalar_prefetch=1,
            grid=grid,
            in_specs=[
                pl.BlockSpec((1, keys), fixed),
                pl.BlockSpec((tq, hp * HD), head_map),
                pl.BlockSpec((keys, HD), kv_map),
                pl.BlockSpec((keys, HD), kv_map),
                pl.BlockSpec((1, keys), fixed),
                pl.BlockSpec((tq, hp * HD), head_map),
            ],
            out_specs=[
                pl.BlockSpec((tq, hp * HD), out_map),
                pl.BlockSpec((1, keys), fixed),
            ],
        ),
        out_shape=[
            jax.ShapeDtypeStruct((qc, width), jnp.bfloat16),
            jax.ShapeDtypeStruct((1, keys), jnp.float32),
        ],
        compiler_params=pltpu.CompilerParams(
            dimension_semantics=("arbitrary", "arbitrary", "arbitrary")
        ),
        cost_estimate=cost,
    )(base, key_pos, query, key_all, value_all, kept, grad_out)


def relay_gather(payload, needed, ctx_at):
    n = lax.axis_size("ctx")
    zero = jnp.zeros_like(payload)
    forward, backward = [payload], [payload]
    for k in range(1, n):
        fwd = [(i, i + k) for i in range(n - k) if needed(i + k, i)]
        relay = [(i + k - 1, i + k) for i, _ in fwd]
        if k > 2 and relay and all(needed(s, r - k) for s, r in relay):
            forward.append(lax.ppermute(forward[-1], "ctx", relay))
        else:
            forward.append(lax.ppermute(payload, "ctx", fwd) if fwd else zero)
        bwd = [(i + k, i) for i in range(n - k) if needed(i, i + k)]
        relay = [(r + 1, r) for _, r in bwd]
        if k > 2 and relay and all(needed(s, r + k) for s, r in relay):
            backward.append(lax.ppermute(backward[-1], "ctx", relay))
        else:
            backward.append(lax.ppermute(payload, "ctx", bwd) if bwd else zero)
    parts = [payload]
    for k in range(1, n):
        parts.append(jnp.where(k <= ctx_at, forward[k], backward[n - k]))
    return parts


def gather_kv(key, value, segment_ids, ctx_at, rep_at, rep_count, needed):
    n = lax.axis_size("ctx")
    key_count, width = key.shape
    seg_rows = -(-key_count // width)
    seg_pad = -(-seg_rows // 16) * 16
    seg_block = jnp.zeros((seg_pad * width,), jnp.bfloat16)
    seg_block = seg_block.at[:key_count].set(segment_ids.astype(jnp.bfloat16))
    seg_block = seg_block.reshape(seg_pad, width)
    split = rep_count == 2
    halves = [jnp.where(rep_at == 0, key, value)] if split else [key, value]
    payloads = [jnp.concatenate([h, seg_block], axis=0) for h in halves]
    gathered = [relay_gather(p, needed, ctx_at) for p in payloads]
    if split:
        mine = gathered[0]
        theirs = [lax.ppermute(p, "rep", [(0, 1), (1, 0)]) for p in mine]
        first = rep_at == 0
        key_parts = [jnp.where(first, a, b) for a, b in zip(mine, theirs)]
        value_parts = [jnp.where(first, b, a) for a, b in zip(mine, theirs)]
    else:
        key_parts, value_parts = gathered
    key_all = jnp.concatenate([p[:key_count] for p in key_parts], axis=0)
    value_all = jnp.concatenate([p[:key_count] for p in value_parts], axis=0)
    seg_all = jnp.concatenate(
        [p[key_count:].reshape(-1)[:key_count] for p in key_parts], axis=0
    ).astype(jnp.int32)
    source = (ctx_at - jnp.arange(n, dtype=jnp.int32)) % n
    key_pos = (source[:, None] * key_count + jnp.arange(key_count, dtype=jnp.int32)[None, :])
    return key_all, value_all, seg_all, key_pos.reshape(1, -1), source


def butterfly_sum(total, axes):
    for axis in axes:
        n = lax.axis_size(axis)
        if n & (n - 1):
            total = lax.psum(total, axis)
            continue
        bit = 1
        while bit < n:
            total = total + lax.ppermute(total, axis, [(i, i ^ bit) for i in range(n)])
            bit *= 2
    return total


def local(query, key, value, out_weight, cotangent, response, segment_ids, masked_segments):
    ctx_count = lax.axis_size("ctx")
    rep_count = lax.axis_size("rep")
    head_count = lax.axis_size("head")
    ctx_at = lax.axis_index("ctx")
    rep_at = lax.axis_index("rep")
    head_at = lax.axis_index("head")
    query_count = query.shape[0]
    key_count = key.shape[0]
    kv_local = key.shape[1] // HD
    heads_local = query.shape[1] // HD
    group_size = heads_local // kv_local
    context_len = key_count * ctx_count
    query_base = context_len - query_count * ctx_count * rep_count
    base = (query_base + (ctx_at * rep_count + rep_at) * query_count).astype(jnp.int32)
    base = jnp.reshape(base, (1,))

    def needed(receiver, block):
        last_query = query_base + (receiver * rep_count + rep_count) * query_count - 1
        return block * key_count <= last_query

    parts = 2 if kv_local % 2 == 0 else 1
    kv_cols = key.shape[1] // parts
    gathered = [
        gather_kv(
            key[:, p * kv_cols:(p + 1) * kv_cols],
            value[:, p * kv_cols:(p + 1) * kv_cols],
            segment_ids, ctx_at, rep_at, rep_count, needed,
        )
        for p in range(parts)
    ]
    seg_shift, key_pos = gathered[0][2], gathered[0][3]
    kept = jnp.where(
        jnp.any(seg_shift[:, None] == masked_segments[None, :], axis=1), 0.0, 1.0
    ).astype(jnp.float32)[None, :]
    onehot = (
        seg_shift[:, None] == jnp.arange(SEG_DEV * ctx_count, dtype=jnp.int32)[None, :]
    ).astype(jnp.float32)

    grad_masked = jnp.where(response[:, None] > 0, cotangent, jnp.zeros_like(cotangent))
    grad_out = jnp.dot(grad_masked, out_weight.T, preferred_element_type=jnp.float32).astype(
        jnp.bfloat16
    )
    steps_per_part = (kv_local // parts) * (group_size // (2 if group_size % 2 == 0 else 1))
    deltas, attr = [], None
    for p in range(parts):
        d_p, a_p = fused_attention(
            base, key_pos, query, gathered[p][0], gathered[p][1], kept, grad_out, group_size,
            col_off=p * steps_per_part,
        )
        deltas.append(d_p)
        attr = a_p if attr is None else attr + a_p
    delta = jnp.concatenate(deltas, axis=1) if parts > 1 else deltas[0]

    inverse = (ctx_at - jnp.arange(ctx_count, dtype=jnp.int32)) % ctx_count
    attr_abs = attr.reshape(ctx_count, key_count)[inverse].reshape(-1)
    seg_part = jnp.dot(attr[0], onehot, precision=lax.Precision.HIGHEST)
    summed = butterfly_sum(jnp.concatenate([attr_abs, seg_part]), ("rep", "ctx", "head"))
    attr_all = summed[:context_len]
    segment_attr = summed[context_len:]

    if head_count == 2:
        cols = out_weight.shape[1] // 2
        send_w = lax.dynamic_slice_in_dim(out_weight, (1 - head_at) * cols, cols, 1)
        send = jnp.dot(delta, send_w, preferred_element_type=jnp.float32)
        got = lax.ppermute(send.astype(jnp.bfloat16), "head", [(0, 1), (1, 0)])
        keep_w = lax.dynamic_slice_in_dim(out_weight, head_at * cols, cols, 1)
        keep = lax.optimization_barrier(jnp.dot(delta, keep_w, preferred_element_type=jnp.float32))
        patch_effect = (keep + got.astype(jnp.float32)).astype(jnp.bfloat16)
    else:
        projected = jnp.dot(delta, out_weight, preferred_element_type=jnp.float32)
        patch_effect = lax.psum_scatter(
            projected.astype(jnp.bfloat16), "head", scatter_dimension=1, tiled=True
        )

    token_attr = lax.dynamic_slice_in_dim(attr_all, ctx_at * key_count, key_count, 0)
    return (patch_effect, token_attr, segment_attr)


def solution(mesh):
    return jax.shard_map(
        local,
        mesh=mesh,
        in_specs=(
            P(("groups", "ctx", "rep"), "head"),
            P(("groups", "ctx"), "head"),
            P(("groups", "ctx"), "head"),
            P("head", None),
            P(("groups", "ctx", "rep"), None),
            P(("groups", "ctx", "rep")),
            P(("groups", "ctx")),
            P("groups"),
        ),
        out_specs=(P(("groups", "ctx", "rep"), "head"), P(("groups", "ctx")), P("groups")),
        check_vma=False,
    )
```

```python
import functools

import jax
import jax.numpy as jnp
from jax import lax
from jax.experimental import pallas as pl
from jax.experimental.pallas import tpu as pltpu
from jax.sharding import PartitionSpec as P

HD = 128
SEG_DEV = 8
NEG_FILL = -1e30
NT_DIMS = (((1,), (1,)), ((), ()))


def attention_kernel(base_ref, kpos_ref, q_ref, k_ref, v_ref, kept_ref, do_ref, delta_ref, attr_ref, *, tq, hp):
    r = pl.program_id(2)
    first = (pl.program_id(0) == 0) & (pl.program_id(1) == 0) & (r == 0)

    @pl.when(first)
    def _():
        attr_ref[...] = jnp.zeros_like(attr_ref)

    k = k_ref[...]
    v = v_ref[...]
    kept = kept_ref[...] > 0.0
    sub = 32 if tq % 32 == 0 else tq
    total = None
    for h in range(hp):
        cols = slice(h * HD, (h + 1) * HD)
        for rb in range(tq // sub):
            rows = slice(rb * sub, (rb + 1) * sub)
            row_pos = base_ref[0] + r * tq + rb * sub + lax.broadcasted_iota(jnp.int32, (sub, 1), 0)
            vis = kpos_ref[...] <= row_pos
            s = lax.dot_general(q_ref[rows, cols], k, NT_DIMS, preferred_element_type=jnp.float32)
            s = s * (HD ** -0.5)
            s_c = jnp.where(vis, s, NEG_FILL)
            s_m = jnp.where(kept, s_c, NEG_FILL)
            m_c = jnp.max(s_c, axis=1, keepdims=True)
            m_m = jnp.max(s_m, axis=1, keepdims=True)
            e_c = jnp.exp(s_c - m_c)
            e_m = jnp.exp(s_m - m_m)
            l_c = jnp.sum(e_c, axis=1, keepdims=True)
            l_m = jnp.sum(e_m, axis=1, keepdims=True)
            o_c = jnp.dot(e_c.astype(jnp.bfloat16), v, preferred_element_type=jnp.float32) / l_c
            o_m = jnp.dot(e_m.astype(jnp.bfloat16), v, preferred_element_type=jnp.float32) / l_m
            delta_ref[rows, cols] = (o_m - o_c).astype(delta_ref.dtype)
            g_rows = do_ref[rows, cols]
            row_dot = jnp.sum(g_rows.astype(jnp.float32) * o_c, axis=1, keepdims=True)
            d_p = lax.dot_general(g_rows, v, NT_DIMS, preferred_element_type=jnp.float32)
            log_total = m_c + jnp.log(l_c)
            prob = e_c * (1.0 / l_c)
            contrib = prob * (d_p + (d_p - row_dot) * (s - log_total))
            part = jnp.sum(contrib, axis=0, keepdims=True)
            total = part if total is None else total + part
    attr_ref[...] += total


def fused_attention(base, key_pos, query, key_all, value_all, kept, grad_out, group_size):
    qc, width = query.shape
    keys, kv_width = key_all.shape
    kv_local = kv_width // HD
    tq = max(8, min(qc, (128 * 2048) // keys))
    n_rows = qc // tq
    hp = 2 if group_size % 2 == 0 else 1
    steps = group_size // hp
    grid = (kv_local, steps, n_rows)

    def head_map(g, j, r, b):
        return (r, g * steps + j)

    def kv_map(g, j, r, b):
        return (0, g)

    def fixed(g, j, r, b):
        return (0, 0)

    flops = 8 * qc * keys * HD * kv_local * group_size
    cost = pl.CostEstimate(
        flops=flops,
        transcendentals=2 * qc * keys * kv_local * group_size,
        bytes_accessed=2 * (query.size + key_all.size + value_all.size + grad_out.size + query.size)
        + 4 * keys,
    )
    return pl.pallas_call(
        functools.partial(attention_kernel, tq=tq, hp=hp),
        grid_spec=pltpu.PrefetchScalarGridSpec(
            num_scalar_prefetch=1,
            grid=grid,
            in_specs=[
                pl.BlockSpec((1, keys), fixed),
                pl.BlockSpec((tq, hp * HD), head_map),
                pl.BlockSpec((keys, HD), kv_map),
                pl.BlockSpec((keys, HD), kv_map),
                pl.BlockSpec((1, keys), fixed),
                pl.BlockSpec((tq, hp * HD), head_map),
            ],
            out_specs=[
                pl.BlockSpec((tq, hp * HD), head_map),
                pl.BlockSpec((1, keys), fixed),
            ],
        ),
        out_shape=[
            jax.ShapeDtypeStruct((qc, width), jnp.bfloat16),
            jax.ShapeDtypeStruct((1, keys), jnp.float32),
        ],
        compiler_params=pltpu.CompilerParams(
            dimension_semantics=("arbitrary", "arbitrary", "arbitrary")
        ),
        cost_estimate=cost,
    )(base, key_pos, query, key_all, value_all, kept, grad_out)


def relay_gather(payload, needed, ctx_at):
    n = lax.axis_size("ctx")
    zero = jnp.zeros_like(payload)
    forward, backward = [payload], [payload]
    for k in range(1, n):
        fwd = [(i, i + k) for i in range(n - k) if needed(i + k, i)]
        relay = [(i + k - 1, i + k) for i, _ in fwd]
        if k > 2 and relay and all(needed(s, r - k) for s, r in relay):
            forward.append(lax.ppermute(forward[-1], "ctx", relay))
        else:
            forward.append(lax.ppermute(payload, "ctx", fwd) if fwd else zero)
        bwd = [(i + k, i) for i in range(n - k) if needed(i, i + k)]
        relay = [(r + 1, r) for _, r in bwd]
        if k > 2 and relay and all(needed(s, r + k) for s, r in relay):
            backward.append(lax.ppermute(backward[-1], "ctx", relay))
        else:
            backward.append(lax.ppermute(payload, "ctx", bwd) if bwd else zero)
    parts = [payload]
    for k in range(1, n):
        parts.append(jnp.where(k <= ctx_at, forward[k], backward[n - k]))
    return parts


def gather_kv(key, value, segment_ids, ctx_at, rep_at, rep_count, needed):
    n = lax.axis_size("ctx")
    key_count, width = key.shape
    seg_rows = -(-key_count // width)
    seg_pad = -(-seg_rows // 16) * 16
    seg_block = jnp.zeros((seg_pad * width,), jnp.bfloat16)
    seg_block = seg_block.at[:key_count].set(segment_ids.astype(jnp.bfloat16))
    seg_block = seg_block.reshape(seg_pad, width)
    split = rep_count == 2
    halves = [jnp.where(rep_at == 0, key, value)] if split else [key, value]
    payloads = [jnp.concatenate([h, seg_block], axis=0) for h in halves]
    gathered = [relay_gather(p, needed, ctx_at) for p in payloads]
    if split:
        mine = gathered[0]
        theirs = [lax.ppermute(p, "rep", [(0, 1), (1, 0)]) for p in mine]
        first = rep_at == 0
        key_parts = [jnp.where(first, a, b) for a, b in zip(mine, theirs)]
        value_parts = [jnp.where(first, b, a) for a, b in zip(mine, theirs)]
    else:
        key_parts, value_parts = gathered
    key_all = jnp.concatenate([p[:key_count] for p in key_parts], axis=0)
    value_all = jnp.concatenate([p[:key_count] for p in value_parts], axis=0)
    seg_all = jnp.concatenate(
        [p[key_count:].reshape(-1)[:key_count] for p in key_parts], axis=0
    ).astype(jnp.int32)
    source = (ctx_at - jnp.arange(n, dtype=jnp.int32)) % n
    key_pos = (source[:, None] * key_count + jnp.arange(key_count, dtype=jnp.int32)[None, :])
    return key_all, value_all, seg_all, key_pos.reshape(1, -1), source


def butterfly_sum(total, axes):
    for axis in axes:
        n = lax.axis_size(axis)
        if n & (n - 1):
            total = lax.psum(total, axis)
            continue
        bit = 1
        while bit < n:
            total = total + lax.ppermute(total, axis, [(i, i ^ bit) for i in range(n)])
            bit *= 2
    return total


def local(query, key, value, out_weight, cotangent, response, segment_ids, masked_segments):
    ctx_count = lax.axis_size("ctx")
    rep_count = lax.axis_size("rep")
    head_count = lax.axis_size("head")
    ctx_at = lax.axis_index("ctx")
    rep_at = lax.axis_index("rep")
    head_at = lax.axis_index("head")
    query_count = query.shape[0]
    key_count = key.shape[0]
    kv_local = key.shape[1] // HD
    heads_local = query.shape[1] // HD
    group_size = heads_local // kv_local
    context_len = key_count * ctx_count
    query_base = context_len - query_count * ctx_count * rep_count
    base = (query_base + (ctx_at * rep_count + rep_at) * query_count).astype(jnp.int32)
    base = jnp.reshape(base, (1,))

    def needed(receiver, block):
        last_query = query_base + (receiver * rep_count + rep_count) * query_count - 1
        return block * key_count <= last_query

    key_all, value_all, seg_shift, key_pos, source = gather_kv(
        key, value, segment_ids, ctx_at, rep_at, rep_count, needed
    )
    kept = jnp.where(
        jnp.any(seg_shift[:, None] == masked_segments[None, :], axis=1), 0.0, 1.0
    ).astype(jnp.float32)[None, :]
    onehot = (
        seg_shift[:, None] == jnp.arange(SEG_DEV * ctx_count, dtype=jnp.int32)[None, :]
    ).astype(jnp.float32)

    grad_masked = jnp.where(response[:, None] > 0, cotangent, jnp.zeros_like(cotangent))
    grad_out = jnp.dot(grad_masked, out_weight.T, preferred_element_type=jnp.float32).astype(
        jnp.bfloat16
    )
    delta, attr = fused_attention(
        base, key_pos, query, key_all, value_all, kept, grad_out, group_size
    )

    inverse = (ctx_at - jnp.arange(ctx_count, dtype=jnp.int32)) % ctx_count
    attr_abs = attr.reshape(ctx_count, key_count)[inverse].reshape(-1)
    seg_part = jnp.dot(attr[0], onehot, precision=lax.Precision.HIGHEST)
    summed = butterfly_sum(jnp.concatenate([attr_abs, seg_part]), ("rep", "ctx", "head"))
    attr_all = summed[:context_len]
    segment_attr = summed[context_len:]

    if head_count == 2:
        cols = out_weight.shape[1] // 2
        send_w = lax.dynamic_slice_in_dim(out_weight, (1 - head_at) * cols, cols, 1)
        send = jnp.dot(delta, send_w, preferred_element_type=jnp.float32)
        got = lax.ppermute(send.astype(jnp.bfloat16), "head", [(0, 1), (1, 0)])
        keep_w = lax.dynamic_slice_in_dim(out_weight, head_at * cols, cols, 1)
        keep = lax.optimization_barrier(jnp.dot(delta, keep_w, preferred_element_type=jnp.float32))
        patch_effect = (keep + got.astype(jnp.float32)).astype(jnp.bfloat16)
    else:
        projected = jnp.dot(delta, out_weight, preferred_element_type=jnp.float32)
        patch_effect = lax.psum_scatter(
            projected.astype(jnp.bfloat16), "head", scatter_dimension=1, tiled=True
        )

    token_attr = lax.dynamic_slice_in_dim(attr_all, ctx_at * key_count, key_count, 0)
    return (patch_effect, token_attr, segment_attr)


def solution(mesh):
    return jax.shard_map(
        local,
        mesh=mesh,
        in_specs=(
            P(("groups", "ctx", "rep"), "head"),
            P(("groups", "ctx"), "head"),
            P(("groups", "ctx"), "head"),
            P("head", None),
            P(("groups", "ctx", "rep"), None),
            P(("groups", "ctx", "rep")),
            P(("groups", "ctx")),
            P("groups"),
        ),
        out_specs=(P(("groups", "ctx", "rep"), "head"), P(("groups", "ctx")), P("groups")),
        check_vma=False,
    )
```

```python
import functools

import jax
import jax.numpy as jnp
from jax import lax
from jax.experimental import pallas as pl
from jax.experimental.pallas import tpu as pltpu
from jax.sharding import PartitionSpec as P

HD = 128
SEG_DEV = 8
NEG_FILL = -1e30
NT_DIMS = (((1,), (1,)), ((), ()))


def attention_kernel(base_ref, kpos_ref, q_ref, k_ref, v_ref, kept_ref, do_ref, delta_ref, attr_ref, *, tq, hp):
    r = pl.program_id(2)
    first = (pl.program_id(0) == 0) & (pl.program_id(1) == 0) & (r == 0)

    @pl.when(first)
    def _():
        attr_ref[...] = jnp.zeros_like(attr_ref)

    k = k_ref[...]
    v = v_ref[...]
    rows = hp * tq
    row_pos = base_ref[0] + r * tq + lax.broadcasted_iota(jnp.int32, (rows, 1), 0) % tq
    vis = kpos_ref[...] <= row_pos
    kept = kept_ref[...] > 0.0
    if hp > 1:
        q = jnp.concatenate([q_ref[:, h * HD:(h + 1) * HD] for h in range(hp)], axis=0)
        g_rows = jnp.concatenate([do_ref[:, h * HD:(h + 1) * HD] for h in range(hp)], axis=0)
    else:
        q = q_ref[...]
        g_rows = do_ref[...]
    s = lax.dot_general(q, k, NT_DIMS, preferred_element_type=jnp.float32) * (HD ** -0.5)
    s_c = jnp.where(vis, s, NEG_FILL)
    s_m = jnp.where(kept, s_c, NEG_FILL)
    m_c = jnp.max(s_c, axis=1, keepdims=True)
    m_m = jnp.max(s_m, axis=1, keepdims=True)
    e_c = jnp.exp(s_c - m_c)
    e_m = jnp.exp(s_m - m_m)
    l_c = jnp.sum(e_c, axis=1, keepdims=True)
    l_m = jnp.sum(e_m, axis=1, keepdims=True)
    o_c = jnp.dot(e_c.astype(jnp.bfloat16), v, preferred_element_type=jnp.float32) / l_c
    o_m = jnp.dot(e_m.astype(jnp.bfloat16), v, preferred_element_type=jnp.float32) / l_m
    delta = (o_m - o_c).astype(delta_ref.dtype)
    for h in range(hp):
        delta_ref[:, h * HD:(h + 1) * HD] = delta[h * tq:(h + 1) * tq]
    row_dot = jnp.sum(g_rows.astype(jnp.float32) * o_c, axis=1, keepdims=True)
    d_p = lax.dot_general(g_rows, v, NT_DIMS, preferred_element_type=jnp.float32)
    log_total = m_c + jnp.log(l_c)
    prob = e_c * (1.0 / l_c)
    contrib = prob * (d_p + (d_p - row_dot) * (s - log_total))
    total = jnp.sum(contrib, axis=0, keepdims=True)
    attr_ref[...] += total


def fused_attention(base, key_pos, query, key_all, value_all, kept, grad_out, group_size):
    qc, width = query.shape
    keys, kv_width = key_all.shape
    kv_local = kv_width // HD
    tq = max(8, min(qc, (128 * 2048) // keys))
    n_rows = qc // tq
    hp = 2 if group_size % 2 == 0 else 1
    steps = group_size // hp
    grid = (kv_local, steps, n_rows)

    def head_map(g, j, r, b):
        return (r, g * steps + j)

    def kv_map(g, j, r, b):
        return (0, g)

    def fixed(g, j, r, b):
        return (0, 0)

    flops = 8 * qc * keys * HD * kv_local * group_size
    cost = pl.CostEstimate(
        flops=flops,
        transcendentals=2 * qc * keys * kv_local * group_size,
        bytes_accessed=2 * (query.size + key_all.size + value_all.size + grad_out.size + query.size)
        + 4 * keys,
    )
    return pl.pallas_call(
        functools.partial(attention_kernel, tq=tq, hp=hp),
        grid_spec=pltpu.PrefetchScalarGridSpec(
            num_scalar_prefetch=1,
            grid=grid,
            in_specs=[
                pl.BlockSpec((1, keys), fixed),
                pl.BlockSpec((tq, hp * HD), head_map),
                pl.BlockSpec((keys, HD), kv_map),
                pl.BlockSpec((keys, HD), kv_map),
                pl.BlockSpec((1, keys), fixed),
                pl.BlockSpec((tq, hp * HD), head_map),
            ],
            out_specs=[
                pl.BlockSpec((tq, hp * HD), head_map),
                pl.BlockSpec((1, keys), fixed),
            ],
        ),
        out_shape=[
            jax.ShapeDtypeStruct((qc, width), jnp.bfloat16),
            jax.ShapeDtypeStruct((1, keys), jnp.float32),
        ],
        compiler_params=pltpu.CompilerParams(
            dimension_semantics=("arbitrary", "arbitrary", "arbitrary")
        ),
        cost_estimate=cost,
    )(base, key_pos, query, key_all, value_all, kept, grad_out)


def relay_gather(payload, needed, ctx_at):
    n = lax.axis_size("ctx")
    zero = jnp.zeros_like(payload)
    forward, backward = [payload], [payload]
    for k in range(1, n):
        fwd = [(i, i + k) for i in range(n - k) if needed(i + k, i)]
        relay = [(i + k - 1, i + k) for i, _ in fwd]
        if k > 2 and relay and all(needed(s, r - k) for s, r in relay):
            forward.append(lax.ppermute(forward[-1], "ctx", relay))
        else:
            forward.append(lax.ppermute(payload, "ctx", fwd) if fwd else zero)
        bwd = [(i + k, i) for i in range(n - k) if needed(i, i + k)]
        relay = [(r + 1, r) for _, r in bwd]
        if k > 2 and relay and all(needed(s, r + k) for s, r in relay):
            backward.append(lax.ppermute(backward[-1], "ctx", relay))
        else:
            backward.append(lax.ppermute(payload, "ctx", bwd) if bwd else zero)
    parts = [payload]
    for k in range(1, n):
        parts.append(jnp.where(k <= ctx_at, forward[k], backward[n - k]))
    return parts


def gather_kv(key, value, segment_ids, ctx_at, rep_at, rep_count, needed):
    n = lax.axis_size("ctx")
    key_count, width = key.shape
    seg_rows = -(-key_count // width)
    seg_pad = -(-seg_rows // 16) * 16
    seg_block = jnp.zeros((seg_pad * width,), jnp.bfloat16)
    seg_block = seg_block.at[:key_count].set(segment_ids.astype(jnp.bfloat16))
    seg_block = seg_block.reshape(seg_pad, width)
    split = rep_count == 2
    halves = [jnp.where(rep_at == 0, key, value)] if split else [key, value]
    payloads = [jnp.concatenate([h, seg_block], axis=0) for h in halves]
    gathered = [relay_gather(p, needed, ctx_at) for p in payloads]
    if split:
        mine = gathered[0]
        theirs = [lax.ppermute(p, "rep", [(0, 1), (1, 0)]) for p in mine]
        first = rep_at == 0
        key_parts = [jnp.where(first, a, b) for a, b in zip(mine, theirs)]
        value_parts = [jnp.where(first, b, a) for a, b in zip(mine, theirs)]
    else:
        key_parts, value_parts = gathered
    key_all = jnp.concatenate([p[:key_count] for p in key_parts], axis=0)
    value_all = jnp.concatenate([p[:key_count] for p in value_parts], axis=0)
    seg_all = jnp.concatenate(
        [p[key_count:].reshape(-1)[:key_count] for p in key_parts], axis=0
    ).astype(jnp.int32)
    source = (ctx_at - jnp.arange(n, dtype=jnp.int32)) % n
    key_pos = (source[:, None] * key_count + jnp.arange(key_count, dtype=jnp.int32)[None, :])
    return key_all, value_all, seg_all, key_pos.reshape(1, -1), source


def butterfly_sum(total, axes):
    for axis in axes:
        n = lax.axis_size(axis)
        if n & (n - 1):
            total = lax.psum(total, axis)
            continue
        bit = 1
        while bit < n:
            total = total + lax.ppermute(total, axis, [(i, i ^ bit) for i in range(n)])
            bit *= 2
    return total


def local(query, key, value, out_weight, cotangent, response, segment_ids, masked_segments):
    ctx_count = lax.axis_size("ctx")
    rep_count = lax.axis_size("rep")
    head_count = lax.axis_size("head")
    ctx_at = lax.axis_index("ctx")
    rep_at = lax.axis_index("rep")
    head_at = lax.axis_index("head")
    query_count = query.shape[0]
    key_count = key.shape[0]
    kv_local = key.shape[1] // HD
    heads_local = query.shape[1] // HD
    group_size = heads_local // kv_local
    context_len = key_count * ctx_count
    query_base = context_len - query_count * ctx_count * rep_count
    base = (query_base + (ctx_at * rep_count + rep_at) * query_count).astype(jnp.int32)
    base = jnp.reshape(base, (1,))

    def needed(receiver, block):
        last_query = query_base + (receiver * rep_count + rep_count) * query_count - 1
        return block * key_count <= last_query

    key_all, value_all, seg_shift, key_pos, source = gather_kv(
        key, value, segment_ids, ctx_at, rep_at, rep_count, needed
    )
    kept = jnp.where(
        jnp.any(seg_shift[:, None] == masked_segments[None, :], axis=1), 0.0, 1.0
    ).astype(jnp.float32)[None, :]
    onehot = (
        seg_shift[:, None] == jnp.arange(SEG_DEV * ctx_count, dtype=jnp.int32)[None, :]
    ).astype(jnp.float32)

    grad_masked = jnp.where(response[:, None] > 0, cotangent, jnp.zeros_like(cotangent))
    grad_out = jnp.dot(grad_masked, out_weight.T, preferred_element_type=jnp.float32).astype(
        jnp.bfloat16
    )
    delta, attr = fused_attention(
        base, key_pos, query, key_all, value_all, kept, grad_out, group_size
    )

    inverse = (ctx_at - jnp.arange(ctx_count, dtype=jnp.int32)) % ctx_count
    attr_abs = attr.reshape(ctx_count, key_count)[inverse].reshape(-1)
    seg_part = jnp.dot(attr[0], onehot, precision=lax.Precision.HIGHEST)
    summed = butterfly_sum(jnp.concatenate([attr_abs, seg_part]), ("rep", "ctx", "head"))
    attr_all = summed[:context_len]
    segment_attr = summed[context_len:]

    if head_count == 2:
        cols = out_weight.shape[1] // 2
        send_w = lax.dynamic_slice_in_dim(out_weight, (1 - head_at) * cols, cols, 1)
        send = jnp.dot(delta, send_w, preferred_element_type=jnp.float32)
        got = lax.ppermute(send.astype(jnp.bfloat16), "head", [(0, 1), (1, 0)])
        keep_w = lax.dynamic_slice_in_dim(out_weight, head_at * cols, cols, 1)
        keep = lax.optimization_barrier(jnp.dot(delta, keep_w, preferred_element_type=jnp.float32))
        patch_effect = (keep + got.astype(jnp.float32)).astype(jnp.bfloat16)
    else:
        projected = jnp.dot(delta, out_weight, preferred_element_type=jnp.float32)
        patch_effect = lax.psum_scatter(
            projected.astype(jnp.bfloat16), "head", scatter_dimension=1, tiled=True
        )

    token_attr = lax.dynamic_slice_in_dim(attr_all, ctx_at * key_count, key_count, 0)
    return (patch_effect, token_attr, segment_attr)


def solution(mesh):
    return jax.shard_map(
        local,
        mesh=mesh,
        in_specs=(
            P(("groups", "ctx", "rep"), "head"),
            P(("groups", "ctx"), "head"),
            P(("groups", "ctx"), "head"),
            P("head", None),
            P(("groups", "ctx", "rep"), None),
            P(("groups", "ctx", "rep")),
            P(("groups", "ctx")),
            P("groups"),
        ),
        out_specs=(P(("groups", "ctx", "rep"), "head"), P(("groups", "ctx")), P("groups")),
        check_vma=False,
    )
```

```python
import functools

import jax
import jax.numpy as jnp
from jax import lax
from jax.experimental import pallas as pl
from jax.experimental.pallas import tpu as pltpu
from jax.sharding import PartitionSpec as P

HD = 128
SEG_DEV = 8
NEG_FILL = -1e30
NT_DIMS = (((1,), (1,)), ((), ()))


def attention_kernel(base_ref, kpos_ref, q_ref, k_ref, v_ref, kept_ref, do_ref, delta_ref, attr_ref, *, tq, hp):
    r = pl.program_id(2)
    first = (pl.program_id(0) == 0) & (pl.program_id(1) == 0) & (r == 0)

    @pl.when(first)
    def _():
        attr_ref[...] = jnp.zeros_like(attr_ref)

    k = k_ref[...]
    v = v_ref[...]
    rows = hp * tq
    row_pos = base_ref[0] + r * tq + lax.broadcasted_iota(jnp.int32, (rows, 1), 0) % tq
    vis = kpos_ref[...] <= row_pos
    kept = kept_ref[...] > 0.0
    if hp > 1:
        q = jnp.concatenate([q_ref[:, h * HD:(h + 1) * HD] for h in range(hp)], axis=0)
        g_rows = jnp.concatenate([do_ref[:, h * HD:(h + 1) * HD] for h in range(hp)], axis=0)
    else:
        q = q_ref[...]
        g_rows = do_ref[...]
    s = lax.dot_general(q, k, NT_DIMS, preferred_element_type=jnp.float32) * (HD ** -0.5)
    s_c = jnp.where(vis, s, NEG_FILL)
    s_m = jnp.where(kept, s_c, NEG_FILL)
    m_c = jnp.max(s_c, axis=1, keepdims=True)
    m_m = jnp.max(s_m, axis=1, keepdims=True)
    e_c = jnp.exp(s_c - m_c)
    e_m = jnp.exp(s_m - m_m)
    l_c = jnp.sum(e_c, axis=1, keepdims=True)
    l_m = jnp.sum(e_m, axis=1, keepdims=True)
    o_c = jnp.dot(e_c.astype(jnp.bfloat16), v, preferred_element_type=jnp.float32) / l_c
    o_m = jnp.dot(e_m.astype(jnp.bfloat16), v, preferred_element_type=jnp.float32) / l_m
    delta = (o_m - o_c).astype(delta_ref.dtype)
    for h in range(hp):
        delta_ref[:, h * HD:(h + 1) * HD] = delta[h * tq:(h + 1) * tq]
    row_dot = jnp.sum(g_rows.astype(jnp.float32) * o_c, axis=1, keepdims=True)
    d_p = lax.dot_general(g_rows, v, NT_DIMS, preferred_element_type=jnp.float32)
    log_total = m_c + jnp.log(l_c)
    prob = e_c * (1.0 / l_c)
    contrib = prob * (d_p + (d_p - row_dot) * (s - log_total))
    total = jnp.sum(contrib, axis=0, keepdims=True)
    attr_ref[...] += total


def fused_attention(base, key_pos, query, key_all, value_all, kept, grad_out, group_size):
    qc, width = query.shape
    keys, kv_width = key_all.shape
    kv_local = kv_width // HD
    tq = max(8, min(qc, (128 * 2048) // keys))
    n_rows = qc // tq
    hp = group_size
    steps = group_size // hp
    grid = (kv_local, steps, n_rows)

    def head_map(g, j, r, b):
        return (r, g * steps + j)

    def kv_map(g, j, r, b):
        return (0, g)

    def fixed(g, j, r, b):
        return (0, 0)

    flops = 8 * qc * keys * HD * kv_local * group_size
    cost = pl.CostEstimate(
        flops=flops,
        transcendentals=2 * qc * keys * kv_local * group_size,
        bytes_accessed=2 * (query.size + key_all.size + value_all.size + grad_out.size + query.size)
        + 4 * keys,
    )
    return pl.pallas_call(
        functools.partial(attention_kernel, tq=tq, hp=hp),
        grid_spec=pltpu.PrefetchScalarGridSpec(
            num_scalar_prefetch=1,
            grid=grid,
            in_specs=[
                pl.BlockSpec((1, keys), fixed),
                pl.BlockSpec((tq, hp * HD), head_map),
                pl.BlockSpec((keys, HD), kv_map),
                pl.BlockSpec((keys, HD), kv_map),
                pl.BlockSpec((1, keys), fixed),
                pl.BlockSpec((tq, hp * HD), head_map),
            ],
            out_specs=[
                pl.BlockSpec((tq, hp * HD), head_map),
                pl.BlockSpec((1, keys), fixed),
            ],
        ),
        out_shape=[
            jax.ShapeDtypeStruct((qc, width), jnp.bfloat16),
            jax.ShapeDtypeStruct((1, keys), jnp.float32),
        ],
        compiler_params=pltpu.CompilerParams(
            dimension_semantics=("arbitrary", "arbitrary", "arbitrary")
        ),
        cost_estimate=cost,
    )(base, key_pos, query, key_all, value_all, kept, grad_out)


def relay_gather(payload, needed, ctx_at):
    n = lax.axis_size("ctx")
    zero = jnp.zeros_like(payload)
    forward, backward = [payload], [payload]
    for k in range(1, n):
        fwd = [(i, i + k) for i in range(n - k) if needed(i + k, i)]
        relay = [(i + k - 1, i + k) for i, _ in fwd]
        if k > 2 and relay and all(needed(s, r - k) for s, r in relay):
            forward.append(lax.ppermute(forward[-1], "ctx", relay))
        else:
            forward.append(lax.ppermute(payload, "ctx", fwd) if fwd else zero)
        bwd = [(i + k, i) for i in range(n - k) if needed(i, i + k)]
        relay = [(r + 1, r) for _, r in bwd]
        if k > 2 and relay and all(needed(s, r + k) for s, r in relay):
            backward.append(lax.ppermute(backward[-1], "ctx", relay))
        else:
            backward.append(lax.ppermute(payload, "ctx", bwd) if bwd else zero)
    parts = [payload]
    for k in range(1, n):
        parts.append(jnp.where(k <= ctx_at, forward[k], backward[n - k]))
    return parts


def gather_kv(key, value, segment_ids, ctx_at, rep_at, rep_count, needed):
    n = lax.axis_size("ctx")
    key_count, width = key.shape
    seg_rows = -(-key_count // width)
    seg_pad = -(-seg_rows // 16) * 16
    seg_block = jnp.zeros((seg_pad * width,), jnp.bfloat16)
    seg_block = seg_block.at[:key_count].set(segment_ids.astype(jnp.bfloat16))
    seg_block = seg_block.reshape(seg_pad, width)
    split = rep_count == 2
    halves = [jnp.where(rep_at == 0, key, value)] if split else [key, value]
    payloads = [jnp.concatenate([h, seg_block], axis=0) for h in halves]
    gathered = [relay_gather(p, needed, ctx_at) for p in payloads]
    if split:
        mine = gathered[0]
        theirs = [lax.ppermute(p, "rep", [(0, 1), (1, 0)]) for p in mine]
        first = rep_at == 0
        key_parts = [jnp.where(first, a, b) for a, b in zip(mine, theirs)]
        value_parts = [jnp.where(first, b, a) for a, b in zip(mine, theirs)]
    else:
        key_parts, value_parts = gathered
    key_all = jnp.concatenate([p[:key_count] for p in key_parts], axis=0)
    value_all = jnp.concatenate([p[:key_count] for p in value_parts], axis=0)
    seg_all = jnp.concatenate(
        [p[key_count:].reshape(-1)[:key_count] for p in key_parts], axis=0
    ).astype(jnp.int32)
    source = (ctx_at - jnp.arange(n, dtype=jnp.int32)) % n
    key_pos = (source[:, None] * key_count + jnp.arange(key_count, dtype=jnp.int32)[None, :])
    return key_all, value_all, seg_all, key_pos.reshape(1, -1), source


def butterfly_sum(total, axes):
    for axis in axes:
        n = lax.axis_size(axis)
        if n & (n - 1):
            total = lax.psum(total, axis)
            continue
        bit = 1
        while bit < n:
            total = total + lax.ppermute(total, axis, [(i, i ^ bit) for i in range(n)])
            bit *= 2
    return total


def local(query, key, value, out_weight, cotangent, response, segment_ids, masked_segments):
    ctx_count = lax.axis_size("ctx")
    rep_count = lax.axis_size("rep")
    head_count = lax.axis_size("head")
    ctx_at = lax.axis_index("ctx")
    rep_at = lax.axis_index("rep")
    head_at = lax.axis_index("head")
    query_count = query.shape[0]
    key_count = key.shape[0]
    kv_local = key.shape[1] // HD
    heads_local = query.shape[1] // HD
    group_size = heads_local // kv_local
    context_len = key_count * ctx_count
    query_base = context_len - query_count * ctx_count * rep_count
    base = (query_base + (ctx_at * rep_count + rep_at) * query_count).astype(jnp.int32)
    base = jnp.reshape(base, (1,))

    def needed(receiver, block):
        last_query = query_base + (receiver * rep_count + rep_count) * query_count - 1
        return block * key_count <= last_query

    key_all, value_all, seg_shift, key_pos, source = gather_kv(
        key, value, segment_ids, ctx_at, rep_at, rep_count, needed
    )
    kept = jnp.where(
        jnp.any(seg_shift[:, None] == masked_segments[None, :], axis=1), 0.0, 1.0
    ).astype(jnp.float32)[None, :]
    onehot = (
        seg_shift[:, None] == jnp.arange(SEG_DEV * ctx_count, dtype=jnp.int32)[None, :]
    ).astype(jnp.float32)

    grad_masked = jnp.where(response[:, None] > 0, cotangent, jnp.zeros_like(cotangent))
    grad_out = jnp.dot(grad_masked, out_weight.T, preferred_element_type=jnp.float32).astype(
        jnp.bfloat16
    )
    delta, attr = fused_attention(
        base, key_pos, query, key_all, value_all, kept, grad_out, group_size
    )

    inverse = (ctx_at - jnp.arange(ctx_count, dtype=jnp.int32)) % ctx_count
    attr_abs = attr.reshape(ctx_count, key_count)[inverse].reshape(-1)
    seg_part = jnp.dot(attr[0], onehot, precision=lax.Precision.HIGHEST)
    summed = butterfly_sum(jnp.concatenate([attr_abs, seg_part]), ("rep", "ctx", "head"))
    attr_all = summed[:context_len]
    segment_attr = summed[context_len:]

    if head_count == 2:
        cols = out_weight.shape[1] // 2
        send_w = lax.dynamic_slice_in_dim(out_weight, (1 - head_at) * cols, cols, 1)
        send = jnp.dot(delta, send_w, preferred_element_type=jnp.float32)
        got = lax.ppermute(send.astype(jnp.bfloat16), "head", [(0, 1), (1, 0)])
        keep_w = lax.dynamic_slice_in_dim(out_weight, head_at * cols, cols, 1)
        keep = lax.optimization_barrier(jnp.dot(delta, keep_w, preferred_element_type=jnp.float32))
        patch_effect = (keep + got.astype(jnp.float32)).astype(jnp.bfloat16)
    else:
        projected = jnp.dot(delta, out_weight, preferred_element_type=jnp.float32)
        patch_effect = lax.psum_scatter(
            projected.astype(jnp.bfloat16), "head", scatter_dimension=1, tiled=True
        )

    token_attr = lax.dynamic_slice_in_dim(attr_all, ctx_at * key_count, key_count, 0)
    return (patch_effect, token_attr, segment_attr)


def solution(mesh):
    return jax.shard_map(
        local,
        mesh=mesh,
        in_specs=(
            P(("groups", "ctx", "rep"), "head"),
            P(("groups", "ctx"), "head"),
            P(("groups", "ctx"), "head"),
            P("head", None),
            P(("groups", "ctx", "rep"), None),
            P(("groups", "ctx", "rep")),
            P(("groups", "ctx")),
            P("groups"),
        ),
        out_specs=(P(("groups", "ctx", "rep"), "head"), P(("groups", "ctx")), P("groups")),
        check_vma=False,
    )
```

```python
import functools

import jax
import jax.numpy as jnp
from jax import lax
from jax.experimental import pallas as pl
from jax.experimental.pallas import tpu as pltpu
from jax.sharding import PartitionSpec as P

HD = 128
SEG_DEV = 8
NEG_FILL = -1e30
NT_DIMS = (((1,), (1,)), ((), ()))


def attention_body(base_ref, kpos_ref, q_ref, kept_ref, do_ref, k_refs, v_refs, delta_ref, attr_ref, tq, hp):
    r = pl.program_id(2)
    kc = k_refs[0].shape[0]
    rows = hp * tq
    row_pos = base_ref[0] + r * tq + lax.broadcasted_iota(jnp.int32, (rows, 1), 0) % tq
    vis = kpos_ref[...] <= row_pos
    kept = kept_ref[...] > 0.0
    if hp > 1:
        q = jnp.concatenate([q_ref[:, h * HD:(h + 1) * HD] for h in range(hp)], axis=0)
        g_rows = jnp.concatenate([do_ref[:, h * HD:(h + 1) * HD] for h in range(hp)], axis=0)
    else:
        q = q_ref[...]
        g_rows = do_ref[...]
    s = jnp.concatenate(
        [lax.dot_general(q, kr[...], NT_DIMS, preferred_element_type=jnp.float32) for kr in k_refs],
        axis=1,
    ) * (HD ** -0.5)
    s_c = jnp.where(vis, s, NEG_FILL)
    s_m = jnp.where(kept, s_c, NEG_FILL)
    m_c = jnp.max(s_c, axis=1, keepdims=True)
    m_m = jnp.max(s_m, axis=1, keepdims=True)
    e_c = jnp.exp(s_c - m_c)
    e_m = jnp.exp(s_m - m_m)
    l_c = jnp.sum(e_c, axis=1, keepdims=True)
    l_m = jnp.sum(e_m, axis=1, keepdims=True)
    eb_c = e_c.astype(jnp.bfloat16)
    eb_m = e_m.astype(jnp.bfloat16)
    o_c = None
    o_m = None
    for i, vr in enumerate(v_refs):
        v = vr[...]
        pc = jnp.dot(eb_c[:, i * kc:(i + 1) * kc], v, preferred_element_type=jnp.float32)
        pm = jnp.dot(eb_m[:, i * kc:(i + 1) * kc], v, preferred_element_type=jnp.float32)
        o_c = pc if o_c is None else o_c + pc
        o_m = pm if o_m is None else o_m + pm
    o_c = o_c / l_c
    o_m = o_m / l_m
    delta = (o_m - o_c).astype(delta_ref.dtype)
    for h in range(hp):
        delta_ref[:, h * HD:(h + 1) * HD] = delta[h * tq:(h + 1) * tq]
    row_dot = jnp.sum(g_rows.astype(jnp.float32) * o_c, axis=1, keepdims=True)
    d_p = jnp.concatenate(
        [lax.dot_general(g_rows, vr[...], NT_DIMS, preferred_element_type=jnp.float32) for vr in v_refs],
        axis=1,
    )
    log_total = m_c + jnp.log(l_c)
    prob = e_c * (1.0 / l_c)
    contrib = prob * (d_p + (d_p - row_dot) * (s - log_total))
    attr_ref[...] += jnp.sum(contrib, axis=0, keepdims=True)


def attention_kernel(base_ref, kpos_ref, q_ref, kept_ref, do_ref, *refs, tq, hp, n, split):
    mine, theirs = refs[:n], refs[n:2 * n]
    delta_ref, attr_ref = refs[2 * n:]
    first = (pl.program_id(0) == 0) & (pl.program_id(1) == 0) & (pl.program_id(2) == 0)

    @pl.when(first)
    def _():
        attr_ref[...] = jnp.zeros_like(attr_ref)

    args = (base_ref, kpos_ref, q_ref, kept_ref, do_ref)
    if not split:
        attention_body(*args, mine, theirs, delta_ref, attr_ref, tq, hp)
        return

    @pl.when(base_ref[1] == 0)
    def _():
        attention_body(*args, mine, theirs, delta_ref, attr_ref, tq, hp)

    @pl.when(base_ref[1] != 0)
    def _():
        attention_body(*args, theirs, mine, delta_ref, attr_ref, tq, hp)


def fused_attention(base, key_pos, query, mine, theirs, kept, grad_out, group_size, split):
    qc = query.shape[0]
    n = len(mine)
    kc = key_pos.shape[1] // n
    keys = kc * n
    kv_width = mine[0].shape[1]
    width = kv_width * group_size
    kv_local = kv_width // HD
    tq = max(8, min(qc, (128 * 2048) // keys))
    n_rows = qc // tq
    hp = group_size
    grid = (kv_local, 1, n_rows)

    def head_map(g, j, r, b):
        return (r, g + j)

    def kv_map(g, j, r, b):
        return (0, g)

    def fixed(g, j, r, b):
        return (0, 0)

    flops = 8 * qc * keys * HD * kv_local * group_size
    cost = pl.CostEstimate(
        flops=flops,
        transcendentals=2 * qc * keys * kv_local * group_size,
        bytes_accessed=2 * (3 * qc * width + 2 * keys * kv_width) + 4 * keys,
    )
    part_spec = pl.BlockSpec((kc, HD), kv_map)
    return pl.pallas_call(
        functools.partial(attention_kernel, tq=tq, hp=hp, n=n, split=split),
        grid_spec=pltpu.PrefetchScalarGridSpec(
            num_scalar_prefetch=1,
            grid=grid,
            in_specs=[
                pl.BlockSpec((1, keys), fixed),
                pl.BlockSpec((tq, hp * HD), head_map),
                pl.BlockSpec((1, keys), fixed),
                pl.BlockSpec((tq, hp * HD), head_map),
            ] + [part_spec] * (2 * n),
            out_specs=[
                pl.BlockSpec((tq, hp * HD), head_map),
                pl.BlockSpec((1, keys), fixed),
            ],
        ),
        out_shape=[
            jax.ShapeDtypeStruct((qc, width), jnp.bfloat16),
            jax.ShapeDtypeStruct((1, keys), jnp.float32),
        ],
        compiler_params=pltpu.CompilerParams(
            dimension_semantics=("arbitrary", "arbitrary", "arbitrary")
        ),
        cost_estimate=cost,
    )(base, key_pos, query, kept, grad_out, *mine, *theirs)


def relay_gather(payload, needed, ctx_at):
    n = lax.axis_size("ctx")
    zero = jnp.zeros_like(payload)
    forward, backward = [payload], [payload]
    for k in range(1, n):
        fwd = [(i, i + k) for i in range(n - k) if needed(i + k, i)]
        relay = [(i + k - 1, i + k) for i, _ in fwd]
        if k > 2 and relay and all(needed(s, r - k) for s, r in relay):
            forward.append(lax.ppermute(forward[-1], "ctx", relay))
        else:
            forward.append(lax.ppermute(payload, "ctx", fwd) if fwd else zero)
        bwd = [(i + k, i) for i in range(n - k) if needed(i, i + k)]
        relay = [(r + 1, r) for _, r in bwd]
        if k > 2 and relay and all(needed(s, r + k) for s, r in relay):
            backward.append(lax.ppermute(backward[-1], "ctx", relay))
        else:
            backward.append(lax.ppermute(payload, "ctx", bwd) if bwd else zero)
    parts = [payload]
    for k in range(1, n):
        parts.append(jnp.where(k <= ctx_at, forward[k], backward[n - k]))
    return parts


def gather_kv(key, value, segment_ids, ctx_at, rep_at, rep_count, needed):
    n = lax.axis_size("ctx")
    key_count, width = key.shape
    seg_rows = -(-key_count // width)
    seg_pad = -(-seg_rows // 16) * 16
    seg_block = jnp.zeros((seg_pad * width,), jnp.bfloat16)
    seg_block = seg_block.at[:key_count].set(segment_ids.astype(jnp.bfloat16))
    seg_block = seg_block.reshape(seg_pad, width)
    split = rep_count == 2
    halves = [jnp.where(rep_at == 0, key, value)] if split else [key, value]
    payloads = [jnp.concatenate([h, seg_block], axis=0) for h in halves]
    gathered = [relay_gather(p, needed, ctx_at) for p in payloads]
    if split:
        mine = gathered[0]
        theirs = [lax.ppermute(p, "rep", [(0, 1), (1, 0)]) for p in mine]
        key_parts = [jnp.where(rep_at == 0, a, b) for a, b in zip(mine, theirs)]
    else:
        mine, theirs = gathered
        key_parts = mine
    seg_all = jnp.concatenate(
        [p[key_count:].reshape(-1)[:key_count] for p in key_parts], axis=0
    ).astype(jnp.int32)
    source = (ctx_at - jnp.arange(n, dtype=jnp.int32)) % n
    key_pos = (source[:, None] * key_count + jnp.arange(key_count, dtype=jnp.int32)[None, :])
    return mine, theirs, seg_all, key_pos.reshape(1, -1), split


def butterfly_sum(total, axes):
    for axis in axes:
        n = lax.axis_size(axis)
        if n & (n - 1):
            total = lax.psum(total, axis)
            continue
        bit = 1
        while bit < n:
            total = total + lax.ppermute(total, axis, [(i, i ^ bit) for i in range(n)])
            bit *= 2
    return total


def local(query, key, value, out_weight, cotangent, response, segment_ids, masked_segments):
    ctx_count = lax.axis_size("ctx")
    rep_count = lax.axis_size("rep")
    head_count = lax.axis_size("head")
    ctx_at = lax.axis_index("ctx")
    rep_at = lax.axis_index("rep")
    head_at = lax.axis_index("head")
    query_count = query.shape[0]
    key_count = key.shape[0]
    kv_local = key.shape[1] // HD
    heads_local = query.shape[1] // HD
    group_size = heads_local // kv_local
    context_len = key_count * ctx_count
    query_base = context_len - query_count * ctx_count * rep_count
    base = (query_base + (ctx_at * rep_count + rep_at) * query_count).astype(jnp.int32)
    base = jnp.stack([base, rep_at.astype(jnp.int32)])

    def needed(receiver, block):
        last_query = query_base + (receiver * rep_count + rep_count) * query_count - 1
        return block * key_count <= last_query

    mine, theirs, seg_shift, key_pos, split = gather_kv(
        key, value, segment_ids, ctx_at, rep_at, rep_count, needed
    )
    kept = jnp.where(
        jnp.any(seg_shift[:, None] == masked_segments[None, :], axis=1), 0.0, 1.0
    ).astype(jnp.float32)[None, :]
    onehot = (
        seg_shift[:, None] == jnp.arange(SEG_DEV * ctx_count, dtype=jnp.int32)[None, :]
    ).astype(jnp.float32)

    grad_masked = jnp.where(response[:, None] > 0, cotangent, jnp.zeros_like(cotangent))
    grad_out = jnp.dot(grad_masked, out_weight.T, preferred_element_type=jnp.float32).astype(
        jnp.bfloat16
    )
    delta, attr = fused_attention(
        base, key_pos, query, mine, theirs, kept, grad_out, group_size, split
    )

    inverse = (ctx_at - jnp.arange(ctx_count, dtype=jnp.int32)) % ctx_count
    attr_abs = attr.reshape(ctx_count, key_count)[inverse].reshape(-1)
    seg_part = jnp.dot(attr[0], onehot, precision=lax.Precision.HIGHEST)
    summed = butterfly_sum(jnp.concatenate([attr_abs, seg_part]), ("rep", "ctx", "head"))
    attr_all = summed[:context_len]
    segment_attr = summed[context_len:]

    if head_count == 2:
        cols = out_weight.shape[1] // 2
        send_w = lax.dynamic_slice_in_dim(out_weight, (1 - head_at) * cols, cols, 1)
        send = jnp.dot(delta, send_w, preferred_element_type=jnp.float32)
        got = lax.ppermute(send.astype(jnp.bfloat16), "head", [(0, 1), (1, 0)])
        keep_w = lax.dynamic_slice_in_dim(out_weight, head_at * cols, cols, 1)
        keep = lax.optimization_barrier(jnp.dot(delta, keep_w, preferred_element_type=jnp.float32))
        patch_effect = (keep + got.astype(jnp.float32)).astype(jnp.bfloat16)
    else:
        projected = jnp.dot(delta, out_weight, preferred_element_type=jnp.float32)
        patch_effect = lax.psum_scatter(
            projected.astype(jnp.bfloat16), "head", scatter_dimension=1, tiled=True
        )

    token_attr = lax.dynamic_slice_in_dim(attr_all, ctx_at * key_count, key_count, 0)
    return (patch_effect, token_attr, segment_attr)


def solution(mesh):
    return jax.shard_map(
        local,
        mesh=mesh,
        in_specs=(
            P(("groups", "ctx", "rep"), "head"),
            P(("groups", "ctx"), "head"),
            P(("groups", "ctx"), "head"),
            P("head", None),
            P(("groups", "ctx", "rep"), None),
            P(("groups", "ctx", "rep")),
            P(("groups", "ctx")),
            P("groups"),
        ),
        out_specs=(P(("groups", "ctx", "rep"), "head"), P(("groups", "ctx")), P("groups")),
        check_vma=False,
    )
```

```python
import functools

import jax
import jax.numpy as jnp
from jax import lax
from jax.experimental import pallas as pl
from jax.experimental.pallas import tpu as pltpu
from jax.sharding import PartitionSpec as P

HD = 128
SEG_DEV = 8
NEG_FILL = -1e30
NT_DIMS = (((1,), (1,)), ((), ()))


def attention_body(base_ref, kpos_ref, q_ref, kept_ref, do_ref, k_refs, v_refs, delta_ref, attr_ref, tq, hp):
    r = pl.program_id(2)
    kc = k_refs[0].shape[0]
    rows = hp * tq
    row_pos = base_ref[0] + r * tq + lax.broadcasted_iota(jnp.int32, (rows, 1), 0) % tq
    vis = kpos_ref[...] <= row_pos
    kept = kept_ref[...] > 0.0
    if hp > 1:
        q = jnp.concatenate([q_ref[:, h * HD:(h + 1) * HD] for h in range(hp)], axis=0)
        g_rows = jnp.concatenate([do_ref[:, h * HD:(h + 1) * HD] for h in range(hp)], axis=0)
    else:
        q = q_ref[...]
        g_rows = do_ref[...]
    s = jnp.concatenate(
        [lax.dot_general(q, kr[...], NT_DIMS, preferred_element_type=jnp.float32) for kr in k_refs],
        axis=1,
    ) * (HD ** -0.5)
    s_c = jnp.where(vis, s, NEG_FILL)
    s_m = jnp.where(kept, s_c, NEG_FILL)
    m_c = jnp.max(s_c, axis=1, keepdims=True)
    m_m = jnp.max(s_m, axis=1, keepdims=True)
    e_c = jnp.exp(s_c - m_c)
    e_m = jnp.exp(s_m - m_m)
    l_c = jnp.sum(e_c, axis=1, keepdims=True)
    l_m = jnp.sum(e_m, axis=1, keepdims=True)
    eb_c = e_c.astype(jnp.bfloat16)
    eb_m = e_m.astype(jnp.bfloat16)
    o_c = None
    o_m = None
    for i, vr in enumerate(v_refs):
        v = vr[...]
        pc = jnp.dot(eb_c[:, i * kc:(i + 1) * kc], v, preferred_element_type=jnp.float32)
        pm = jnp.dot(eb_m[:, i * kc:(i + 1) * kc], v, preferred_element_type=jnp.float32)
        o_c = pc if o_c is None else o_c + pc
        o_m = pm if o_m is None else o_m + pm
    o_c = o_c / l_c
    o_m = o_m / l_m
    delta = (o_m - o_c).astype(delta_ref.dtype)
    for h in range(hp):
        delta_ref[:, h * HD:(h + 1) * HD] = delta[h * tq:(h + 1) * tq]
    row_dot = jnp.sum(g_rows.astype(jnp.float32) * o_c, axis=1, keepdims=True)
    d_p = jnp.concatenate(
        [lax.dot_general(g_rows, vr[...], NT_DIMS, preferred_element_type=jnp.float32) for vr in v_refs],
        axis=1,
    )
    log_total = m_c + jnp.log(l_c)
    prob = e_c * (1.0 / l_c)
    contrib = prob * (d_p + (d_p - row_dot) * (s - log_total))
    attr_ref[...] += jnp.sum(contrib, axis=0, keepdims=True)


def attention_kernel(base_ref, kpos_ref, q_ref, kept_ref, do_ref, *refs, tq, hp, n, split):
    mine, theirs = refs[:n], refs[n:2 * n]
    delta_ref, attr_ref = refs[2 * n:]
    first = (pl.program_id(0) == 0) & (pl.program_id(1) == 0) & (pl.program_id(2) == 0)

    @pl.when(first)
    def _():
        attr_ref[...] = jnp.zeros_like(attr_ref)

    args = (base_ref, kpos_ref, q_ref, kept_ref, do_ref)
    if not split:
        attention_body(*args, mine, theirs, delta_ref, attr_ref, tq, hp)
        return

    @pl.when(base_ref[1] == 0)
    def _():
        attention_body(*args, mine, theirs, delta_ref, attr_ref, tq, hp)

    @pl.when(base_ref[1] != 0)
    def _():
        attention_body(*args, theirs, mine, delta_ref, attr_ref, tq, hp)


def fused_attention(base, key_pos, query, mine, theirs, kept, grad_out, group_size, split):
    qc = query.shape[0]
    n = len(mine)
    kc = key_pos.shape[1] // n
    keys = kc * n
    kv_width = mine[0].shape[1]
    width = kv_width * group_size
    kv_local = kv_width // HD
    tq = max(8, min(qc, (128 * 2048) // keys))
    n_rows = qc // tq
    hp = group_size
    grid = (kv_local, 1, n_rows)

    def head_map(g, j, r, b):
        return (r, g + j)

    def kv_map(g, j, r, b):
        return (0, g)

    def fixed(g, j, r, b):
        return (0, 0)

    flops = 8 * qc * keys * HD * kv_local * group_size
    cost = pl.CostEstimate(
        flops=flops,
        transcendentals=2 * qc * keys * kv_local * group_size,
        bytes_accessed=2 * (3 * qc * width + 2 * keys * kv_width) + 4 * keys,
    )
    part_spec = pl.BlockSpec((kc, HD), kv_map)
    return pl.pallas_call(
        functools.partial(attention_kernel, tq=tq, hp=hp, n=n, split=split),
        grid_spec=pltpu.PrefetchScalarGridSpec(
            num_scalar_prefetch=1,
            grid=grid,
            in_specs=[
                pl.BlockSpec((1, keys), fixed),
                pl.BlockSpec((tq, hp * HD), head_map),
                pl.BlockSpec((1, keys), fixed),
                pl.BlockSpec((tq, hp * HD), head_map),
            ] + [part_spec] * (2 * n),
            out_specs=[
                pl.BlockSpec((tq, hp * HD), head_map),
                pl.BlockSpec((1, keys), fixed),
            ],
        ),
        out_shape=[
            jax.ShapeDtypeStruct((qc, width), jnp.bfloat16),
            jax.ShapeDtypeStruct((1, keys), jnp.float32),
        ],
        compiler_params=pltpu.CompilerParams(
            dimension_semantics=("arbitrary", "arbitrary", "arbitrary")
        ),
        cost_estimate=cost,
    )(base, key_pos, query, kept, grad_out, *mine, *theirs)


def relay_gather(payload, needed, ctx_at):
    n = lax.axis_size("ctx")
    zero = jnp.zeros_like(payload)
    forward, backward = [payload], [payload]
    for k in range(1, n):
        fwd = [(i, i + k) for i in range(n - k) if needed(i + k, i)]
        relay = [(i + k - 1, i + k) for i, _ in fwd]
        if k > 2 and relay and all(needed(s, r - k) for s, r in relay):
            forward.append(lax.ppermute(forward[-1], "ctx", relay))
        else:
            forward.append(lax.ppermute(payload, "ctx", fwd) if fwd else zero)
        bwd = [(i + k, i) for i in range(n - k) if needed(i, i + k)]
        relay = [(r + 1, r) for _, r in bwd]
        if k > 2 and relay and all(needed(s, r + k) for s, r in relay):
            backward.append(lax.ppermute(backward[-1], "ctx", relay))
        else:
            backward.append(lax.ppermute(payload, "ctx", bwd) if bwd else zero)
    parts = [payload]
    for k in range(1, n):
        parts.append(jnp.where(k <= ctx_at, forward[k], backward[n - k]))
    return parts


def gather_kv(key, value, segment_ids, ctx_at, rep_at, rep_count, needed):
    n = lax.axis_size("ctx")
    key_count, width = key.shape
    seg_rows = -(-key_count // width)
    seg_pad = -(-seg_rows // 16) * 16
    seg_block = jnp.zeros((seg_pad * width,), jnp.bfloat16)
    seg_block = seg_block.at[:key_count].set(segment_ids.astype(jnp.bfloat16))
    seg_block = seg_block.reshape(seg_pad, width)
    split = rep_count == 2
    halves = [jnp.where(rep_at == 0, key, value)] if split else [key, value]
    payloads = [jnp.concatenate([h, seg_block], axis=0) for h in halves]
    gathered = [relay_gather(p, needed, ctx_at) for p in payloads]
    if split:
        mine = gathered[0]
        theirs = [lax.ppermute(p, "rep", [(0, 1), (1, 0)]) for p in mine]
        key_parts = [jnp.where(rep_at == 0, a, b) for a, b in zip(mine, theirs)]
    else:
        mine, theirs = gathered
        key_parts = mine
    seg_all = jnp.concatenate(
        [p[key_count:].reshape(-1)[:key_count] for p in key_parts], axis=0
    ).astype(jnp.int32)
    source = (ctx_at - jnp.arange(n, dtype=jnp.int32)) % n
    key_pos = (source[:, None] * key_count + jnp.arange(key_count, dtype=jnp.int32)[None, :])
    return mine, theirs, seg_all, key_pos.reshape(1, -1), split


def butterfly_sum(total, axes):
    for axis in axes:
        n = lax.axis_size(axis)
        if n & (n - 1):
            total = lax.psum(total, axis)
            continue
        bit = 1
        while bit < n:
            total = total + lax.ppermute(total, axis, [(i, i ^ bit) for i in range(n)])
            bit *= 2
    return total


def local(query, key, value, out_weight, cotangent, response, segment_ids, masked_segments):
    ctx_count = lax.axis_size("ctx")
    rep_count = lax.axis_size("rep")
    head_count = lax.axis_size("head")
    ctx_at = lax.axis_index("ctx")
    rep_at = lax.axis_index("rep")
    head_at = lax.axis_index("head")
    query_count = query.shape[0]
    key_count = key.shape[0]
    kv_local = key.shape[1] // HD
    heads_local = query.shape[1] // HD
    group_size = heads_local // kv_local
    context_len = key_count * ctx_count
    query_base = context_len - query_count * ctx_count * rep_count
    base = (query_base + (ctx_at * rep_count + rep_at) * query_count).astype(jnp.int32)
    base = jnp.stack([base, rep_at.astype(jnp.int32)])

    def needed(receiver, block):
        last_query = query_base + (receiver * rep_count + rep_count) * query_count - 1
        return block * key_count <= last_query

    mine, theirs, seg_shift, key_pos, split = gather_kv(
        key, value, segment_ids, ctx_at, rep_at, rep_count, needed
    )
    kept = jnp.where(
        jnp.any(seg_shift[:, None] == masked_segments[None, :], axis=1), 0.0, 1.0
    ).astype(jnp.float32)[None, :]
    onehot = (
        seg_shift[:, None] == jnp.arange(SEG_DEV * ctx_count, dtype=jnp.int32)[None, :]
    ).astype(jnp.float32)

    grad_masked = jnp.where(response[:, None] > 0, cotangent, jnp.zeros_like(cotangent))
    grad_out = jnp.dot(grad_masked, out_weight.T, preferred_element_type=jnp.float32).astype(
        jnp.bfloat16
    )
    delta, attr = fused_attention(
        base, key_pos, query, mine, theirs, kept, grad_out, group_size, split
    )

    inverse = (ctx_at - jnp.arange(ctx_count, dtype=jnp.int32)) % ctx_count
    order = (inverse[:, None] * key_count + jnp.arange(key_count, dtype=jnp.int32)[None, :]).reshape(-1)
    attr_abs = jnp.take(attr, order, axis=1)
    seg_part = jnp.dot(attr, onehot, precision=lax.Precision.HIGHEST)
    summed = butterfly_sum(jnp.concatenate([attr_abs, seg_part], axis=1), ("rep", "ctx", "head"))
    attr_all = summed[0, :context_len]
    segment_attr = summed[0, context_len:]

    if head_count == 2:
        cols = out_weight.shape[1] // 2
        send_w = lax.dynamic_slice_in_dim(out_weight, (1 - head_at) * cols, cols, 1)
        send = jnp.dot(delta, send_w, preferred_element_type=jnp.float32)
        got = lax.ppermute(send.astype(jnp.bfloat16), "head", [(0, 1), (1, 0)])
        keep_w = lax.dynamic_slice_in_dim(out_weight, head_at * cols, cols, 1)
        keep = lax.optimization_barrier(jnp.dot(delta, keep_w, preferred_element_type=jnp.float32))
        patch_effect = (keep + got.astype(jnp.float32)).astype(jnp.bfloat16)
    else:
        projected = jnp.dot(delta, out_weight, preferred_element_type=jnp.float32)
        patch_effect = lax.psum_scatter(
            projected.astype(jnp.bfloat16), "head", scatter_dimension=1, tiled=True
        )

    token_attr = lax.dynamic_slice_in_dim(attr_all, ctx_at * key_count, key_count, 0)
    return (patch_effect, token_attr, segment_attr)


def solution(mesh):
    return jax.shard_map(
        local,
        mesh=mesh,
        in_specs=(
            P(("groups", "ctx", "rep"), "head"),
            P(("groups", "ctx"), "head"),
            P(("groups", "ctx"), "head"),
            P("head", None),
            P(("groups", "ctx", "rep"), None),
            P(("groups", "ctx", "rep")),
            P(("groups", "ctx")),
            P("groups"),
        ),
        out_specs=(P(("groups", "ctx", "rep"), "head"), P(("groups", "ctx")), P("groups")),
        check_vma=False,
    )
```

```python
import functools

import jax
import jax.numpy as jnp
from jax import lax
from jax.experimental import pallas as pl
from jax.experimental.pallas import tpu as pltpu
from jax.sharding import PartitionSpec as P

HD = 128
SEG_DEV = 8
NEG_FILL = -1e30
NT_DIMS = (((1,), (1,)), ((), ()))


def attention_body(base_ref, kpos_ref, q_ref, kept_ref, do_ref, k_refs, v_refs, delta_ref, attr_ref, tq, hp):
    r = pl.program_id(2)
    kc = k_refs[0].shape[0]
    rows = hp * tq
    row_pos = base_ref[0] + r * tq + lax.broadcasted_iota(jnp.int32, (rows, 1), 0) % tq
    if hp > 1:
        q = jnp.concatenate([q_ref[:, h * HD:(h + 1) * HD] for h in range(hp)], axis=0)
        g_rows = jnp.concatenate([do_ref[:, h * HD:(h + 1) * HD] for h in range(hp)], axis=0)
    else:
        q = q_ref[...]
        g_rows = do_ref[...]
    spans = [slice(i * kc, (i + 1) * kc) for i in range(len(k_refs))]
    s_l, sc_l, sm_l = [], [], []
    for i, kr in enumerate(k_refs):
        s_i = lax.dot_general(q, kr[...], NT_DIMS, preferred_element_type=jnp.float32)
        s_i = s_i * (HD ** -0.5)
        sc_i = jnp.where(kpos_ref[:, spans[i]] <= row_pos, s_i, NEG_FILL)
        sm_i = jnp.where(kept_ref[:, spans[i]] > 0.0, sc_i, NEG_FILL)
        s_l.append(s_i)
        sc_l.append(sc_i)
        sm_l.append(sm_i)
    m_c = functools.reduce(jnp.maximum, [jnp.max(x, axis=1, keepdims=True) for x in sc_l])
    m_m = functools.reduce(jnp.maximum, [jnp.max(x, axis=1, keepdims=True) for x in sm_l])
    ec_l = [jnp.exp(x - m_c) for x in sc_l]
    em_l = [jnp.exp(x - m_m) for x in sm_l]
    l_c = functools.reduce(jnp.add, [jnp.sum(x, axis=1, keepdims=True) for x in ec_l])
    l_m = functools.reduce(jnp.add, [jnp.sum(x, axis=1, keepdims=True) for x in em_l])
    o_c = None
    o_m = None
    for i, vr in enumerate(v_refs):
        v = vr[...]
        pc = jnp.dot(ec_l[i].astype(jnp.bfloat16), v, preferred_element_type=jnp.float32)
        pm = jnp.dot(em_l[i].astype(jnp.bfloat16), v, preferred_element_type=jnp.float32)
        o_c = pc if o_c is None else o_c + pc
        o_m = pm if o_m is None else o_m + pm
    o_c = o_c / l_c
    o_m = o_m / l_m
    delta = (o_m - o_c).astype(delta_ref.dtype)
    for h in range(hp):
        delta_ref[:, h * HD:(h + 1) * HD] = delta[h * tq:(h + 1) * tq]
    row_dot = jnp.sum(g_rows.astype(jnp.float32) * o_c, axis=1, keepdims=True)
    log_total = m_c + jnp.log(l_c)
    inv = 1.0 / l_c
    for i, vr in enumerate(v_refs):
        d_p = lax.dot_general(g_rows, vr[...], NT_DIMS, preferred_element_type=jnp.float32)
        contrib = (ec_l[i] * inv) * (d_p + (d_p - row_dot) * (s_l[i] - log_total))
        attr_ref[:, spans[i]] += jnp.sum(contrib, axis=0, keepdims=True)


def attention_kernel(base_ref, kpos_ref, q_ref, kept_ref, do_ref, *refs, tq, hp, n, split):
    mine, theirs = refs[:n], refs[n:2 * n]
    delta_ref, attr_ref = refs[2 * n:]
    first = (pl.program_id(0) == 0) & (pl.program_id(1) == 0) & (pl.program_id(2) == 0)

    @pl.when(first)
    def _():
        attr_ref[...] = jnp.zeros_like(attr_ref)

    args = (base_ref, kpos_ref, q_ref, kept_ref, do_ref)
    if not split:
        attention_body(*args, mine, theirs, delta_ref, attr_ref, tq, hp)
        return

    @pl.when(base_ref[1] == 0)
    def _():
        attention_body(*args, mine, theirs, delta_ref, attr_ref, tq, hp)

    @pl.when(base_ref[1] != 0)
    def _():
        attention_body(*args, theirs, mine, delta_ref, attr_ref, tq, hp)


def fused_attention(base, key_pos, query, mine, theirs, kept, grad_out, group_size, split):
    qc = query.shape[0]
    n = len(mine)
    kc = key_pos.shape[1] // n
    keys = kc * n
    kv_width = mine[0].shape[1]
    width = kv_width * group_size
    kv_local = kv_width // HD
    tq = max(8, min(qc, (128 * 2048) // keys))
    n_rows = qc // tq
    hp = group_size
    grid = (kv_local, 1, n_rows)

    def head_map(g, j, r, b):
        return (r, g + j)

    def kv_map(g, j, r, b):
        return (0, g)

    def fixed(g, j, r, b):
        return (0, 0)

    flops = 8 * qc * keys * HD * kv_local * group_size
    cost = pl.CostEstimate(
        flops=flops,
        transcendentals=2 * qc * keys * kv_local * group_size,
        bytes_accessed=2 * (3 * qc * width + 2 * keys * kv_width) + 4 * keys,
    )
    part_spec = pl.BlockSpec((kc, HD), kv_map)
    return pl.pallas_call(
        functools.partial(attention_kernel, tq=tq, hp=hp, n=n, split=split),
        grid_spec=pltpu.PrefetchScalarGridSpec(
            num_scalar_prefetch=1,
            grid=grid,
            in_specs=[
                pl.BlockSpec((1, keys), fixed),
                pl.BlockSpec((tq, hp * HD), head_map),
                pl.BlockSpec((1, keys), fixed),
                pl.BlockSpec((tq, hp * HD), head_map),
            ] + [part_spec] * (2 * n),
            out_specs=[
                pl.BlockSpec((tq, hp * HD), head_map),
                pl.BlockSpec((1, keys), fixed),
            ],
        ),
        out_shape=[
            jax.ShapeDtypeStruct((qc, width), jnp.bfloat16),
            jax.ShapeDtypeStruct((1, keys), jnp.float32),
        ],
        compiler_params=pltpu.CompilerParams(
            dimension_semantics=("arbitrary", "arbitrary", "arbitrary")
        ),
        cost_estimate=cost,
    )(base, key_pos, query, kept, grad_out, *mine, *theirs)


def relay_gather(payload, needed, ctx_at):
    n = lax.axis_size("ctx")
    zero = jnp.zeros_like(payload)
    forward, backward = [payload], [payload]
    for k in range(1, n):
        fwd = [(i, i + k) for i in range(n - k) if needed(i + k, i)]
        relay = [(i + k - 1, i + k) for i, _ in fwd]
        if k > 2 and relay and all(needed(s, r - k) for s, r in relay):
            forward.append(lax.ppermute(forward[-1], "ctx", relay))
        else:
            forward.append(lax.ppermute(payload, "ctx", fwd) if fwd else zero)
        bwd = [(i + k, i) for i in range(n - k) if needed(i, i + k)]
        relay = [(r + 1, r) for _, r in bwd]
        if k > 2 and relay and all(needed(s, r + k) for s, r in relay):
            backward.append(lax.ppermute(backward[-1], "ctx", relay))
        else:
            backward.append(lax.ppermute(payload, "ctx", bwd) if bwd else zero)
    parts = [payload]
    for k in range(1, n):
        parts.append(jnp.where(k <= ctx_at, forward[k], backward[n - k]))
    return parts


def gather_kv(key, value, segment_ids, ctx_at, rep_at, rep_count, needed):
    n = lax.axis_size("ctx")
    key_count, width = key.shape
    seg_rows = -(-key_count // width)
    seg_pad = -(-seg_rows // 16) * 16
    seg_block = jnp.zeros((seg_pad * width,), jnp.bfloat16)
    seg_block = seg_block.at[:key_count].set(segment_ids.astype(jnp.bfloat16))
    seg_block = seg_block.reshape(seg_pad, width)
    split = rep_count == 2
    halves = [jnp.where(rep_at == 0, key, value)] if split else [key, value]
    payloads = [jnp.concatenate([h, seg_block], axis=0) for h in halves]
    gathered = [relay_gather(p, needed, ctx_at) for p in payloads]
    if split:
        mine = gathered[0]
        theirs = [lax.ppermute(p, "rep", [(0, 1), (1, 0)]) for p in mine]
        key_parts = [jnp.where(rep_at == 0, a, b) for a, b in zip(mine, theirs)]
    else:
        mine, theirs = gathered
        key_parts = mine
    seg_all = jnp.concatenate(
        [p[key_count:].reshape(-1)[:key_count] for p in key_parts], axis=0
    ).astype(jnp.int32)
    source = (ctx_at - jnp.arange(n, dtype=jnp.int32)) % n
    key_pos = (source[:, None] * key_count + jnp.arange(key_count, dtype=jnp.int32)[None, :])
    return mine, theirs, seg_all, key_pos.reshape(1, -1), split


def butterfly_sum(total, axes):
    for axis in axes:
        n = lax.axis_size(axis)
        if n & (n - 1):
            total = lax.psum(total, axis)
            continue
        bit = 1
        while bit < n:
            total = total + lax.ppermute(total, axis, [(i, i ^ bit) for i in range(n)])
            bit *= 2
    return total


def local(query, key, value, out_weight, cotangent, response, segment_ids, masked_segments):
    ctx_count = lax.axis_size("ctx")
    rep_count = lax.axis_size("rep")
    head_count = lax.axis_size("head")
    ctx_at = lax.axis_index("ctx")
    rep_at = lax.axis_index("rep")
    head_at = lax.axis_index("head")
    query_count = query.shape[0]
    key_count = key.shape[0]
    kv_local = key.shape[1] // HD
    heads_local = query.shape[1] // HD
    group_size = heads_local // kv_local
    context_len = key_count * ctx_count
    query_base = context_len - query_count * ctx_count * rep_count
    base = (query_base + (ctx_at * rep_count + rep_at) * query_count).astype(jnp.int32)
    base = jnp.stack([base, rep_at.astype(jnp.int32)])

    def needed(receiver, block):
        last_query = query_base + (receiver * rep_count + rep_count) * query_count - 1
        return block * key_count <= last_query

    mine, theirs, seg_shift, key_pos, split = gather_kv(
        key, value, segment_ids, ctx_at, rep_at, rep_count, needed
    )
    kept = jnp.where(
        jnp.any(seg_shift[:, None] == masked_segments[None, :], axis=1), 0.0, 1.0
    ).astype(jnp.float32)[None, :]
    onehot = (
        seg_shift[:, None] == jnp.arange(SEG_DEV * ctx_count, dtype=jnp.int32)[None, :]
    ).astype(jnp.float32)

    grad_masked = jnp.where(response[:, None] > 0, cotangent, jnp.zeros_like(cotangent))
    grad_out = jnp.dot(grad_masked, out_weight.T, preferred_element_type=jnp.float32).astype(
        jnp.bfloat16
    )
    delta, attr = fused_attention(
        base, key_pos, query, mine, theirs, kept, grad_out, group_size, split
    )

    inverse = (ctx_at - jnp.arange(ctx_count, dtype=jnp.int32)) % ctx_count
    attr_abs = attr.reshape(ctx_count, key_count)[inverse].reshape(-1)
    seg_part = jnp.dot(attr[0], onehot, precision=lax.Precision.HIGHEST)
    summed = butterfly_sum(jnp.concatenate([attr_abs, seg_part]), ("rep", "ctx", "head"))
    attr_all = summed[:context_len]
    segment_attr = summed[context_len:]

    if head_count == 2:
        cols = out_weight.shape[1] // 2
        send_w = lax.dynamic_slice_in_dim(out_weight, (1 - head_at) * cols, cols, 1)
        send = jnp.dot(delta, send_w, preferred_element_type=jnp.float32)
        got = lax.ppermute(send.astype(jnp.bfloat16), "head", [(0, 1), (1, 0)])
        keep_w = lax.dynamic_slice_in_dim(out_weight, head_at * cols, cols, 1)
        keep = lax.optimization_barrier(jnp.dot(delta, keep_w, preferred_element_type=jnp.float32))
        patch_effect = (keep + got.astype(jnp.float32)).astype(jnp.bfloat16)
    else:
        projected = jnp.dot(delta, out_weight, preferred_element_type=jnp.float32)
        patch_effect = lax.psum_scatter(
            projected.astype(jnp.bfloat16), "head", scatter_dimension=1, tiled=True
        )

    token_attr = lax.dynamic_slice_in_dim(attr_all, ctx_at * key_count, key_count, 0)
    return (patch_effect, token_attr, segment_attr)


def solution(mesh):
    return jax.shard_map(
        local,
        mesh=mesh,
        in_specs=(
            P(("groups", "ctx", "rep"), "head"),
            P(("groups", "ctx"), "head"),
            P(("groups", "ctx"), "head"),
            P("head", None),
            P(("groups", "ctx", "rep"), None),
            P(("groups", "ctx", "rep")),
            P(("groups", "ctx")),
            P("groups"),
        ),
        out_specs=(P(("groups", "ctx", "rep"), "head"), P(("groups", "ctx")), P("groups")),
        check_vma=False,
    )
```

```python
import functools

import jax
import jax.numpy as jnp
from jax import lax
from jax.experimental import pallas as pl
from jax.experimental.pallas import tpu as pltpu
from jax.sharding import PartitionSpec as P

HD = 128
SEG_DEV = 8
NEG_FILL = -1e30
NT_DIMS = (((1,), (1,)), ((), ()))


def attention_body(base_ref, kpos_ref, q_ref, kept_ref, do_ref, k_refs, v_refs, delta_ref, attr_ref, tq, hp):
    r = pl.program_id(2)
    kc = k_refs[0].shape[0]
    rows = hp * tq
    row_pos = base_ref[0] + r * tq + lax.broadcasted_iota(jnp.int32, (rows, 1), 0) % tq
    if hp > 1:
        q = jnp.concatenate([q_ref[:, h * HD:(h + 1) * HD] for h in range(hp)], axis=0)
        g_rows = jnp.concatenate([do_ref[:, h * HD:(h + 1) * HD] for h in range(hp)], axis=0)
    else:
        q = q_ref[...]
        g_rows = do_ref[...]
    spans = [slice(i * kc, (i + 1) * kc) for i in range(len(k_refs))]
    s_l, sc_l, sm_l = [], [], []
    for i, kr in enumerate(k_refs):
        s_i = lax.dot_general(q, kr[...], NT_DIMS, preferred_element_type=jnp.float32)
        s_i = s_i * (HD ** -0.5)
        sc_i = jnp.where(kpos_ref[:, spans[i]] <= row_pos, s_i, NEG_FILL)
        sm_i = jnp.where(kept_ref[:, spans[i]] > 0.0, sc_i, NEG_FILL)
        s_l.append(s_i)
        sc_l.append(sc_i)
        sm_l.append(sm_i)
    m_c = functools.reduce(jnp.maximum, [jnp.max(x, axis=1, keepdims=True) for x in sc_l])
    m_m = functools.reduce(jnp.maximum, [jnp.max(x, axis=1, keepdims=True) for x in sm_l])
    ec_l = [jnp.exp(x - m_c) for x in sc_l]
    em_l = [jnp.exp(x - m_m) for x in sm_l]
    l_c = functools.reduce(jnp.add, [jnp.sum(x, axis=1, keepdims=True) for x in ec_l])
    l_m = functools.reduce(jnp.add, [jnp.sum(x, axis=1, keepdims=True) for x in em_l])
    o_c = None
    o_m = None
    for i, vr in enumerate(v_refs):
        v = vr[...]
        pc = jnp.dot(ec_l[i].astype(jnp.bfloat16), v, preferred_element_type=jnp.float32)
        pm = jnp.dot(em_l[i].astype(jnp.bfloat16), v, preferred_element_type=jnp.float32)
        o_c = pc if o_c is None else o_c + pc
        o_m = pm if o_m is None else o_m + pm
    o_c = o_c / l_c
    o_m = o_m / l_m
    delta = (o_m - o_c).astype(delta_ref.dtype)
    for h in range(hp):
        delta_ref[:, h * HD:(h + 1) * HD] = delta[h * tq:(h + 1) * tq]
    row_dot = jnp.sum(g_rows.astype(jnp.float32) * o_c, axis=1, keepdims=True)
    log_total = m_c + jnp.log(l_c)
    inv = 1.0 / l_c
    for i, vr in enumerate(v_refs):
        d_p = lax.dot_general(g_rows, vr[...], NT_DIMS, preferred_element_type=jnp.float32)
        contrib = (ec_l[i] * inv) * (d_p + (d_p - row_dot) * (s_l[i] - log_total))
        attr_ref[spans[i]] += jnp.sum(contrib, axis=0)


def attention_kernel(base_ref, kpos_ref, q_ref, kept_ref, do_ref, *refs, tq, hp, n, split):
    mine, theirs = refs[:n], refs[n:2 * n]
    delta_ref, attr_ref = refs[2 * n:]
    first = (pl.program_id(0) == 0) & (pl.program_id(1) == 0) & (pl.program_id(2) == 0)

    @pl.when(first)
    def _():
        attr_ref[...] = jnp.zeros_like(attr_ref)

    args = (base_ref, kpos_ref, q_ref, kept_ref, do_ref)
    if not split:
        attention_body(*args, mine, theirs, delta_ref, attr_ref, tq, hp)
        return

    @pl.when(base_ref[1] == 0)
    def _():
        attention_body(*args, mine, theirs, delta_ref, attr_ref, tq, hp)

    @pl.when(base_ref[1] != 0)
    def _():
        attention_body(*args, theirs, mine, delta_ref, attr_ref, tq, hp)


def fused_attention(base, key_pos, query, mine, theirs, kept, grad_out, group_size, split):
    qc = query.shape[0]
    n = len(mine)
    kc = key_pos.shape[1] // n
    keys = kc * n
    kv_width = mine[0].shape[1]
    width = kv_width * group_size
    kv_local = kv_width // HD
    tq = max(8, min(qc, (128 * 2048) // keys))
    n_rows = qc // tq
    hp = group_size
    grid = (kv_local, 1, n_rows)

    def head_map(g, j, r, b):
        return (r, g + j)

    def kv_map(g, j, r, b):
        return (0, g)

    def fixed(g, j, r, b):
        return (0, 0)

    flops = 8 * qc * keys * HD * kv_local * group_size
    cost = pl.CostEstimate(
        flops=flops,
        transcendentals=2 * qc * keys * kv_local * group_size,
        bytes_accessed=2 * (3 * qc * width + 2 * keys * kv_width) + 4 * keys,
    )
    part_spec = pl.BlockSpec((kc, HD), kv_map)
    return pl.pallas_call(
        functools.partial(attention_kernel, tq=tq, hp=hp, n=n, split=split),
        grid_spec=pltpu.PrefetchScalarGridSpec(
            num_scalar_prefetch=1,
            grid=grid,
            in_specs=[
                pl.BlockSpec((1, keys), fixed),
                pl.BlockSpec((tq, hp * HD), head_map),
                pl.BlockSpec((1, keys), fixed),
                pl.BlockSpec((tq, hp * HD), head_map),
            ] + [part_spec] * (2 * n),
            out_specs=[
                pl.BlockSpec((tq, hp * HD), head_map),
                pl.BlockSpec((keys,), lambda g, j, r, b: (0,)),
            ],
        ),
        out_shape=[
            jax.ShapeDtypeStruct((qc, width), jnp.bfloat16),
            jax.ShapeDtypeStruct((keys,), jnp.float32),
        ],
        compiler_params=pltpu.CompilerParams(
            dimension_semantics=("arbitrary", "arbitrary", "arbitrary")
        ),
        cost_estimate=cost,
    )(base, key_pos, query, kept, grad_out, *mine, *theirs)


def relay_gather(payload, needed, ctx_at):
    n = lax.axis_size("ctx")
    zero = jnp.zeros_like(payload)
    forward, backward = [payload], [payload]
    for k in range(1, n):
        fwd = [(i, i + k) for i in range(n - k) if needed(i + k, i)]
        relay = [(i + k - 1, i + k) for i, _ in fwd]
        if k > 2 and relay and all(needed(s, r - k) for s, r in relay):
            forward.append(lax.ppermute(forward[-1], "ctx", relay))
        else:
            forward.append(lax.ppermute(payload, "ctx", fwd) if fwd else zero)
        bwd = [(i + k, i) for i in range(n - k) if needed(i, i + k)]
        relay = [(r + 1, r) for _, r in bwd]
        if k > 2 and relay and all(needed(s, r + k) for s, r in relay):
            backward.append(lax.ppermute(backward[-1], "ctx", relay))
        else:
            backward.append(lax.ppermute(payload, "ctx", bwd) if bwd else zero)
    parts = [payload]
    for k in range(1, n):
        parts.append(jnp.where(k <= ctx_at, forward[k], backward[n - k]))
    return parts


def gather_kv(key, value, segment_ids, ctx_at, rep_at, rep_count, needed):
    n = lax.axis_size("ctx")
    key_count, width = key.shape
    seg_rows = -(-key_count // width)
    seg_pad = -(-seg_rows // 16) * 16
    seg_block = jnp.zeros((seg_pad * width,), jnp.bfloat16)
    seg_block = seg_block.at[:key_count].set(segment_ids.astype(jnp.bfloat16))
    seg_block = seg_block.reshape(seg_pad, width)
    split = rep_count == 2
    halves = [jnp.where(rep_at == 0, key, value)] if split else [key, value]
    payloads = [jnp.concatenate([h, seg_block], axis=0) for h in halves]
    gathered = [relay_gather(p, needed, ctx_at) for p in payloads]
    if split:
        mine = gathered[0]
        theirs = [lax.ppermute(p, "rep", [(0, 1), (1, 0)]) for p in mine]
        key_parts = [jnp.where(rep_at == 0, a, b) for a, b in zip(mine, theirs)]
    else:
        mine, theirs = gathered
        key_parts = mine
    seg_all = jnp.concatenate(
        [p[key_count:].reshape(-1)[:key_count] for p in key_parts], axis=0
    ).astype(jnp.int32)
    source = (ctx_at - jnp.arange(n, dtype=jnp.int32)) % n
    key_pos = (source[:, None] * key_count + jnp.arange(key_count, dtype=jnp.int32)[None, :])
    return mine, theirs, seg_all, key_pos.reshape(1, -1), split


def butterfly_sum(total, axes):
    for axis in axes:
        n = lax.axis_size(axis)
        if n & (n - 1):
            total = lax.psum(total, axis)
            continue
        bit = 1
        while bit < n:
            total = total + lax.ppermute(total, axis, [(i, i ^ bit) for i in range(n)])
            bit *= 2
    return total


def local(query, key, value, out_weight, cotangent, response, segment_ids, masked_segments):
    ctx_count = lax.axis_size("ctx")
    rep_count = lax.axis_size("rep")
    head_count = lax.axis_size("head")
    ctx_at = lax.axis_index("ctx")
    rep_at = lax.axis_index("rep")
    head_at = lax.axis_index("head")
    query_count = query.shape[0]
    key_count = key.shape[0]
    kv_local = key.shape[1] // HD
    heads_local = query.shape[1] // HD
    group_size = heads_local // kv_local
    context_len = key_count * ctx_count
    query_base = context_len - query_count * ctx_count * rep_count
    base = (query_base + (ctx_at * rep_count + rep_at) * query_count).astype(jnp.int32)
    base = jnp.stack([base, rep_at.astype(jnp.int32)])

    def needed(receiver, block):
        last_query = query_base + (receiver * rep_count + rep_count) * query_count - 1
        return block * key_count <= last_query

    mine, theirs, seg_shift, key_pos, split = gather_kv(
        key, value, segment_ids, ctx_at, rep_at, rep_count, needed
    )
    kept = jnp.where(
        jnp.any(seg_shift[:, None] == masked_segments[None, :], axis=1), 0.0, 1.0
    ).astype(jnp.float32)[None, :]
    onehot = (
        seg_shift[:, None] == jnp.arange(SEG_DEV * ctx_count, dtype=jnp.int32)[None, :]
    ).astype(jnp.float32)

    grad_masked = jnp.where(response[:, None] > 0, cotangent, jnp.zeros_like(cotangent))
    grad_out = jnp.dot(grad_masked, out_weight.T, preferred_element_type=jnp.float32).astype(
        jnp.bfloat16
    )
    delta, attr = fused_attention(
        base, key_pos, query, mine, theirs, kept, grad_out, group_size, split
    )

    inverse = (ctx_at - jnp.arange(ctx_count, dtype=jnp.int32)) % ctx_count
    attr_abs = attr.reshape(ctx_count, key_count)[inverse].reshape(-1)
    seg_part = jnp.dot(attr, onehot, precision=lax.Precision.HIGHEST)
    summed = butterfly_sum(jnp.concatenate([attr_abs, seg_part]), ("rep", "ctx", "head"))
    attr_all = summed[:context_len]
    segment_attr = summed[context_len:]

    if head_count == 2:
        cols = out_weight.shape[1] // 2
        send_w = lax.dynamic_slice_in_dim(out_weight, (1 - head_at) * cols, cols, 1)
        send = jnp.dot(delta, send_w, preferred_element_type=jnp.float32)
        got = lax.ppermute(send.astype(jnp.bfloat16), "head", [(0, 1), (1, 0)])
        keep_w = lax.dynamic_slice_in_dim(out_weight, head_at * cols, cols, 1)
        keep = lax.optimization_barrier(jnp.dot(delta, keep_w, preferred_element_type=jnp.float32))
        patch_effect = (keep + got.astype(jnp.float32)).astype(jnp.bfloat16)
    else:
        projected = jnp.dot(delta, out_weight, preferred_element_type=jnp.float32)
        patch_effect = lax.psum_scatter(
            projected.astype(jnp.bfloat16), "head", scatter_dimension=1, tiled=True
        )

    token_attr = lax.dynamic_slice_in_dim(attr_all, ctx_at * key_count, key_count, 0)
    return (patch_effect, token_attr, segment_attr)


def solution(mesh):
    return jax.shard_map(
        local,
        mesh=mesh,
        in_specs=(
            P(("groups", "ctx", "rep"), "head"),
            P(("groups", "ctx"), "head"),
            P(("groups", "ctx"), "head"),
            P("head", None),
            P(("groups", "ctx", "rep"), None),
            P(("groups", "ctx", "rep")),
            P(("groups", "ctx")),
            P("groups"),
        ),
        out_specs=(P(("groups", "ctx", "rep"), "head"), P(("groups", "ctx")), P("groups")),
        check_vma=False,
    )
```

```python
import functools

import jax
import jax.numpy as jnp
from jax import lax
from jax.experimental import pallas as pl
from jax.experimental.pallas import tpu as pltpu
from jax.sharding import PartitionSpec as P

HD = 128
SEG_DEV = 8
NEG_FILL = -1e30
NT_DIMS = (((1,), (1,)), ((), ()))


def attention_body(base_ref, kpos_ref, q_ref, kept_ref, do_ref, k_refs, v_refs, delta_ref, attr_ref, tq, hp):
    r = pl.program_id(2)
    kc = k_refs[0].shape[0]
    rows = hp * tq
    row_pos = base_ref[0] + r * tq + lax.broadcasted_iota(jnp.int32, (rows, 1), 0) % tq
    if hp > 1:
        q = jnp.concatenate([q_ref[:, h * HD:(h + 1) * HD] for h in range(hp)], axis=0)
        g_rows = jnp.concatenate([do_ref[:, h * HD:(h + 1) * HD] for h in range(hp)], axis=0)
    else:
        q = q_ref[...]
        g_rows = do_ref[...]
    spans = [slice(i * kc, (i + 1) * kc) for i in range(len(k_refs))]
    s_l, sc_l, sm_l = [], [], []
    for i, kr in enumerate(k_refs):
        s_i = lax.dot_general(q, kr[...], NT_DIMS, preferred_element_type=jnp.float32)
        s_i = s_i * (HD ** -0.5)
        sc_i = jnp.where(kpos_ref[:, spans[i]] <= row_pos, s_i, NEG_FILL)
        sm_i = jnp.where(kept_ref[:, spans[i]] > 0.0, sc_i, NEG_FILL)
        s_l.append(s_i)
        sc_l.append(sc_i)
        sm_l.append(sm_i)
    m_c = functools.reduce(jnp.maximum, [jnp.max(x, axis=1, keepdims=True) for x in sc_l])
    m_m = functools.reduce(jnp.maximum, [jnp.max(x, axis=1, keepdims=True) for x in sm_l])
    ec_l = [jnp.exp(x - m_c) for x in sc_l]
    em_l = [jnp.exp(x - m_m) for x in sm_l]
    l_c = functools.reduce(jnp.add, [jnp.sum(x, axis=1, keepdims=True) for x in ec_l])
    l_m = functools.reduce(jnp.add, [jnp.sum(x, axis=1, keepdims=True) for x in em_l])
    o_c = None
    o_m = None
    for i, vr in enumerate(v_refs):
        v = vr[...]
        pc = jnp.dot(ec_l[i].astype(jnp.bfloat16), v, preferred_element_type=jnp.float32)
        pm = jnp.dot(em_l[i].astype(jnp.bfloat16), v, preferred_element_type=jnp.float32)
        o_c = pc if o_c is None else o_c + pc
        o_m = pm if o_m is None else o_m + pm
    o_c = o_c / l_c
    o_m = o_m / l_m
    delta = (o_m - o_c).astype(delta_ref.dtype)
    for h in range(hp):
        delta_ref[:, h * HD:(h + 1) * HD] = delta[h * tq:(h + 1) * tq]
    row_dot = jnp.sum(g_rows.astype(jnp.float32) * o_c, axis=1, keepdims=True)
    log_total = m_c + jnp.log(l_c)
    inv = 1.0 / l_c
    for i, vr in enumerate(v_refs):
        d_p = lax.dot_general(g_rows, vr[...], NT_DIMS, preferred_element_type=jnp.float32)
        contrib = (ec_l[i] * inv) * (d_p + (d_p - row_dot) * (s_l[i] - log_total))
        src = (base_ref[2] - i + len(v_refs)) % len(v_refs)
        at = pl.ds(pl.multiple_of(src * kc, kc), kc)
        attr_ref[at] += jnp.sum(contrib, axis=0)


def attention_kernel(base_ref, kpos_ref, q_ref, kept_ref, do_ref, *refs, tq, hp, n, split):
    mine, theirs = refs[:n], refs[n:2 * n]
    delta_ref, attr_ref = refs[2 * n:]
    first = (pl.program_id(0) == 0) & (pl.program_id(1) == 0) & (pl.program_id(2) == 0)

    @pl.when(first)
    def _():
        attr_ref[...] = jnp.zeros_like(attr_ref)

    args = (base_ref, kpos_ref, q_ref, kept_ref, do_ref)
    if not split:
        attention_body(*args, mine, theirs, delta_ref, attr_ref, tq, hp)
        return

    @pl.when(base_ref[1] == 0)
    def _():
        attention_body(*args, mine, theirs, delta_ref, attr_ref, tq, hp)

    @pl.when(base_ref[1] != 0)
    def _():
        attention_body(*args, theirs, mine, delta_ref, attr_ref, tq, hp)


def fused_attention(base, key_pos, query, mine, theirs, kept, grad_out, group_size, split):
    qc = query.shape[0]
    n = len(mine)
    kc = key_pos.shape[1] // n
    keys = kc * n
    kv_width = mine[0].shape[1]
    width = kv_width * group_size
    kv_local = kv_width // HD
    tq = max(8, min(qc, (128 * 2048) // keys))
    n_rows = qc // tq
    hp = group_size
    grid = (kv_local, 1, n_rows)

    def head_map(g, j, r, b):
        return (r, g + j)

    def kv_map(g, j, r, b):
        return (0, g)

    def fixed(g, j, r, b):
        return (0, 0)

    flops = 8 * qc * keys * HD * kv_local * group_size
    cost = pl.CostEstimate(
        flops=flops,
        transcendentals=2 * qc * keys * kv_local * group_size,
        bytes_accessed=2 * (3 * qc * width + 2 * keys * kv_width) + 4 * keys,
    )
    part_spec = pl.BlockSpec((kc, HD), kv_map)
    return pl.pallas_call(
        functools.partial(attention_kernel, tq=tq, hp=hp, n=n, split=split),
        grid_spec=pltpu.PrefetchScalarGridSpec(
            num_scalar_prefetch=1,
            grid=grid,
            in_specs=[
                pl.BlockSpec((1, keys), fixed),
                pl.BlockSpec((tq, hp * HD), head_map),
                pl.BlockSpec((1, keys), fixed),
                pl.BlockSpec((tq, hp * HD), head_map),
            ] + [part_spec] * (2 * n),
            out_specs=[
                pl.BlockSpec((tq, hp * HD), head_map),
                pl.BlockSpec((keys,), lambda g, j, r, b: (0,)),
            ],
        ),
        out_shape=[
            jax.ShapeDtypeStruct((qc, width), jnp.bfloat16),
            jax.ShapeDtypeStruct((keys,), jnp.float32),
        ],
        compiler_params=pltpu.CompilerParams(
            dimension_semantics=("arbitrary", "arbitrary", "arbitrary")
        ),
        cost_estimate=cost,
    )(base, key_pos, query, kept, grad_out, *mine, *theirs)


def relay_gather(payload, needed, ctx_at):
    n = lax.axis_size("ctx")
    zero = jnp.zeros_like(payload)
    forward, backward = [payload], [payload]
    for k in range(1, n):
        fwd = [(i, i + k) for i in range(n - k) if needed(i + k, i)]
        relay = [(i + k - 1, i + k) for i, _ in fwd]
        if k > 2 and relay and all(needed(s, r - k) for s, r in relay):
            forward.append(lax.ppermute(forward[-1], "ctx", relay))
        else:
            forward.append(lax.ppermute(payload, "ctx", fwd) if fwd else zero)
        bwd = [(i + k, i) for i in range(n - k) if needed(i, i + k)]
        relay = [(r + 1, r) for _, r in bwd]
        if k > 2 and relay and all(needed(s, r + k) for s, r in relay):
            backward.append(lax.ppermute(backward[-1], "ctx", relay))
        else:
            backward.append(lax.ppermute(payload, "ctx", bwd) if bwd else zero)
    parts = [payload]
    for k in range(1, n):
        parts.append(jnp.where(k <= ctx_at, forward[k], backward[n - k]))
    return parts


def gather_kv(key, value, segment_ids, ctx_at, rep_at, rep_count, needed):
    n = lax.axis_size("ctx")
    key_count, width = key.shape
    seg_rows = -(-key_count // width)
    seg_pad = -(-seg_rows // 16) * 16
    seg_block = jnp.zeros((seg_pad * width,), jnp.bfloat16)
    seg_block = seg_block.at[:key_count].set(segment_ids.astype(jnp.bfloat16))
    seg_block = seg_block.reshape(seg_pad, width)
    split = rep_count == 2
    halves = [jnp.where(rep_at == 0, key, value)] if split else [key, value]
    payloads = [jnp.concatenate([h, seg_block], axis=0) for h in halves]
    gathered = [relay_gather(p, needed, ctx_at) for p in payloads]
    if split:
        mine = gathered[0]
        theirs = [lax.ppermute(p, "rep", [(0, 1), (1, 0)]) for p in mine]
        key_parts = [jnp.where(rep_at == 0, a, b) for a, b in zip(mine, theirs)]
    else:
        mine, theirs = gathered
        key_parts = mine
    seg_all = jnp.concatenate(
        [p[key_count:].reshape(-1)[:key_count] for p in key_parts], axis=0
    ).astype(jnp.int32)
    source = (ctx_at - jnp.arange(n, dtype=jnp.int32)) % n
    key_pos = (source[:, None] * key_count + jnp.arange(key_count, dtype=jnp.int32)[None, :])
    return mine, theirs, seg_all, key_pos.reshape(1, -1), split


def butterfly_sum(total, axes):
    for axis in axes:
        n = lax.axis_size(axis)
        if n & (n - 1):
            total = lax.psum(total, axis)
            continue
        bit = 1
        while bit < n:
            total = total + lax.ppermute(total, axis, [(i, i ^ bit) for i in range(n)])
            bit *= 2
    return total


def local(query, key, value, out_weight, cotangent, response, segment_ids, masked_segments):
    ctx_count = lax.axis_size("ctx")
    rep_count = lax.axis_size("rep")
    head_count = lax.axis_size("head")
    ctx_at = lax.axis_index("ctx")
    rep_at = lax.axis_index("rep")
    head_at = lax.axis_index("head")
    query_count = query.shape[0]
    key_count = key.shape[0]
    kv_local = key.shape[1] // HD
    heads_local = query.shape[1] // HD
    group_size = heads_local // kv_local
    context_len = key_count * ctx_count
    query_base = context_len - query_count * ctx_count * rep_count
    base = (query_base + (ctx_at * rep_count + rep_at) * query_count).astype(jnp.int32)
    base = jnp.stack([base, rep_at.astype(jnp.int32), ctx_at.astype(jnp.int32)])

    def needed(receiver, block):
        last_query = query_base + (receiver * rep_count + rep_count) * query_count - 1
        return block * key_count <= last_query

    mine, theirs, seg_shift, key_pos, split = gather_kv(
        key, value, segment_ids, ctx_at, rep_at, rep_count, needed
    )
    kept = jnp.where(
        jnp.any(seg_shift[:, None] == masked_segments[None, :], axis=1), 0.0, 1.0
    ).astype(jnp.float32)[None, :]
    inverse = (ctx_at - jnp.arange(ctx_count, dtype=jnp.int32)) % ctx_count
    seg_abs = seg_shift.reshape(ctx_count, key_count)[inverse].reshape(-1)
    onehot = (
        seg_abs[:, None] == jnp.arange(SEG_DEV * ctx_count, dtype=jnp.int32)[None, :]
    ).astype(jnp.float32)

    grad_masked = jnp.where(response[:, None] > 0, cotangent, jnp.zeros_like(cotangent))
    grad_out = jnp.dot(grad_masked, out_weight.T, preferred_element_type=jnp.float32).astype(
        jnp.bfloat16
    )
    delta, attr = fused_attention(
        base, key_pos, query, mine, theirs, kept, grad_out, group_size, split
    )

    inverse = (ctx_at - jnp.arange(ctx_count, dtype=jnp.int32)) % ctx_count
    attr_abs = attr
    seg_part = jnp.dot(attr, onehot, precision=lax.Precision.HIGHEST)
    summed = butterfly_sum(jnp.concatenate([attr_abs, seg_part]), ("rep", "ctx", "head"))
    attr_all = summed[:context_len]
    segment_attr = summed[context_len:]

    if head_count == 2:
        cols = out_weight.shape[1] // 2
        send_w = lax.dynamic_slice_in_dim(out_weight, (1 - head_at) * cols, cols, 1)
        send = jnp.dot(delta, send_w, preferred_element_type=jnp.float32)
        got = lax.ppermute(send.astype(jnp.bfloat16), "head", [(0, 1), (1, 0)])
        keep_w = lax.dynamic_slice_in_dim(out_weight, head_at * cols, cols, 1)
        keep = lax.optimization_barrier(jnp.dot(delta, keep_w, preferred_element_type=jnp.float32))
        patch_effect = (keep + got.astype(jnp.float32)).astype(jnp.bfloat16)
    else:
        projected = jnp.dot(delta, out_weight, preferred_element_type=jnp.float32)
        patch_effect = lax.psum_scatter(
            projected.astype(jnp.bfloat16), "head", scatter_dimension=1, tiled=True
        )

    token_attr = lax.dynamic_slice_in_dim(attr_all, ctx_at * key_count, key_count, 0)
    return (patch_effect, token_attr, segment_attr)


def solution(mesh):
    return jax.shard_map(
        local,
        mesh=mesh,
        in_specs=(
            P(("groups", "ctx", "rep"), "head"),
            P(("groups", "ctx"), "head"),
            P(("groups", "ctx"), "head"),
            P("head", None),
            P(("groups", "ctx", "rep"), None),
            P(("groups", "ctx", "rep")),
            P(("groups", "ctx")),
            P("groups"),
        ),
        out_specs=(P(("groups", "ctx", "rep"), "head"), P(("groups", "ctx")), P("groups")),
        check_vma=False,
    )
```

```python
import functools

import jax
import jax.numpy as jnp
from jax import lax
from jax.experimental import pallas as pl
from jax.experimental.pallas import tpu as pltpu
from jax.sharding import PartitionSpec as P

HD = 128
SEG_DEV = 8
NEG_FILL = -1e30
NT_DIMS = (((1,), (1,)), ((), ()))


def attention_body(base_ref, kpos_ref, q_ref, kept_ref, do_ref, k_refs, v_refs, delta_ref, attr_ref, tq, hp):
    r = pl.program_id(2)
    kc = k_refs[0].shape[0]
    rows = hp * tq
    row_pos = base_ref[0] + r * tq + lax.broadcasted_iota(jnp.int32, (rows, 1), 0) % tq
    if hp > 1:
        q = jnp.concatenate([q_ref[:, h * HD:(h + 1) * HD] for h in range(hp)], axis=0)
        g_rows = jnp.concatenate([do_ref[:, h * HD:(h + 1) * HD] for h in range(hp)], axis=0)
    else:
        q = q_ref[...]
        g_rows = do_ref[...]
    spans = [slice(i * kc, (i + 1) * kc) for i in range(len(k_refs))]
    s_l, sc_l, sm_l = [], [], []
    for i, kr in enumerate(k_refs):
        s_i = lax.dot_general(q, kr[...], NT_DIMS, preferred_element_type=jnp.float32)
        s_i = s_i * (HD ** -0.5)
        sc_i = jnp.where(kpos_ref[:, spans[i]] <= row_pos, s_i, NEG_FILL)
        sm_i = jnp.where(kept_ref[:, spans[i]] > 0.0, sc_i, NEG_FILL)
        s_l.append(s_i)
        sc_l.append(sc_i)
        sm_l.append(sm_i)
    m_c = functools.reduce(jnp.maximum, [jnp.max(x, axis=1, keepdims=True) for x in sc_l])
    m_m = functools.reduce(jnp.maximum, [jnp.max(x, axis=1, keepdims=True) for x in sm_l])
    ec_l = [jnp.exp(x - m_c) for x in sc_l]
    em_l = [jnp.exp(x - m_m) for x in sm_l]
    l_c = functools.reduce(jnp.add, [jnp.sum(x, axis=1, keepdims=True) for x in ec_l])
    l_m = functools.reduce(jnp.add, [jnp.sum(x, axis=1, keepdims=True) for x in em_l])
    o_c = None
    o_m = None
    for i, vr in enumerate(v_refs):
        v = vr[...]
        pc = jnp.dot(ec_l[i].astype(jnp.bfloat16), v, preferred_element_type=jnp.float32)
        pm = jnp.dot(em_l[i].astype(jnp.bfloat16), v, preferred_element_type=jnp.float32)
        o_c = pc if o_c is None else o_c + pc
        o_m = pm if o_m is None else o_m + pm
    o_c = o_c / l_c
    o_m = o_m / l_m
    delta = (o_m - o_c).astype(delta_ref.dtype)
    for h in range(hp):
        delta_ref[:, h * HD:(h + 1) * HD] = delta[h * tq:(h + 1) * tq]
    row_dot = jnp.sum(g_rows.astype(jnp.float32) * o_c, axis=1, keepdims=True)
    log_total = m_c + jnp.log(l_c)
    inv = 1.0 / l_c
    for i, vr in enumerate(v_refs):
        d_p = lax.dot_general(g_rows, vr[...], NT_DIMS, preferred_element_type=jnp.float32)
        contrib = (ec_l[i] * inv) * (d_p + (d_p - row_dot) * (s_l[i] - log_total))
        attr_ref[spans[i]] += jnp.sum(contrib, axis=0)


def attention_kernel(base_ref, kpos_ref, q_ref, kept_ref, do_ref, *refs, tq, hp, n, split):
    mine, theirs = refs[:n], refs[n:2 * n]
    delta_ref, attr_ref = refs[2 * n:]
    first = (pl.program_id(0) == 0) & (pl.program_id(1) == 0) & (pl.program_id(2) == 0)

    @pl.when(first)
    def _():
        attr_ref[...] = jnp.zeros_like(attr_ref)

    args = (base_ref, kpos_ref, q_ref, kept_ref, do_ref)
    if not split:
        attention_body(*args, mine, theirs, delta_ref, attr_ref, tq, hp)
        return

    @pl.when(base_ref[1] == 0)
    def _():
        attention_body(*args, mine, theirs, delta_ref, attr_ref, tq, hp)

    @pl.when(base_ref[1] != 0)
    def _():
        attention_body(*args, theirs, mine, delta_ref, attr_ref, tq, hp)


def fused_attention(base, key_pos, query, mine, theirs, kept, grad_out, group_size, split):
    qc = query.shape[0]
    n = len(mine)
    kc = key_pos.shape[1] // n
    keys = kc * n
    kv_width = mine[0].shape[1]
    width = kv_width * group_size
    kv_local = kv_width // HD
    tq = max(8, min(qc, (128 * 2048) // keys))
    n_rows = qc // tq
    hp = group_size
    grid = (kv_local, 1, n_rows)

    def head_map(g, j, r, b):
        return (r, g + j)

    def kv_map(g, j, r, b):
        return (0, g)

    def fixed(g, j, r, b):
        return (0, 0)

    flops = 8 * qc * keys * HD * kv_local * group_size
    cost = pl.CostEstimate(
        flops=flops,
        transcendentals=2 * qc * keys * kv_local * group_size,
        bytes_accessed=2 * (3 * qc * width + 2 * keys * kv_width) + 4 * keys,
    )
    part_spec = pl.BlockSpec((kc, HD), kv_map)
    return pl.pallas_call(
        functools.partial(attention_kernel, tq=tq, hp=hp, n=n, split=split),
        grid_spec=pltpu.PrefetchScalarGridSpec(
            num_scalar_prefetch=1,
            grid=grid,
            in_specs=[
                pl.BlockSpec((1, keys), fixed),
                pl.BlockSpec((tq, hp * HD), head_map),
                pl.BlockSpec((1, keys), fixed),
                pl.BlockSpec((tq, hp * HD), head_map),
            ] + [part_spec] * (2 * n),
            out_specs=[
                pl.BlockSpec((tq, hp * HD), head_map),
                pl.BlockSpec((keys,), lambda g, j, r, b: (0,)),
            ],
        ),
        out_shape=[
            jax.ShapeDtypeStruct((qc, width), jnp.bfloat16),
            jax.ShapeDtypeStruct((keys,), jnp.float32),
        ],
        compiler_params=pltpu.CompilerParams(
            dimension_semantics=("arbitrary", "arbitrary", "arbitrary")
        ),
        cost_estimate=cost,
    )(base, key_pos, query, kept, grad_out, *mine, *theirs)


def relay_gather(payload, needed, ctx_at):
    n = lax.axis_size("ctx")
    zero = jnp.zeros_like(payload)
    forward, backward = [payload], [payload]
    for k in range(1, n):
        fwd = [(i, i + k) for i in range(n - k) if needed(i + k, i)]
        relay = [(i + k - 1, i + k) for i, _ in fwd]
        if k > 2 and relay and all(needed(s, r - k) for s, r in relay):
            forward.append(lax.ppermute(forward[-1], "ctx", relay))
        else:
            forward.append(lax.ppermute(payload, "ctx", fwd) if fwd else zero)
        bwd = [(i + k, i) for i in range(n - k) if needed(i, i + k)]
        relay = [(r + 1, r) for _, r in bwd]
        if k > 2 and relay and all(needed(s, r + k) for s, r in relay):
            backward.append(lax.ppermute(backward[-1], "ctx", relay))
        else:
            backward.append(lax.ppermute(payload, "ctx", bwd) if bwd else zero)
    parts = [payload]
    for k in range(1, n):
        parts.append(jnp.where(k <= ctx_at, forward[k], backward[n - k]))
    return parts


def gather_kv(key, value, segment_ids, ctx_at, rep_at, rep_count, needed):
    n = lax.axis_size("ctx")
    key_count, width = key.shape
    seg_rows = -(-key_count // width)
    seg_pad = -(-seg_rows // 16) * 16
    seg_block = jnp.zeros((seg_pad * width,), jnp.bfloat16)
    seg_block = seg_block.at[:key_count].set(segment_ids.astype(jnp.bfloat16))
    seg_block = seg_block.reshape(seg_pad, width)
    split = rep_count == 2
    halves = [jnp.where(rep_at == 0, key, value)] if split else [key, value]
    payloads = [jnp.concatenate([h, seg_block], axis=0) for h in halves]
    gathered = [relay_gather(p, needed, ctx_at) for p in payloads]
    if split:
        mine = gathered[0]
        theirs = [lax.ppermute(p, "rep", [(0, 1), (1, 0)]) for p in mine]
        key_parts = [jnp.where(rep_at == 0, a, b) for a, b in zip(mine, theirs)]
    else:
        mine, theirs = gathered
        key_parts = mine
    seg_all = jnp.concatenate(
        [p[key_count:].reshape(-1)[:key_count] for p in key_parts], axis=0
    ).astype(jnp.int32)
    source = (ctx_at - jnp.arange(n, dtype=jnp.int32)) % n
    key_pos = (source[:, None] * key_count + jnp.arange(key_count, dtype=jnp.int32)[None, :])
    return mine, theirs, seg_all, key_pos.reshape(1, -1), split


def butterfly_sum(total, axes):
    for axis in axes:
        n = lax.axis_size(axis)
        if n & (n - 1):
            total = lax.psum(total, axis)
            continue
        bit = 1
        while bit < n:
            total = total + lax.ppermute(total, axis, [(i, i ^ bit) for i in range(n)])
            bit *= 2
    return total


def local(query, key, value, out_weight, cotangent, response, segment_ids, masked_segments):
    ctx_count = lax.axis_size("ctx")
    rep_count = lax.axis_size("rep")
    head_count = lax.axis_size("head")
    ctx_at = lax.axis_index("ctx")
    rep_at = lax.axis_index("rep")
    head_at = lax.axis_index("head")
    query_count = query.shape[0]
    key_count = key.shape[0]
    kv_local = key.shape[1] // HD
    heads_local = query.shape[1] // HD
    group_size = heads_local // kv_local
    context_len = key_count * ctx_count
    query_base = context_len - query_count * ctx_count * rep_count
    base = (query_base + (ctx_at * rep_count + rep_at) * query_count).astype(jnp.int32)
    base = jnp.stack([base, rep_at.astype(jnp.int32)])

    def needed(receiver, block):
        last_query = query_base + (receiver * rep_count + rep_count) * query_count - 1
        return block * key_count <= last_query

    mine, theirs, seg_shift, key_pos, split = gather_kv(
        key, value, segment_ids, ctx_at, rep_at, rep_count, needed
    )
    kept = jnp.where(
        jnp.any(seg_shift[:, None] == masked_segments[None, :], axis=1), 0.0, 1.0
    ).astype(jnp.float32)[None, :]
    onehot = (
        seg_shift[:, None] == jnp.arange(SEG_DEV * ctx_count, dtype=jnp.int32)[None, :]
    ).astype(jnp.float32)

    grad_masked = jnp.where(response[:, None] > 0, cotangent, jnp.zeros_like(cotangent))
    grad_out = jnp.dot(grad_masked, out_weight.T, preferred_element_type=jnp.float32).astype(
        jnp.bfloat16
    )
    delta, attr = fused_attention(
        base, key_pos, query, mine, theirs, kept, grad_out, group_size, split
    )

    inverse = (ctx_at - jnp.arange(ctx_count, dtype=jnp.int32)) % ctx_count
    attr_abs = attr.reshape(ctx_count, key_count)[inverse].reshape(-1)
    seg_part = jnp.sum(jnp.where(onehot > 0.0, attr[:, None], 0.0), axis=0)
    summed = butterfly_sum(jnp.concatenate([attr_abs, seg_part]), ("rep", "ctx", "head"))
    attr_all = summed[:context_len]
    segment_attr = summed[context_len:]

    if head_count == 2:
        cols = out_weight.shape[1] // 2
        send_w = lax.dynamic_slice_in_dim(out_weight, (1 - head_at) * cols, cols, 1)
        send = jnp.dot(delta, send_w, preferred_element_type=jnp.float32)
        got = lax.ppermute(send.astype(jnp.bfloat16), "head", [(0, 1), (1, 0)])
        keep_w = lax.dynamic_slice_in_dim(out_weight, head_at * cols, cols, 1)
        keep = lax.optimization_barrier(jnp.dot(delta, keep_w, preferred_element_type=jnp.float32))
        patch_effect = (keep + got.astype(jnp.float32)).astype(jnp.bfloat16)
    else:
        projected = jnp.dot(delta, out_weight, preferred_element_type=jnp.float32)
        patch_effect = lax.psum_scatter(
            projected.astype(jnp.bfloat16), "head", scatter_dimension=1, tiled=True
        )

    token_attr = lax.dynamic_slice_in_dim(attr_all, ctx_at * key_count, key_count, 0)
    return (patch_effect, token_attr, segment_attr)


def solution(mesh):
    return jax.shard_map(
        local,
        mesh=mesh,
        in_specs=(
            P(("groups", "ctx", "rep"), "head"),
            P(("groups", "ctx"), "head"),
            P(("groups", "ctx"), "head"),
            P("head", None),
            P(("groups", "ctx", "rep"), None),
            P(("groups", "ctx", "rep")),
            P(("groups", "ctx")),
            P("groups"),
        ),
        out_specs=(P(("groups", "ctx", "rep"), "head"), P(("groups", "ctx")), P("groups")),
        check_vma=False,
    )
```
